32 devices in a mesh: req: 8 (over y, x, core), hid: 4 (over z).
Axes of the slice: x: 2, y: 2, z: 4, core: 2. Of those that a mesh axis runs over, the one named last changes fastest.
Arguments:
- hidden_in: bfloat16 [2048, 1024], P('req', 'hid'), may hold values from -6 to 6
- segments: int32 [8, 256], P('req'), may hold values from 0 to 7, never falling along the last dimension, each value on 1 to 128 neighbouring positions
- prefix_group: int32 [8, 8], P('req'), may hold values from 0 to 15
- prefix_cache: bfloat16 [16, 1024, 8, 128], P('req', None, 'hid'), may hold values from -400 to 400
- page_table: int32 [8, 2], P('req'), may hold values from 0 to 1, each once within a row
- norm_gain: float32 [1024], replicated, may hold values from 0.1 to 1.9
- w_query: bfloat16 [1024, 1024], P(None, 'hid'), may hold values from -0.1875 to 0.1875
- w_keyval: bfloat16 [1024, 1024], P(None, 'hid'), may hold values from -0.1875 to 0.1875
- w_out: bfloat16 [1024, 1024], P('hid'), may hold values from -0.1875 to 0.1875
- moe_gain: float32 [1024], replicated, may hold values from 0.1 to 1.9
- routes: int32 [2048, 8], P('req'), may hold values from 0 to 15, all different within a row; in each aligned block of 256 rows (0 to 255, 256 to 511, ...) at most 256 rows name the same one
- gates: float32 [2048, 8], P('req'), may hold values from 0.05 to 0.5
- w_gate_up: bfloat16 [16, 2, 1024, 512], P('req', None, None, 'hid'), may hold values from -0.1875 to 0.1875
- w_down: bfloat16 [16, 512, 1024], P('req', 'hid'), may hold values from -0.25 to 0.25
Outputs:
- hidden_out: bfloat16 [2048, 1024], P('req', 'hid')
- kv_pages: bfloat16 [16, 128, 8, 128], P('req', None, 'hid')
The draws below stay inside these ranges and needn't reach their ends.
Inputs may be any that keep to these rules, and one draw needn't show every extreme that they name: `routes`: within the 256 rows of one row of the stream no expert is named by more than 256 tokens. `page_table`: each row is a permutation of 0 to 1. `segments`: segment numbers of a row never fall; each of the 8 documents has 1 to 128 tokens.
All inputs are finite; a program needn't handle non-finite values.
Results may differ from the reference program's by a relative error of at most 0.013.
Values may be sent and summed in bfloat16 or wider, within the bound.
No kernel may reach another device: no remote copies, remote signals or barrier semaphores. Data moves between devices by JAX's collectives and lax.ppermute only.
A program may use at most 128 MiB of HBM per device.

```python
import math
import jax
import jax.numpy as jnp
import numpy as np
from jax import lax

D = 1024
H = 16
KVH = 8
HD = 64
FF = 512
TOP = 8
TOK_DEV = 256
SEGS = 8
PRE = 1024
PAGE = 128
REQS = 8
TOKENS = 2048
EXPERTS = 16
GROUPS = 16
MOSTSEG = 128
CAP = 256
PAGES_DEV = 2
POOL = 16


def draw_prefix_cache(key, part):
    array_shape = (GROUPS, PRE, KVH, 2 * HD)
    drawn = jnp.clip(jax.random.normal(jax.random.fold_in(key, 1), array_shape, jnp.float32), -6.0, 6.0)
    return drawn.astype(jnp.bfloat16)


def set_ends(entries, own_key, smallest, high):
    dims = entries.shape
    place = [jax.random.randint(jax.random.fold_in(own_key, axis), (), 0, dims[axis]) for axis in range(len(dims))]
    entries = entries.at[tuple(place)].set(smallest)
    longest = dims.index(max(dims))
    place[longest] = (place[longest] + 1) % dims[longest]
    return entries.at[tuple(place)].set(high)


def level_of(stream_key, extent, split, low, top_value):
    def one(axis_at, shards_of):
        heights = jax.random.uniform(jax.random.fold_in(jax.random.fold_in(stream_key, 6), axis_at), (shards_of,), jnp.float32, low / len(split), top_value / len(split))
        return jnp.repeat(jnp.exp(heights), extent[axis_at] // shards_of).reshape((-1,) + (1,) * (len(extent) - axis_at - 1))

    factor_of = one(*split[0])
    for cut in split[1:]:
        factor_of = factor_of * one(*cut)
    return factor_of


def split_up(amount, total, bound, lean):
    weights = [(1 << 20) // math.isqrt(standing ** lean) + 1 for standing in range(2, amount + 1)]
    rest, holding = total - bound - (amount - 1), [1] * (amount - 1)
    while rest > 0:
        candidates = [i for i in range(amount - 1) if holding[i] < bound]
        mass, budget = sum([weights[i] for i in candidates]), rest
        for i in candidates:
            more = min(bound - holding[i], max(1, budget * weights[i] // mass), rest)
            holding[i] = holding[i] + more
            rest = rest - more
    return np.array([bound] + holding)


def ragged(rng, number_of, total, bound, lean):
    if number_of == 2:
        one = jax.random.randint(rng, (), max(1, total - bound), min(bound, total - 1) + 1)
        return jnp.stack([one, total - one])
    tallies = jnp.asarray(split_up(number_of, total, bound, lean), jnp.int32)
    pairs = (number_of - 1) // 2
    source_of, receiver = tallies[1:1 + 2 * pairs:2], tallies[2:2 + 2 * pairs:2]
    room = jnp.minimum(source_of - 1, bound - receiver)
    passed = jax.random.randint(jax.random.fold_in(rng, 1), (pairs,), 0, 1 << 20) % (room + 1)
    tallies = tallies.at[1:1 + 2 * pairs:2].set(source_of - passed).at[2:2 + 2 * pairs:2].set(receiver + passed)
    return tallies[jax.random.permutation(jax.random.fold_in(rng, 2), number_of)]


def shared_out(rng, own, number, rows, count, top, limit, slope):
    ranking = jax.random.permutation(rng, count)
    heavy_load, common = shares(count, rows * top, limit, slope, True), shares(count, rows * top, limit, slope, False)
    places = jnp.arange(count)

    def named(lengths, offset_by):
        used = int((lengths > 0).sum())
        fixed = max(1, used // 4)
        shifted = fixed + (places - fixed + offset_by * (used - fixed)) % max(1, count - fixed)
        return jnp.zeros((count,), jnp.int32).at[ranking[jnp.where(places < fixed, places, shifted)]].set(jnp.asarray(lengths, jnp.int32))

    lengths = jnp.where(number % 4 == 0, named(heavy_load, number // 4), named(common, number - number // 4 - 1))
    mixed = jax.random.permutation(jax.random.fold_in(own, 3), count)
    source_of, sink = mixed[0:count // 2 * 2:2], mixed[1:count // 2 * 2:2]
    margin = jnp.minimum(lengths[source_of] - 1, limit - lengths[sink]) // 2
    margin = jnp.where((source_of == ranking[0]) | (sink == ranking[0]) | (lengths[sink] == 0), 0, jnp.maximum(margin, 0))
    shifted = jax.random.randint(jax.random.fold_in(own, 4), (count // 2,), 0, 1 << 20) % (margin + 1)
    lengths = lengths.at[source_of].add(-shifted).at[sink].add(shifted)
    items = jnp.searchsorted(jnp.cumsum(lengths), jnp.arange(rows * top), side="right").astype(jnp.int32)
    grid = items.reshape(top, rows).T
    grid = grid[jax.random.permutation(jax.random.fold_in(own, 1), rows)]
    offset_by = jax.random.randint(jax.random.fold_in(own, 2), (rows, 1), 0, top)
    return jnp.take_along_axis(grid, (jnp.arange(top)[None, :] + offset_by) % top, axis=1)


def shares(number_of, total, most, lean, full):
    weights = [(1 << 20) // math.isqrt(grade ** lean) + 1 for grade in range(1, number_of + 1)]
    largest = most if full else min(most, max(-(-total // number_of), total * weights[0] // sum(weights)))
    least = 1 if total - largest >= number_of - 1 else 0
    given, spare = [largest] + [least] * (number_of - 1), total - largest - least * (number_of - 1)
    while spare > 0:
        free = [i for i in range(1, number_of) if given[i] < largest] or [i for i in range(1, number_of) if given[i] < most]
        pool, left = sum([weights[i] for i in free]), spare
        for i in free:
            addition = min(most - given[i], max(1, left * weights[i] // pool), spare)
            given[i] = given[i] + addition
            spare = spare - addition
    return np.array(given)


def gaussian(own_key, dims, width, bound, shards=(), kind=jnp.bfloat16):
    entries = jax.random.normal(own_key, dims, jnp.float32) * width
    if len(shards) > 0:
        entries = level_of(own_key, dims, shards, -0.22, 0.18) * entries
    return jnp.clip(entries, min=-bound, max=bound).astype(kind)


def setup_inputs(seed: int = 0) -> dict:
    keys = jax.random.split(jax.random.key(seed), 15)
    hidden_in = gaussian(keys[0], (TOKENS, D), 1.0, 6.0, ((0, 8), (1, 4)))
    segments = jax.vmap(lambda own: jnp.searchsorted(jnp.cumsum(ragged(own, SEGS, TOK_DEV, MOSTSEG, 2)), jnp.arange(TOK_DEV), side="right"))(jax.random.split(keys[1], REQS)).reshape((REQS, TOK_DEV)).astype(jnp.int32)
    prefix_group = set_ends(jax.random.randint(keys[2], (REQS, SEGS), 0, GROUPS), jax.random.fold_in(keys[2], 1), 0, GROUPS - 1).astype(jnp.int32)
    prefix_cache = draw_prefix_cache(jax.random.fold_in(keys[14], 71), 0)
    page_table = jax.vmap(lambda own: jax.random.permutation(own, PAGES_DEV))(jax.random.split(keys[4], REQS)).reshape((REQS, PAGES_DEV)).astype(jnp.int32)
    norm_gain = jnp.clip(1.0 + 0.18 * jax.random.normal(keys[5], (D,), jnp.float32), 0.1, 1.9)
    w_query = gaussian(keys[6], (D, H * HD), D ** -0.5, 0.1875, ((1, 4),))
    w_keyval = gaussian(keys[7], (D, KVH * 2 * HD), D ** -0.5, 0.1875, ((1, 4),))
    w_out = gaussian(keys[8], (H * HD, D), (H * HD) ** -0.5, 0.1875, ((0, 4),))
    moe_gain = jnp.clip(1.0 + 0.18 * jax.random.normal(keys[9], (D,), jnp.float32), 0.1, 1.9)
    routes_keys = jax.random.split(jax.random.fold_in(keys[10], 1), TOKENS // TOK_DEV)
    routes_turns = jax.random.permutation(jax.random.fold_in(keys[10], 3), TOKENS // TOK_DEV)
    routes = jax.vmap(lambda own, number: shared_out(jax.random.fold_in(keys[10], 2), own, number, TOK_DEV, EXPERTS, TOP, CAP, 2))(routes_keys, routes_turns).reshape((TOKENS, TOP))
    gates = jnp.clip(jnp.exp(math.log(0.5) - 2.3025851 * jax.random.uniform(keys[11], (TOKENS, TOP), jnp.float32) ** level_of(keys[11], (TOKENS, TOP), ((0, 8),), -0.2, 0.2)), 0.05, 0.5)
    w_gate_up = gaussian(keys[12], (EXPERTS, 2, D, FF), D ** -0.5, 0.1875, ((0, 8), (3, 4)))
    w_down = gaussian(keys[13], (EXPERTS, FF, D), FF ** -0.5, 0.25, ((0, 8), (1, 4)))
    return dict(hidden_in=hidden_in, segments=segments, prefix_group=prefix_group, prefix_cache=prefix_cache, page_table=page_table, norm_gain=norm_gain, w_query=w_query, w_keyval=w_keyval, w_out=w_out, moe_gain=moe_gain, routes=routes, gates=gates, w_gate_up=w_gate_up, w_down=w_down)


EPSILON = 1e-06
THETA = 10000.0

def rms_scale(row_data, gain_row):
    floats = row_data.astype(jnp.float32)
    mean_square = lax.optimization_barrier(jnp.mean(floats * floats, axis=-1, keepdims=True))
    return (floats * lax.rsqrt(mean_square + EPSILON) * gain_row).astype(jnp.bfloat16)

def rotate(features, positions):
    half_dim = features.shape[-1] // 2
    frequency = THETA ** (-2.0 * jnp.arange(half_dim, dtype=jnp.float32) / features.shape[-1])
    angles = positions.astype(jnp.float32)[:, None] * frequency[None, :]
    cosine = jnp.cos(angles)[:, None, :]
    sine_part = jnp.sin(angles)[:, None, :]
    front_half = features[..., :half_dim]
    second = features[..., half_dim:]
    return jnp.concatenate([front_half * cosine - second * sine_part, second * cosine + front_half * sine_part], axis=-1)

def positions_of(segment_row, offset):
    earlier = lax.optimization_barrier(jnp.sum((segment_row[None, :] < segment_row[:, None]).astype(jnp.int32), axis=1))
    token_index = jnp.arange(segment_row.shape[0], dtype=jnp.int32)
    return token_index - earlier + offset

def group_of_tokens(segment_row, group_row):
    labels = jnp.arange(group_row.shape[0], dtype=jnp.int32)
    return lax.optimization_barrier(jnp.sum(jnp.where(segment_row[:, None] == labels[None, :], group_row[None, :], 0), axis=1))

def slots_of(route_rows, experts):
    flat_routes = route_rows.reshape(-1)
    onehot = (flat_routes[:, None] == jnp.arange(experts, dtype=jnp.int32)[None, :]).astype(jnp.int32)
    before = jnp.cumsum(onehot, axis=0) - onehot
    return (flat_routes, lax.optimization_barrier(jnp.sum(before * onehot, axis=1)))

def attend_device(query_rows, key_rows, value_rows, segment_row, group_row, prefix_cache):
    token_index = jnp.arange(TOK_DEV, dtype=jnp.int32)

    def attend_one(inputs):
        query_now, group_now, segment_now, index_now = inputs
        chosen = lax.dynamic_index_in_dim(prefix_cache, group_now, 0, keepdims=False)
        all_keys = jnp.concatenate([key_rows, chosen[..., :HD]], axis=0).astype(jnp.float32)
        all_values = jnp.concatenate([value_rows, chosen[..., HD:]], axis=0).astype(jnp.float32)
        seen = jnp.concatenate([(segment_row == segment_now) & (token_index <= index_now), jnp.ones((PRE,), bool)])
        grouped_query = query_now.reshape(KVH, H // KVH, HD).astype(jnp.float32)
        scores = jnp.einsum('kgd,skd->kgs', grouped_query, all_keys) * HD ** (-0.5)
        scores = jnp.where(seen[None, None, :], scores, -jnp.inf)
        row_max = lax.optimization_barrier(jnp.max(scores, axis=-1, keepdims=True))
        numerators = jnp.exp(scores - row_max)
        totals = lax.optimization_barrier(jnp.sum(numerators, axis=-1))
        rounded = lax.optimization_barrier(numerators.astype(jnp.bfloat16)).astype(jnp.float32)
        weighted = jnp.einsum('kgs,skd->kgd', rounded, all_values)
        return (weighted / totals[..., None]).reshape(H * HD).astype(jnp.bfloat16)
    return lax.map(attend_one, (query_rows, group_row, segment_row, token_index))

def reference(hidden_in, segments, prefix_group, prefix_cache, page_table, norm_gain, w_query, w_keyval, w_out, moe_gain, routes, gates, w_gate_up, w_down):
    normed = rms_scale(hidden_in, norm_gain)
    position = jax.vmap(lambda segment_row: positions_of(segment_row, PRE))(segments).reshape(-1)
    projected = jnp.dot(normed, w_query, preferred_element_type=jnp.float32).reshape(TOKENS, H, HD)
    queries = rotate(projected, position).astype(jnp.bfloat16)
    key_value = jnp.dot(normed, w_keyval, preferred_element_type=jnp.float32).reshape(TOKENS, KVH, 2 * HD)
    key_rows = rotate(key_value[..., :HD], position).astype(jnp.bfloat16)
    value_rows = key_value[..., HD:].astype(jnp.bfloat16)
    pages = jnp.concatenate([key_rows, value_rows], axis=-1).reshape(REQS, PAGES_DEV, PAGE, KVH, 2 * HD)
    kv_pages = jax.vmap(lambda page_rows, order: jnp.zeros_like(page_rows).at[order].set(page_rows))(pages, page_table)
    kv_pages = kv_pages.reshape(POOL, PAGE, KVH, 2 * HD)
    token_group = jax.vmap(group_of_tokens)(segments, prefix_group)
    attention = lax.map(lambda device_data: attend_device(device_data[0], device_data[1], device_data[2], device_data[3], device_data[4], prefix_cache), (queries.reshape(REQS, TOK_DEV, H, HD), key_rows.reshape(REQS, TOK_DEV, KVH, HD), value_rows.reshape(REQS, TOK_DEV, KVH, HD), segments, token_group)).reshape(TOKENS, H * HD)
    middle = (hidden_in.astype(jnp.float32) + jnp.dot(attention, w_out, preferred_element_type=jnp.float32)).astype(jnp.bfloat16)
    normed_moe = rms_scale(middle, moe_gain)
    route_blocks = routes.reshape(REQS, TOK_DEV, TOP)
    flat_routes, slot = jax.vmap(lambda route_block: slots_of(route_block, EXPERTS))(route_blocks)
    target = flat_routes * CAP + slot
    token_rows = jnp.repeat(normed_moe.reshape(REQS, TOK_DEV, D), TOP, axis=1)
    buffers = jax.vmap(lambda rows_now, where_to: jnp.zeros((EXPERTS * CAP, D), jnp.bfloat16).at[where_to].set(rows_now))(token_rows, target)
    by_expert = buffers.reshape(REQS, EXPERTS, CAP, D).transpose(1, 0, 2, 3)

    def run_expert(inputs):
        expert_in, gate_up, down_proj = inputs
        flat_in = expert_in.reshape(REQS * CAP, D)
        gate_proj = jnp.dot(flat_in, gate_up[0], preferred_element_type=jnp.float32)
        up_proj = jnp.dot(flat_in, gate_up[1], preferred_element_type=jnp.float32)
        hidden = (jax.nn.silu(gate_proj) * up_proj).astype(jnp.bfloat16)
        return jnp.dot(hidden, down_proj, preferred_element_type=jnp.float32).astype(jnp.bfloat16).reshape(REQS, CAP, D)
    expert_out = lax.map(run_expert, (by_expert, w_gate_up, w_down))
    per_device = expert_out.transpose(1, 0, 2, 3).reshape(REQS, EXPERTS * CAP, D)
    picked = jax.vmap(lambda table_rows, where_from: table_rows[where_from])(per_device, target).reshape(TOKENS, TOP, D)
    expert_sum = lax.optimization_barrier(jnp.sum(picked.astype(jnp.float32) * gates[:, :, None], axis=1))
    hidden_out = (middle.astype(jnp.float32) + expert_sum).astype(jnp.bfloat16)
    return (hidden_out, kv_pages)
```

```python
import jax
import jax.numpy as jnp
from jax import lax
from jax.sharding import PartitionSpec as P

PAGE = 128


EPSILON = 1e-06
THETA = 10000.0


def rms_scale(row_data, gain_row):
    floats = row_data.astype(jnp.float32)
    mean_square = jnp.mean(floats * floats, axis=-1, keepdims=True)
    return (floats * lax.rsqrt(mean_square + EPSILON) * gain_row).astype(jnp.bfloat16)


def rotate(features, positions):
    half_dim = features.shape[-1] // 2
    frequency = THETA ** (-2.0 * jnp.arange(half_dim, dtype=jnp.float32) / features.shape[-1])
    angles = positions.astype(jnp.float32)[:, None] * frequency[None, :]
    cosine = jnp.cos(angles)[:, None, :]
    sine_part = jnp.sin(angles)[:, None, :]
    front_half = features[..., :half_dim]
    second = features[..., half_dim:]
    return jnp.concatenate(
        [front_half * cosine - second * sine_part, second * cosine + front_half * sine_part],
        axis=-1,
    )


def positions_of(segment_row, offset):
    earlier = jnp.sum((segment_row[None, :] < segment_row[:, None]).astype(jnp.int32), axis=1)
    token_index = jnp.arange(segment_row.shape[0], dtype=jnp.int32)
    return token_index - earlier + offset


def slots_of(route_rows, experts):
    flat_routes = route_rows.reshape(-1)
    onehot = (flat_routes[:, None] == jnp.arange(experts, dtype=jnp.int32)[None, :]).astype(
        jnp.int32
    )
    before = jnp.cumsum(onehot, axis=0) - onehot
    return (flat_routes, jnp.sum(before * onehot, axis=1))


def expert_rows(received, gate_up, down_proj):
    local_experts = down_proj.shape[0]
    slot_count = received.shape[1]
    model_width = received.shape[2]
    grouped = received.reshape(-1, local_experts, slot_count, model_width)
    gate_proj = jnp.einsum(
        "recd,edf->recf", grouped, gate_up[:, 0], preferred_element_type=jnp.float32
    )
    up_proj = jnp.einsum(
        "recd,edf->recf", grouped, gate_up[:, 1], preferred_element_type=jnp.float32
    )
    hidden = (jax.nn.silu(gate_proj) * up_proj).astype(jnp.bfloat16)
    produced = jnp.einsum("recf,efd->recd", hidden, down_proj, preferred_element_type=jnp.float32)
    return produced.reshape(-1, slot_count, model_width)


def shards(
    hidden_in,
    segments,
    prefix_group,
    prefix_cache,
    page_table,
    norm_gain,
    w_query,
    w_keyval,
    w_out,
    moe_gain,
    routes,
    gates,
    w_gate_up,
    w_down,
):
    req_count = lax.axis_size("req")
    whole = lax.all_gather(hidden_in, "hid", axis=1, tiled=True)
    tok_count = whole.shape[0]
    model_width = whole.shape[1]
    segment_row = segments[0]
    prefix_len = prefix_cache.shape[1]
    kv_heads = prefix_cache.shape[2]
    head_dim = prefix_cache.shape[3] // 2
    score_scale = head_dim ** (-0.5)
    normed = rms_scale(whole, norm_gain)
    position = positions_of(segment_row, prefix_len)
    projected = jnp.dot(normed, w_query, preferred_element_type=jnp.float32).reshape(
        tok_count, -1, head_dim
    )
    queries = rotate(projected, position).astype(jnp.bfloat16)
    q_groups = queries.shape[1] // kv_heads
    grouped_query = queries.reshape(tok_count, kv_heads, q_groups, head_dim)
    key_value = jnp.dot(normed, w_keyval, preferred_element_type=jnp.float32).reshape(
        tok_count, kv_heads, 2 * head_dim
    )
    key_rows = rotate(key_value[..., :head_dim], position).astype(jnp.bfloat16)
    value_rows = key_value[..., head_dim:].astype(jnp.bfloat16)
    pages = jnp.concatenate([key_rows, value_rows], axis=-1).reshape(
        -1, PAGE, kv_heads, 2 * head_dim
    )
    kv_pages = jnp.zeros_like(pages).at[page_table[0]].set(pages)
    token_index = jnp.arange(tok_count, dtype=jnp.int32)
    visible = (segment_row[None, :] == segment_row[:, None]) & (
        token_index[None, :] <= token_index[:, None]
    )
    local_scores = (
        jnp.einsum("tkgd,skd->kgts", grouped_query, key_rows, preferred_element_type=jnp.float32)
        * score_scale
    )
    local_scores = jnp.where(visible[None, None], local_scores, -jnp.inf)
    row_max = jnp.max(local_scores, axis=-1)
    numerators = jnp.exp(local_scores - row_max[..., None])
    totals = jnp.sum(numerators, axis=-1)
    weighted = jnp.einsum(
        "kgts,skd->kgtd",
        numerators.astype(jnp.bfloat16),
        value_rows,
        preferred_element_type=jnp.float32,
    )
    gathered = lax.all_gather(prefix_cache, "req", axis=0, tiled=True)
    window = tok_count // 2
    seg_count = prefix_group.shape[1]
    for seg in range(seg_count):
        start_row = jnp.minimum(jnp.sum((segment_row < seg).astype(jnp.int32)), tok_count - window)
        chosen = lax.dynamic_index_in_dim(gathered, prefix_group[0, seg], 0, keepdims=False)
        query_window = lax.dynamic_slice_in_dim(grouped_query, start_row, window, 0)
        scores = (
            jnp.einsum(
                "tkgd,skd->kgts",
                query_window,
                chosen[..., :head_dim],
                preferred_element_type=jnp.float32,
            )
            * score_scale
        )
        old_max = lax.dynamic_slice_in_dim(row_max, start_row, window, 2)
        old_total = lax.dynamic_slice_in_dim(totals, start_row, window, 2)
        old_weighted = lax.dynamic_slice_in_dim(weighted, start_row, window, 2)
        new_max = jnp.maximum(old_max, jnp.max(scores, axis=-1))
        decay_factor = jnp.exp(old_max - new_max)
        fresh = jnp.exp(scores - new_max[..., None])
        added = jnp.einsum(
            "kgts,skd->kgtd",
            fresh.astype(jnp.bfloat16),
            chosen[..., head_dim:],
            preferred_element_type=jnp.float32,
        )
        new_total = old_total * decay_factor + jnp.sum(fresh, axis=-1)
        new_weighted = old_weighted * decay_factor[..., None] + added
        inside = lax.dynamic_slice_in_dim(segment_row, start_row, window, 0) == seg
        row_max = lax.dynamic_update_slice_in_dim(
            row_max, jnp.where(inside[None, None], new_max, old_max), start_row, 2
        )
        totals = lax.dynamic_update_slice_in_dim(
            totals, jnp.where(inside[None, None], new_total, old_total), start_row, 2
        )
        weighted = lax.dynamic_update_slice_in_dim(
            weighted,
            jnp.where(inside[None, None, :, None], new_weighted, old_weighted),
            start_row,
            2,
        )
    attention = (
        (weighted / totals[..., None])
        .transpose(2, 0, 1, 3)
        .reshape(tok_count, -1)
        .astype(jnp.bfloat16)
    )
    share_width = hidden_in.shape[1]
    whole_attention = lax.all_gather(attention, "hid", axis=1, tiled=True)
    whole_w_out = lax.all_gather(w_out, "hid", axis=0, tiled=True)
    projected_out = jnp.dot(whole_attention, whole_w_out, preferred_element_type=jnp.float32)
    middle = (whole.astype(jnp.float32) + projected_out).astype(jnp.bfloat16)
    middle_share = lax.dynamic_slice_in_dim(
        middle, lax.axis_index("hid") * share_width, share_width, 1
    )
    normed_moe = rms_scale(middle, moe_gain)
    all_gate_up = lax.all_gather(w_gate_up, "req", axis=0, tiled=True)
    all_down = lax.all_gather(w_down, "req", axis=0, tiled=True)
    experts = all_down.shape[0]
    expert_ids = jnp.arange(experts, dtype=jnp.int32)
    combine = jnp.sum(
        jnp.where(routes[:, :, None] == expert_ids[None, None, :], gates[:, :, None], 0.0), axis=1
    )
    gate_proj = jnp.einsum(
        "td,edf->tef", normed_moe, all_gate_up[:, 0], preferred_element_type=jnp.float32
    )
    up_proj = jnp.einsum(
        "td,edf->tef", normed_moe, all_gate_up[:, 1], preferred_element_type=jnp.float32
    )
    hidden = (jax.nn.silu(gate_proj) * up_proj * combine[:, :, None]).astype(jnp.bfloat16)
    partial_out = jnp.einsum(
        "tef,efd->td", hidden, all_down, preferred_element_type=jnp.float32
    )
    expert_sum = lax.psum_scatter(
        partial_out.astype(jnp.bfloat16), "hid", scatter_dimension=1, tiled=True
    ).astype(jnp.float32)
    hidden_out = (middle_share.astype(jnp.float32) + expert_sum).astype(jnp.bfloat16)
    return (hidden_out, kv_pages)


def solution(mesh):
    in_specs = (
        P("req", "hid"),
        P("req", None),
        P("req", None),
        P("req", None, "hid", None),
        P("req", None),
        P(),
        P(None, "hid"),
        P(None, "hid"),
        P("hid", None),
        P(),
        P("req", None),
        P("req", None),
        P("req", None, None, "hid"),
        P("req", "hid", None),
    )
    out_specs = (P("req", "hid"), P("req", None, "hid", None))
    return jax.shard_map(shards, mesh=mesh, in_specs=in_specs, out_specs=out_specs, check_vma=False)
```

```python
import jax
import jax.numpy as jnp
from jax import lax
from jax.sharding import PartitionSpec as P

PAGE = 128


EPSILON = 1e-06
THETA = 10000.0


def rms_scale(row_data, gain_row):
    floats = row_data.astype(jnp.float32)
    mean_square = jnp.mean(floats * floats, axis=-1, keepdims=True)
    return (floats * lax.rsqrt(mean_square + EPSILON) * gain_row).astype(jnp.bfloat16)


def rotate(features, positions):
    half_dim = features.shape[-1] // 2
    frequency = THETA ** (-2.0 * jnp.arange(half_dim, dtype=jnp.float32) / features.shape[-1])
    angles = positions.astype(jnp.float32)[:, None] * frequency[None, :]
    cosine = jnp.cos(angles)[:, None, :]
    sine_part = jnp.sin(angles)[:, None, :]
    front_half = features[..., :half_dim]
    second = features[..., half_dim:]
    return jnp.concatenate(
        [front_half * cosine - second * sine_part, second * cosine + front_half * sine_part],
        axis=-1,
    )


def positions_of(segment_row, offset):
    earlier = jnp.sum((segment_row[None, :] < segment_row[:, None]).astype(jnp.int32), axis=1)
    token_index = jnp.arange(segment_row.shape[0], dtype=jnp.int32)
    return token_index - earlier + offset


def slots_of(route_rows, experts):
    flat_routes = route_rows.reshape(-1)
    onehot = (flat_routes[:, None] == jnp.arange(experts, dtype=jnp.int32)[None, :]).astype(
        jnp.int32
    )
    before = jnp.cumsum(onehot, axis=0) - onehot
    return (flat_routes, jnp.sum(before * onehot, axis=1))


def expert_rows(received, gate_up, down_proj):
    local_experts = down_proj.shape[0]
    slot_count = received.shape[1]
    model_width = received.shape[2]
    grouped = received.reshape(-1, local_experts, slot_count, model_width)
    gate_proj = jnp.einsum(
        "recd,edf->recf", grouped, gate_up[:, 0], preferred_element_type=jnp.float32
    )
    up_proj = jnp.einsum(
        "recd,edf->recf", grouped, gate_up[:, 1], preferred_element_type=jnp.float32
    )
    hidden = (jax.nn.silu(gate_proj) * up_proj).astype(jnp.bfloat16)
    produced = jnp.einsum("recf,efd->recd", hidden, down_proj, preferred_element_type=jnp.float32)
    return produced.reshape(-1, slot_count, model_width)


def shifted_copies(block, axis_name):
    count = lax.axis_size(axis_name)
    copies = [block]
    for shift in range(1, count):
        pairs = [(index, (index + shift) % count) for index in range(count)]
        copies.append(lax.ppermute(block, axis_name, pairs))
    return copies


def gather_in_order(block, axis_name, axis):
    count = lax.axis_size(axis_name)
    copies = jnp.stack(shifted_copies(block, axis_name))
    order = (lax.axis_index(axis_name) - jnp.arange(count, dtype=jnp.int32)) % count
    picked = jnp.take(copies, order, axis=0)
    return jnp.concatenate([picked[index] for index in range(count)], axis=axis)


def shards(
    hidden_in,
    segments,
    prefix_group,
    prefix_cache,
    page_table,
    norm_gain,
    w_query,
    w_keyval,
    w_out,
    moe_gain,
    routes,
    gates,
    w_gate_up,
    w_down,
):
    req_count = lax.axis_size("req")
    whole = gather_in_order(hidden_in, "hid", 1)
    tok_count = whole.shape[0]
    model_width = whole.shape[1]
    segment_row = segments[0]
    prefix_len = prefix_cache.shape[1]
    kv_heads = prefix_cache.shape[2]
    head_dim = prefix_cache.shape[3] // 2
    score_scale = head_dim ** (-0.5)
    normed = rms_scale(whole, norm_gain)
    position = positions_of(segment_row, prefix_len)
    projected = jnp.dot(normed, w_query, preferred_element_type=jnp.float32).reshape(
        tok_count, -1, head_dim
    )
    queries = rotate(projected, position).astype(jnp.bfloat16)
    q_groups = queries.shape[1] // kv_heads
    grouped_query = queries.reshape(tok_count, kv_heads, q_groups, head_dim)
    key_value = jnp.dot(normed, w_keyval, preferred_element_type=jnp.float32).reshape(
        tok_count, kv_heads, 2 * head_dim
    )
    key_rows = rotate(key_value[..., :head_dim], position).astype(jnp.bfloat16)
    value_rows = key_value[..., head_dim:].astype(jnp.bfloat16)
    pages = jnp.concatenate([key_rows, value_rows], axis=-1).reshape(
        -1, PAGE, kv_heads, 2 * head_dim
    )
    kv_pages = jnp.zeros_like(pages).at[page_table[0]].set(pages)
    token_index = jnp.arange(tok_count, dtype=jnp.int32)
    visible = (segment_row[None, :] == segment_row[:, None]) & (
        token_index[None, :] <= token_index[:, None]
    )
    local_scores = (
        jnp.einsum("tkgd,skd->kgts", grouped_query, key_rows, preferred_element_type=jnp.float32)
        * score_scale
    )
    local_scores = jnp.where(visible[None, None], local_scores, -jnp.inf)
    row_max = jnp.max(local_scores, axis=-1)
    numerators = jnp.exp(local_scores - row_max[..., None])
    totals = jnp.sum(numerators, axis=-1)
    weighted = jnp.einsum(
        "kgts,skd->kgtd",
        numerators.astype(jnp.bfloat16),
        value_rows,
        preferred_element_type=jnp.float32,
    )
    gathered = lax.all_gather(prefix_cache, "req", axis=0, tiled=True)
    window = tok_count // 2
    seg_count = prefix_group.shape[1]
    for seg in range(seg_count):
        start_row = jnp.minimum(jnp.sum((segment_row < seg).astype(jnp.int32)), tok_count - window)
        chosen = lax.dynamic_index_in_dim(gathered, prefix_group[0, seg], 0, keepdims=False)
        query_window = lax.dynamic_slice_in_dim(grouped_query, start_row, window, 0)
        scores = (
            jnp.einsum(
                "tkgd,skd->kgts",
                query_window,
                chosen[..., :head_dim],
                preferred_element_type=jnp.float32,
            )
            * score_scale
        )
        old_max = lax.dynamic_slice_in_dim(row_max, start_row, window, 2)
        old_total = lax.dynamic_slice_in_dim(totals, start_row, window, 2)
        old_weighted = lax.dynamic_slice_in_dim(weighted, start_row, window, 2)
        new_max = jnp.maximum(old_max, jnp.max(scores, axis=-1))
        decay_factor = jnp.exp(old_max - new_max)
        fresh = jnp.exp(scores - new_max[..., None])
        added = jnp.einsum(
            "kgts,skd->kgtd",
            fresh.astype(jnp.bfloat16),
            chosen[..., head_dim:],
            preferred_element_type=jnp.float32,
        )
        new_total = old_total * decay_factor + jnp.sum(fresh, axis=-1)
        new_weighted = old_weighted * decay_factor[..., None] + added
        inside = lax.dynamic_slice_in_dim(segment_row, start_row, window, 0) == seg
        row_max = lax.dynamic_update_slice_in_dim(
            row_max, jnp.where(inside[None, None], new_max, old_max), start_row, 2
        )
        totals = lax.dynamic_update_slice_in_dim(
            totals, jnp.where(inside[None, None], new_total, old_total), start_row, 2
        )
        weighted = lax.dynamic_update_slice_in_dim(
            weighted,
            jnp.where(inside[None, None, :, None], new_weighted, old_weighted),
            start_row,
            2,
        )
    attention = (
        (weighted / totals[..., None])
        .transpose(2, 0, 1, 3)
        .reshape(tok_count, -1)
        .astype(jnp.bfloat16)
    )
    share_width = hidden_in.shape[1]
    whole_attention = jnp.concatenate(shifted_copies(attention, "hid"), axis=1)
    whole_w_out = jnp.concatenate(shifted_copies(w_out, "hid"), axis=0)
    projected_out = jnp.dot(whole_attention, whole_w_out, preferred_element_type=jnp.float32)
    middle = (whole.astype(jnp.float32) + projected_out).astype(jnp.bfloat16)
    middle_share = lax.dynamic_slice_in_dim(
        middle, lax.axis_index("hid") * share_width, share_width, 1
    )
    normed_moe = rms_scale(middle, moe_gain)
    all_gate_up = lax.all_gather(w_gate_up, "req", axis=0, tiled=True)
    local_experts = w_down.shape[0]
    all_down = jnp.concatenate(shifted_copies(w_down, "req"), axis=0)
    experts = all_down.shape[0]
    down_ids = (
        (lax.axis_index("req") - jnp.arange(req_count, dtype=jnp.int32)[:, None]) % req_count
    ) * local_experts + jnp.arange(local_experts, dtype=jnp.int32)[None, :]
    order = down_ids.reshape(-1)
    expert_ids = jnp.arange(experts, dtype=jnp.int32)
    combine = jnp.sum(
        jnp.where(routes[:, :, None] == expert_ids[None, None, :], gates[:, :, None], 0.0), axis=1
    )
    gate_proj = jnp.einsum(
        "td,edf->tef", normed_moe, all_gate_up[:, 0], preferred_element_type=jnp.float32
    )
    up_proj = jnp.einsum(
        "td,edf->tef", normed_moe, all_gate_up[:, 1], preferred_element_type=jnp.float32
    )
    hidden = (jax.nn.silu(gate_proj) * up_proj * combine[:, :, None]).astype(jnp.bfloat16)
    partial_out = jnp.einsum(
        "tef,efd->td", jnp.take(hidden, order, axis=1), all_down, preferred_element_type=jnp.float32
    )
    expert_sum = lax.psum_scatter(
        partial_out.astype(jnp.bfloat16), "hid", scatter_dimension=1, tiled=True
    ).astype(jnp.float32)
    hidden_out = (middle_share.astype(jnp.float32) + expert_sum).astype(jnp.bfloat16)
    return (hidden_out, kv_pages)


def solution(mesh):
    in_specs = (
        P("req", "hid"),
        P("req", None),
        P("req", None),
        P("req", None, "hid", None),
        P("req", None),
        P(),
        P(None, "hid"),
        P(None, "hid"),
        P("hid", None),
        P(),
        P("req", None),
        P("req", None),
        P("req", None, None, "hid"),
        P("req", "hid", None),
    )
    out_specs = (P("req", "hid"), P("req", None, "hid", None))
    return jax.shard_map(shards, mesh=mesh, in_specs=in_specs, out_specs=out_specs, check_vma=False)
```

```python
import jax
import jax.numpy as jnp
from jax import lax
from jax.sharding import PartitionSpec as P

PAGE = 128


EPSILON = 1e-06
THETA = 10000.0


def rms_scale(row_data, gain_row):
    floats = row_data.astype(jnp.float32)
    mean_square = jnp.mean(floats * floats, axis=-1, keepdims=True)
    return (floats * lax.rsqrt(mean_square + EPSILON) * gain_row).astype(jnp.bfloat16)


def rotate(features, positions):
    half_dim = features.shape[-1] // 2
    frequency = THETA ** (-2.0 * jnp.arange(half_dim, dtype=jnp.float32) / features.shape[-1])
    angles = positions.astype(jnp.float32)[:, None] * frequency[None, :]
    cosine = jnp.cos(angles)[:, None, :]
    sine_part = jnp.sin(angles)[:, None, :]
    front_half = features[..., :half_dim]
    second = features[..., half_dim:]
    return jnp.concatenate(
        [front_half * cosine - second * sine_part, second * cosine + front_half * sine_part],
        axis=-1,
    )


def positions_of(segment_row, offset):
    earlier = jnp.sum((segment_row[None, :] < segment_row[:, None]).astype(jnp.int32), axis=1)
    token_index = jnp.arange(segment_row.shape[0], dtype=jnp.int32)
    return token_index - earlier + offset


def slots_of(route_rows, experts):
    flat_routes = route_rows.reshape(-1)
    onehot = (flat_routes[:, None] == jnp.arange(experts, dtype=jnp.int32)[None, :]).astype(
        jnp.int32
    )
    before = jnp.cumsum(onehot, axis=0) - onehot
    return (flat_routes, jnp.sum(before * onehot, axis=1))


def expert_rows(received, gate_up, down_proj):
    local_experts = down_proj.shape[0]
    slot_count = received.shape[1]
    model_width = received.shape[2]
    grouped = received.reshape(-1, local_experts, slot_count, model_width)
    gate_proj = jnp.einsum(
        "recd,edf->recf", grouped, gate_up[:, 0], preferred_element_type=jnp.float32
    )
    up_proj = jnp.einsum(
        "recd,edf->recf", grouped, gate_up[:, 1], preferred_element_type=jnp.float32
    )
    hidden = (jax.nn.silu(gate_proj) * up_proj).astype(jnp.bfloat16)
    produced = jnp.einsum("recf,efd->recd", hidden, down_proj, preferred_element_type=jnp.float32)
    return produced.reshape(-1, slot_count, model_width)


def shifted_copies(block, axis_name):
    count = lax.axis_size(axis_name)
    copies = [block]
    for shift in range(1, count):
        pairs = [(index, (index + shift) % count) for index in range(count)]
        copies.append(lax.ppermute(block, axis_name, pairs))
    return copies


def gather_in_order(block, axis_name, axis):
    count = lax.axis_size(axis_name)
    copies = jnp.stack(shifted_copies(block, axis_name))
    order = (lax.axis_index(axis_name) - jnp.arange(count, dtype=jnp.int32)) % count
    picked = jnp.take(copies, order, axis=0)
    return jnp.concatenate([picked[index] for index in range(count)], axis=axis)


def cross_chip_copies(block, axis_name):
    count = lax.axis_size(axis_name)
    pair = 2 if count % 2 == 0 else 1
    chips = count // pair
    me = lax.axis_index(axis_name)
    chip, core = me // pair, me % pair
    copies, sources = [block], [me]
    for shift in range(1, chips):
        pairs = [
            (c * pair + k, ((c + shift) % chips) * pair + k)
            for c in range(chips)
            for k in range(pair)
        ]
        copies.append(lax.ppermute(block, axis_name, pairs))
        sources.append(((chip - shift) % chips) * pair + core)
    return copies, sources


def sibling_copies(copies, sources, axis_name):
    count = lax.axis_size(axis_name)
    if count % 2:
        return list(copies), list(sources)
    swap = [(index, index + 1 - 2 * (index % 2)) for index in range(count)]
    moved = [lax.ppermute(piece, axis_name, swap) for piece in copies]
    flipped = [source + 1 - 2 * (source % 2) for source in sources]
    return list(copies) + moved, list(sources) + flipped


def shards(
    hidden_in,
    segments,
    prefix_group,
    prefix_cache,
    page_table,
    norm_gain,
    w_query,
    w_keyval,
    w_out,
    moe_gain,
    routes,
    gates,
    w_gate_up,
    w_down,
):
    req_count = lax.axis_size("req")
    whole = gather_in_order(hidden_in, "hid", 1)
    tok_count = whole.shape[0]
    model_width = whole.shape[1]
    segment_row = segments[0]
    prefix_len = prefix_cache.shape[1]
    kv_heads = prefix_cache.shape[2]
    head_dim = prefix_cache.shape[3] // 2
    score_scale = head_dim ** (-0.5)
    normed = rms_scale(whole, norm_gain)
    position = positions_of(segment_row, prefix_len)
    projected = jnp.dot(normed, w_query, preferred_element_type=jnp.float32).reshape(
        tok_count, -1, head_dim
    )
    queries = rotate(projected, position).astype(jnp.bfloat16)
    q_groups = queries.shape[1] // kv_heads
    grouped_query = queries.reshape(tok_count, kv_heads, q_groups, head_dim)
    key_value = jnp.dot(normed, w_keyval, preferred_element_type=jnp.float32).reshape(
        tok_count, kv_heads, 2 * head_dim
    )
    key_rows = rotate(key_value[..., :head_dim], position).astype(jnp.bfloat16)
    value_rows = key_value[..., head_dim:].astype(jnp.bfloat16)
    pages = jnp.concatenate([key_rows, value_rows], axis=-1).reshape(
        -1, PAGE, kv_heads, 2 * head_dim
    )
    kv_pages = jnp.zeros_like(pages).at[page_table[0]].set(pages)
    token_index = jnp.arange(tok_count, dtype=jnp.int32)
    visible = (segment_row[None, :] == segment_row[:, None]) & (
        token_index[None, :] <= token_index[:, None]
    )
    local_scores = (
        jnp.einsum("tkgd,skd->kgts", grouped_query, key_rows, preferred_element_type=jnp.float32)
        * score_scale
    )
    local_scores = jnp.where(visible[None, None], local_scores, -jnp.inf)
    row_max = jnp.max(local_scores, axis=-1)
    numerators = jnp.exp(local_scores - row_max[..., None])
    totals = jnp.sum(numerators, axis=-1)
    weighted = jnp.einsum(
        "kgts,skd->kgtd",
        numerators.astype(jnp.bfloat16),
        value_rows,
        preferred_element_type=jnp.float32,
    )
    prefix_near, prefix_from = cross_chip_copies(prefix_cache, "req")
    w_gate_up, w_down, prefix_near = lax.optimization_barrier((w_gate_up, w_down, prefix_near))
    prefix_all, prefix_from = sibling_copies(prefix_near, prefix_from, "req")
    gathered = jnp.concatenate(prefix_all, axis=0)
    local_groups = prefix_cache.shape[0]
    group_owner = prefix_group[0] // local_groups
    owner_slot = sum(
        jnp.where(group_owner == source, position, 0) for position, source in enumerate(prefix_from)
    )
    group_place = owner_slot * local_groups + prefix_group[0] % local_groups
    window = tok_count // 2
    seg_count = prefix_group.shape[1]
    for seg in range(seg_count):
        start_row = jnp.minimum(jnp.sum((segment_row < seg).astype(jnp.int32)), tok_count - window)
        chosen = lax.dynamic_index_in_dim(gathered, group_place[seg], 0, keepdims=False)
        query_window = lax.dynamic_slice_in_dim(grouped_query, start_row, window, 0)
        scores = (
            jnp.einsum(
                "tkgd,skd->kgts",
                query_window,
                chosen[..., :head_dim],
                preferred_element_type=jnp.float32,
            )
            * score_scale
        )
        old_max = lax.dynamic_slice_in_dim(row_max, start_row, window, 2)
        old_total = lax.dynamic_slice_in_dim(totals, start_row, window, 2)
        old_weighted = lax.dynamic_slice_in_dim(weighted, start_row, window, 2)
        new_max = jnp.maximum(old_max, jnp.max(scores, axis=-1))
        decay_factor = jnp.exp(old_max - new_max)
        fresh = jnp.exp(scores - new_max[..., None])
        added = jnp.einsum(
            "kgts,skd->kgtd",
            fresh.astype(jnp.bfloat16),
            chosen[..., head_dim:],
            preferred_element_type=jnp.float32,
        )
        new_total = old_total * decay_factor + jnp.sum(fresh, axis=-1)
        new_weighted = old_weighted * decay_factor[..., None] + added
        inside = lax.dynamic_slice_in_dim(segment_row, start_row, window, 0) == seg
        row_max = lax.dynamic_update_slice_in_dim(
            row_max, jnp.where(inside[None, None], new_max, old_max), start_row, 2
        )
        totals = lax.dynamic_update_slice_in_dim(
            totals, jnp.where(inside[None, None], new_total, old_total), start_row, 2
        )
        weighted = lax.dynamic_update_slice_in_dim(
            weighted,
            jnp.where(inside[None, None, :, None], new_weighted, old_weighted),
            start_row,
            2,
        )
    attention = (
        (weighted / totals[..., None])
        .transpose(2, 0, 1, 3)
        .reshape(tok_count, -1)
        .astype(jnp.bfloat16)
    )
    share_width = hidden_in.shape[1]
    whole_attention = jnp.concatenate(shifted_copies(attention, "hid"), axis=1)
    whole_w_out = jnp.concatenate(shifted_copies(w_out, "hid"), axis=0)
    projected_out = jnp.dot(whole_attention, whole_w_out, preferred_element_type=jnp.float32)
    middle = (whole.astype(jnp.float32) + projected_out).astype(jnp.bfloat16)
    middle_share = lax.dynamic_slice_in_dim(
        middle, lax.axis_index("hid") * share_width, share_width, 1
    )
    normed_moe = rms_scale(middle, moe_gain)
    local_experts = w_down.shape[0]
    gate_up_near, weight_from = cross_chip_copies(w_gate_up, "req")
    down_near, _ = cross_chip_copies(w_down, "req")
    gate_up_all, weight_from_all = sibling_copies(gate_up_near, weight_from, "req")
    down_all, _ = sibling_copies(down_near, weight_from, "req")
    local_ids = jnp.arange(local_experts, dtype=jnp.int32)
    partial_out = jnp.zeros((tok_count, model_width), jnp.float32)
    for gate_up_piece, down_piece, source in zip(gate_up_all, down_all, weight_from_all):
        piece_ids = source * local_experts + local_ids
        combine = jnp.sum(
            jnp.where(routes[:, :, None] == piece_ids[None, None, :], gates[:, :, None], 0.0),
            axis=1,
        )
        gate_proj = jnp.einsum(
            "td,edf->tef", normed_moe, gate_up_piece[:, 0], preferred_element_type=jnp.float32
        )
        up_proj = jnp.einsum(
            "td,edf->tef", normed_moe, gate_up_piece[:, 1], preferred_element_type=jnp.float32
        )
        hidden = (jax.nn.silu(gate_proj) * up_proj * combine[:, :, None]).astype(jnp.bfloat16)
        partial_out = partial_out + jnp.einsum(
            "tef,efd->td", hidden, down_piece, preferred_element_type=jnp.float32
        )
    expert_sum = lax.psum_scatter(
        partial_out.astype(jnp.bfloat16), "hid", scatter_dimension=1, tiled=True
    ).astype(jnp.float32)
    hidden_out = (middle_share.astype(jnp.float32) + expert_sum).astype(jnp.bfloat16)
    return (hidden_out, kv_pages)


def solution(mesh):
    in_specs = (
        P("req", "hid"),
        P("req", None),
        P("req", None),
        P("req", None, "hid", None),
        P("req", None),
        P(),
        P(None, "hid"),
        P(None, "hid"),
        P("hid", None),
        P(),
        P("req", None),
        P("req", None),
        P("req", None, None, "hid"),
        P("req", "hid", None),
    )
    out_specs = (P("req", "hid"), P("req", None, "hid", None))
    return jax.shard_map(shards, mesh=mesh, in_specs=in_specs, out_specs=out_specs, check_vma=False)
```

```python
import jax
import jax.numpy as jnp
from jax import lax
from jax.sharding import PartitionSpec as P

PAGE = 128


EPSILON = 1e-06
THETA = 10000.0


def rms_scale(row_data, gain_row):
    floats = row_data.astype(jnp.float32)
    mean_square = jnp.mean(floats * floats, axis=-1, keepdims=True)
    return (floats * lax.rsqrt(mean_square + EPSILON) * gain_row).astype(jnp.bfloat16)


def rotate(features, positions):
    half_dim = features.shape[-1] // 2
    frequency = THETA ** (-2.0 * jnp.arange(half_dim, dtype=jnp.float32) / features.shape[-1])
    angles = positions.astype(jnp.float32)[:, None] * frequency[None, :]
    cosine = jnp.cos(angles)[:, None, :]
    sine_part = jnp.sin(angles)[:, None, :]
    front_half = features[..., :half_dim]
    second = features[..., half_dim:]
    return jnp.concatenate(
        [front_half * cosine - second * sine_part, second * cosine + front_half * sine_part],
        axis=-1,
    )


def positions_of(segment_row, offset):
    earlier = jnp.sum((segment_row[None, :] < segment_row[:, None]).astype(jnp.int32), axis=1)
    token_index = jnp.arange(segment_row.shape[0], dtype=jnp.int32)
    return token_index - earlier + offset


def slots_of(route_rows, experts):
    flat_routes = route_rows.reshape(-1)
    onehot = (flat_routes[:, None] == jnp.arange(experts, dtype=jnp.int32)[None, :]).astype(
        jnp.int32
    )
    before = jnp.cumsum(onehot, axis=0) - onehot
    return (flat_routes, jnp.sum(before * onehot, axis=1))


def expert_rows(received, gate_up, down_proj):
    local_experts = down_proj.shape[0]
    slot_count = received.shape[1]
    model_width = received.shape[2]
    grouped = received.reshape(-1, local_experts, slot_count, model_width)
    gate_proj = jnp.einsum(
        "recd,edf->recf", grouped, gate_up[:, 0], preferred_element_type=jnp.float32
    )
    up_proj = jnp.einsum(
        "recd,edf->recf", grouped, gate_up[:, 1], preferred_element_type=jnp.float32
    )
    hidden = (jax.nn.silu(gate_proj) * up_proj).astype(jnp.bfloat16)
    produced = jnp.einsum("recf,efd->recd", hidden, down_proj, preferred_element_type=jnp.float32)
    return produced.reshape(-1, slot_count, model_width)


def shifted_copies(block, axis_name):
    count = lax.axis_size(axis_name)
    copies = [block]
    for shift in range(1, count):
        pairs = [(index, (index + shift) % count) for index in range(count)]
        copies.append(lax.ppermute(block, axis_name, pairs))
    return copies


def gather_in_order(block, axis_name, axis):
    count = lax.axis_size(axis_name)
    copies = jnp.stack(shifted_copies(block, axis_name))
    order = (lax.axis_index(axis_name) - jnp.arange(count, dtype=jnp.int32)) % count
    picked = jnp.take(copies, order, axis=0)
    return jnp.concatenate([picked[index] for index in range(count)], axis=axis)


def shards(
    hidden_in,
    segments,
    prefix_group,
    prefix_cache,
    page_table,
    norm_gain,
    w_query,
    w_keyval,
    w_out,
    moe_gain,
    routes,
    gates,
    w_gate_up,
    w_down,
):
    req_count = lax.axis_size("req")
    whole = gather_in_order(hidden_in, "hid", 1)
    tok_count = whole.shape[0]
    model_width = whole.shape[1]
    segment_row = segments[0]
    prefix_len = prefix_cache.shape[1]
    kv_heads = prefix_cache.shape[2]
    head_dim = prefix_cache.shape[3] // 2
    score_scale = head_dim ** (-0.5)
    normed = rms_scale(whole, norm_gain)
    position = positions_of(segment_row, prefix_len)
    projected = jnp.dot(normed, w_query, preferred_element_type=jnp.float32).reshape(
        tok_count, -1, head_dim
    )
    queries = rotate(projected, position).astype(jnp.bfloat16)
    queries, w_gate_up, w_down = lax.optimization_barrier((queries, w_gate_up, w_down))
    q_groups = queries.shape[1] // kv_heads
    grouped_query = queries.reshape(tok_count, kv_heads, q_groups, head_dim)
    key_value = jnp.dot(normed, w_keyval, preferred_element_type=jnp.float32).reshape(
        tok_count, kv_heads, 2 * head_dim
    )
    key_rows = rotate(key_value[..., :head_dim], position).astype(jnp.bfloat16)
    value_rows = key_value[..., head_dim:].astype(jnp.bfloat16)
    pages = jnp.concatenate([key_rows, value_rows], axis=-1).reshape(
        -1, PAGE, kv_heads, 2 * head_dim
    )
    kv_pages = jnp.zeros_like(pages).at[page_table[0]].set(pages)
    token_index = jnp.arange(tok_count, dtype=jnp.int32)
    visible = (segment_row[None, :] == segment_row[:, None]) & (
        token_index[None, :] <= token_index[:, None]
    )
    local_scores = (
        jnp.einsum("tkgd,skd->kgts", grouped_query, key_rows, preferred_element_type=jnp.float32)
        * score_scale
    )
    local_scores = jnp.where(visible[None, None], local_scores, -jnp.inf)
    row_max = jnp.max(local_scores, axis=-1)
    numerators = jnp.exp(local_scores - row_max[..., None])
    totals = jnp.sum(numerators, axis=-1)
    weighted = jnp.einsum(
        "kgts,skd->kgtd",
        numerators.astype(jnp.bfloat16),
        value_rows,
        preferred_element_type=jnp.float32,
    )
    gathered = lax.all_gather(prefix_cache, "req", axis=0, tiled=True)
    window = tok_count // 2
    seg_count = prefix_group.shape[1]
    for seg in range(seg_count):
        start_row = jnp.minimum(jnp.sum((segment_row < seg).astype(jnp.int32)), tok_count - window)
        chosen = lax.dynamic_index_in_dim(gathered, prefix_group[0, seg], 0, keepdims=False)
        query_window = lax.dynamic_slice_in_dim(grouped_query, start_row, window, 0)
        scores = (
            jnp.einsum(
                "tkgd,skd->kgts",
                query_window,
                chosen[..., :head_dim],
                preferred_element_type=jnp.float32,
            )
            * score_scale
        )
        old_max = lax.dynamic_slice_in_dim(row_max, start_row, window, 2)
        old_total = lax.dynamic_slice_in_dim(totals, start_row, window, 2)
        old_weighted = lax.dynamic_slice_in_dim(weighted, start_row, window, 2)
        new_max = jnp.maximum(old_max, jnp.max(scores, axis=-1))
        decay_factor = jnp.exp(old_max - new_max)
        fresh = jnp.exp(scores - new_max[..., None])
        added = jnp.einsum(
            "kgts,skd->kgtd",
            fresh.astype(jnp.bfloat16),
            chosen[..., head_dim:],
            preferred_element_type=jnp.float32,
        )
        new_total = old_total * decay_factor + jnp.sum(fresh, axis=-1)
        new_weighted = old_weighted * decay_factor[..., None] + added
        inside = lax.dynamic_slice_in_dim(segment_row, start_row, window, 0) == seg
        row_max = lax.dynamic_update_slice_in_dim(
            row_max, jnp.where(inside[None, None], new_max, old_max), start_row, 2
        )
        totals = lax.dynamic_update_slice_in_dim(
            totals, jnp.where(inside[None, None], new_total, old_total), start_row, 2
        )
        weighted = lax.dynamic_update_slice_in_dim(
            weighted,
            jnp.where(inside[None, None, :, None], new_weighted, old_weighted),
            start_row,
            2,
        )
    attention = (
        (weighted / totals[..., None])
        .transpose(2, 0, 1, 3)
        .reshape(tok_count, -1)
        .astype(jnp.bfloat16)
    )
    share_width = hidden_in.shape[1]
    whole_attention = jnp.concatenate(shifted_copies(attention, "hid"), axis=1)
    whole_w_out = jnp.concatenate(shifted_copies(w_out, "hid"), axis=0)
    projected_out = jnp.dot(whole_attention, whole_w_out, preferred_element_type=jnp.float32)
    middle = (whole.astype(jnp.float32) + projected_out).astype(jnp.bfloat16)
    middle_share = lax.dynamic_slice_in_dim(
        middle, lax.axis_index("hid") * share_width, share_width, 1
    )
    normed_moe = rms_scale(middle, moe_gain)
    all_gate_up = lax.all_gather(w_gate_up, "req", axis=0, tiled=True)
    all_down = lax.all_gather(w_down, "req", axis=0, tiled=True)
    experts = all_down.shape[0]
    expert_ids = jnp.arange(experts, dtype=jnp.int32)
    combine = jnp.sum(
        jnp.where(routes[:, :, None] == expert_ids[None, None, :], gates[:, :, None], 0.0), axis=1
    )
    gate_proj = jnp.einsum(
        "td,edf->tef", normed_moe, all_gate_up[:, 0], preferred_element_type=jnp.float32
    )
    up_proj = jnp.einsum(
        "td,edf->tef", normed_moe, all_gate_up[:, 1], preferred_element_type=jnp.float32
    )
    hidden = (jax.nn.silu(gate_proj) * up_proj * combine[:, :, None]).astype(jnp.bfloat16)
    partial_out = jnp.einsum(
        "tef,efd->td", hidden, all_down, preferred_element_type=jnp.float32
    )
    hid_count = lax.axis_size("hid")
    hid_index = lax.axis_index("hid")
    expert_sum = lax.dynamic_slice_in_dim(partial_out, hid_index * share_width, share_width, 1)
    for shift in range(1, hid_count):
        block = (hid_index + shift) % hid_count
        outgoing = lax.dynamic_slice_in_dim(partial_out, block * share_width, share_width, 1)
        pairs = [(index, (index + shift) % hid_count) for index in range(hid_count)]
        incoming = lax.ppermute(outgoing.astype(jnp.bfloat16), "hid", pairs)
        expert_sum = expert_sum + incoming.astype(jnp.float32)
    hidden_out = (middle_share.astype(jnp.float32) + expert_sum).astype(jnp.bfloat16)
    return (hidden_out, kv_pages)


def solution(mesh):
    in_specs = (
        P("req", "hid"),
        P("req", None),
        P("req", None),
        P("req", None, "hid", None),
        P("req", None),
        P(),
        P(None, "hid"),
        P(None, "hid"),
        P("hid", None),
        P(),
        P("req", None),
        P("req", None),
        P("req", None, None, "hid"),
        P("req", "hid", None),
    )
    out_specs = (P("req", "hid"), P("req", None, "hid", None))
    return jax.shard_map(shards, mesh=mesh, in_specs=in_specs, out_specs=out_specs, check_vma=False)
```

```python
import jax
import jax.numpy as jnp
from jax import lax
from jax.sharding import PartitionSpec as P
from jax.experimental import pallas as pl
from jax.experimental.pallas import tpu as pltpu

PAGE = 128


EPSILON = 1e-06
THETA = 10000.0


def rms_scale(row_data, gain_row):
    floats = row_data.astype(jnp.float32)
    mean_square = jnp.mean(floats * floats, axis=-1, keepdims=True)
    return (floats * lax.rsqrt(mean_square + EPSILON) * gain_row).astype(jnp.bfloat16)


def rotate(features, positions):
    half_dim = features.shape[-1] // 2
    frequency = THETA ** (-2.0 * jnp.arange(half_dim, dtype=jnp.float32) / features.shape[-1])
    angles = positions.astype(jnp.float32)[:, None] * frequency[None, :]
    cosine = jnp.cos(angles)[:, None, :]
    sine_part = jnp.sin(angles)[:, None, :]
    front_half = features[..., :half_dim]
    second = features[..., half_dim:]
    return jnp.concatenate(
        [front_half * cosine - second * sine_part, second * cosine + front_half * sine_part],
        axis=-1,
    )


def positions_of(segment_row, offset):
    earlier = jnp.sum((segment_row[None, :] < segment_row[:, None]).astype(jnp.int32), axis=1)
    token_index = jnp.arange(segment_row.shape[0], dtype=jnp.int32)
    return token_index - earlier + offset


def slots_of(route_rows, experts):
    flat_routes = route_rows.reshape(-1)
    onehot = (flat_routes[:, None] == jnp.arange(experts, dtype=jnp.int32)[None, :]).astype(
        jnp.int32
    )
    before = jnp.cumsum(onehot, axis=0) - onehot
    return (flat_routes, jnp.sum(before * onehot, axis=1))


def expert_rows(received, gate_up, down_proj):
    local_experts = down_proj.shape[0]
    slot_count = received.shape[1]
    model_width = received.shape[2]
    grouped = received.reshape(-1, local_experts, slot_count, model_width)
    gate_proj = jnp.einsum(
        "recd,edf->recf", grouped, gate_up[:, 0], preferred_element_type=jnp.float32
    )
    up_proj = jnp.einsum(
        "recd,edf->recf", grouped, gate_up[:, 1], preferred_element_type=jnp.float32
    )
    hidden = (jax.nn.silu(gate_proj) * up_proj).astype(jnp.bfloat16)
    produced = jnp.einsum("recf,efd->recd", hidden, down_proj, preferred_element_type=jnp.float32)
    return produced.reshape(-1, slot_count, model_width)


def shifted_copies(block, axis_name):
    count = lax.axis_size(axis_name)
    copies = [block]
    for shift in range(1, count):
        pairs = [(index, (index + shift) % count) for index in range(count)]
        copies.append(lax.ppermute(block, axis_name, pairs))
    return copies


def gather_in_order(block, axis_name, axis):
    count = lax.axis_size(axis_name)
    copies = jnp.stack(shifted_copies(block, axis_name))
    order = (lax.axis_index(axis_name) - jnp.arange(count, dtype=jnp.int32)) % count
    picked = jnp.take(copies, order, axis=0)
    return jnp.concatenate([picked[index] for index in range(count)], axis=axis)


def attention_body(group_ref, bound_ref, q_ref, k_ref, v_ref, segq_ref, segk_ref, prefix_ref, out_ref):
    block = pl.program_id(1)
    seg = pl.program_id(2)
    seg_count = pl.num_programs(2)
    rows = q_ref.shape[2]
    tokens = k_ref.shape[1]
    head_dim = q_ref.shape[3]

    @pl.when(seg == 0)
    def _():
        out_ref[...] = jnp.zeros_like(out_ref)

    first = bound_ref[seg]
    last = bound_ref[seg + seg_count]
    active = (first < (block + 1) * rows) & (last > block * rows)

    @pl.when(active)
    def _():
        seg_q = segq_ref[...]
        seg_k = segk_ref[...]
        t_idx = block * rows + lax.broadcasted_iota(jnp.int32, (rows, tokens), 0)
        u_idx = lax.broadcasted_iota(jnp.int32, (rows, tokens), 1)
        visible = (seg_q == seg_k) & (u_idx <= t_idx)
        keys = k_ref[0]
        values = v_ref[0]
        prefix = prefix_ref[0, 0]
        prefix_keys = prefix[:, :head_dim]
        prefix_values = prefix[:, head_dim:]
        scale = head_dim ** (-0.5)
        mine = seg_q == seg
        contract = (((1,), (1,)), ((), ()))
        for group in range(q_ref.shape[1]):
            query = q_ref[0, group]
            local = lax.dot_general(query, keys, contract, preferred_element_type=jnp.float32) * scale
            local = jnp.where(visible, local, -jnp.inf)
            cached = (
                lax.dot_general(query, prefix_keys, contract, preferred_element_type=jnp.float32)
                * scale
            )
            top = jnp.maximum(
                jnp.max(local, axis=1, keepdims=True), jnp.max(cached, axis=1, keepdims=True)
            )
            local_num = jnp.exp(local - top)
            cached_num = jnp.exp(cached - top)
            total = jnp.sum(local_num, axis=1, keepdims=True) + jnp.sum(
                cached_num, axis=1, keepdims=True
            )
            summed = jnp.dot(
                local_num.astype(jnp.bfloat16), values, preferred_element_type=jnp.float32
            ) + jnp.dot(
                cached_num.astype(jnp.bfloat16), prefix_values, preferred_element_type=jnp.float32
            )
            out_ref[0, group] = jnp.where(mine, summed / total, out_ref[0, group])


def attend(grouped_query, key_rows, value_rows, segment_row, group_row, prefix_heads, interpret=False):
    tok_count, kv_heads, q_groups, head_dim = grouped_query.shape
    seg_count = group_row.shape[0]
    prefix_len = prefix_heads.shape[2]
    rows = min(128, tok_count)
    labels = jnp.arange(seg_count, dtype=jnp.int32)
    first = jnp.sum((segment_row[None, :] < labels[:, None]).astype(jnp.int32), axis=1)
    last = jnp.sum((segment_row[None, :] <= labels[:, None]).astype(jnp.int32), axis=1)
    bounds = jnp.concatenate([first, last])
    query_heads = grouped_query.transpose(1, 2, 0, 3)
    key_heads = key_rows.transpose(1, 0, 2)
    value_heads = value_rows.transpose(1, 0, 2)
    seg_col = segment_row.reshape(tok_count, 1)
    seg_line = segment_row.reshape(1, tok_count)
    grid_spec = pltpu.PrefetchScalarGridSpec(
        num_scalar_prefetch=2,
        grid=(kv_heads, tok_count // rows, seg_count),
        in_specs=[
            pl.BlockSpec((1, q_groups, rows, head_dim), lambda h, b, s, gr, bd: (h, 0, b, 0)),
            pl.BlockSpec((1, tok_count, head_dim), lambda h, b, s, gr, bd: (h, 0, 0)),
            pl.BlockSpec((1, tok_count, head_dim), lambda h, b, s, gr, bd: (h, 0, 0)),
            pl.BlockSpec((rows, 1), lambda h, b, s, gr, bd: (b, 0)),
            pl.BlockSpec((1, tok_count), lambda h, b, s, gr, bd: (0, 0)),
            pl.BlockSpec(
                (1, 1, prefix_len, 2 * head_dim), lambda h, b, s, gr, bd: (gr[s], h, 0, 0)
            ),
        ],
        out_specs=pl.BlockSpec((1, q_groups, rows, head_dim), lambda h, b, s, gr, bd: (h, 0, b, 0)),
    )
    out = pl.pallas_call(
        attention_body,
        grid_spec=grid_spec,
        out_shape=jax.ShapeDtypeStruct((kv_heads, q_groups, tok_count, head_dim), jnp.float32),
        compiler_params=pltpu.CompilerParams(
            dimension_semantics=("arbitrary", "arbitrary", "arbitrary")
        ),
        interpret=interpret,
    )(group_row, bounds, query_heads, key_heads, value_heads, seg_col, seg_line, prefix_heads)
    return out.transpose(2, 0, 1, 3).reshape(tok_count, -1).astype(jnp.bfloat16)


def shards(
    hidden_in,
    segments,
    prefix_group,
    prefix_cache,
    page_table,
    norm_gain,
    w_query,
    w_keyval,
    w_out,
    moe_gain,
    routes,
    gates,
    w_gate_up,
    w_down,
):
    req_count = lax.axis_size("req")
    whole = gather_in_order(hidden_in, "hid", 1)
    tok_count = whole.shape[0]
    model_width = whole.shape[1]
    segment_row = segments[0]
    prefix_len = prefix_cache.shape[1]
    kv_heads = prefix_cache.shape[2]
    head_dim = prefix_cache.shape[3] // 2
    score_scale = head_dim ** (-0.5)
    normed = rms_scale(whole, norm_gain)
    position = positions_of(segment_row, prefix_len)
    projected = jnp.dot(normed, w_query, preferred_element_type=jnp.float32).reshape(
        tok_count, -1, head_dim
    )
    queries = rotate(projected, position).astype(jnp.bfloat16)
    queries, w_gate_up, w_down = lax.optimization_barrier((queries, w_gate_up, w_down))
    q_groups = queries.shape[1] // kv_heads
    grouped_query = queries.reshape(tok_count, kv_heads, q_groups, head_dim)
    key_value = jnp.dot(normed, w_keyval, preferred_element_type=jnp.float32).reshape(
        tok_count, kv_heads, 2 * head_dim
    )
    key_rows = rotate(key_value[..., :head_dim], position).astype(jnp.bfloat16)
    value_rows = key_value[..., head_dim:].astype(jnp.bfloat16)
    pages = jnp.concatenate([key_rows, value_rows], axis=-1).reshape(
        -1, PAGE, kv_heads, 2 * head_dim
    )
    kv_pages = jnp.zeros_like(pages).at[page_table[0]].set(pages)
    gathered = lax.all_gather(prefix_cache, "req", axis=0, tiled=True)
    attention = attend(
        grouped_query, key_rows, value_rows, segment_row, prefix_group[0],
        gathered.transpose(0, 2, 1, 3),
    )
    share_width = hidden_in.shape[1]
    whole_attention = jnp.concatenate(shifted_copies(attention, "hid"), axis=1)
    whole_w_out = jnp.concatenate(shifted_copies(w_out, "hid"), axis=0)
    projected_out = jnp.dot(whole_attention, whole_w_out, preferred_element_type=jnp.float32)
    middle = (whole.astype(jnp.float32) + projected_out).astype(jnp.bfloat16)
    middle_share = lax.dynamic_slice_in_dim(
        middle, lax.axis_index("hid") * share_width, share_width, 1
    )
    normed_moe = rms_scale(middle, moe_gain)
    all_gate_up = lax.all_gather(w_gate_up, "req", axis=0, tiled=True)
    all_down = lax.all_gather(w_down, "req", axis=0, tiled=True)
    experts = all_down.shape[0]
    expert_ids = jnp.arange(experts, dtype=jnp.int32)
    combine = jnp.sum(
        jnp.where(routes[:, :, None] == expert_ids[None, None, :], gates[:, :, None], 0.0), axis=1
    )
    gate_proj = jnp.einsum(
        "td,edf->tef", normed_moe, all_gate_up[:, 0], preferred_element_type=jnp.float32
    )
    up_proj = jnp.einsum(
        "td,edf->tef", normed_moe, all_gate_up[:, 1], preferred_element_type=jnp.float32
    )
    hidden = (jax.nn.silu(gate_proj) * up_proj * combine[:, :, None]).astype(jnp.bfloat16)
    partial_out = jnp.einsum(
        "tef,efd->td", hidden, all_down, preferred_element_type=jnp.float32
    )
    hid_count = lax.axis_size("hid")
    hid_index = lax.axis_index("hid")
    expert_sum = lax.dynamic_slice_in_dim(partial_out, hid_index * share_width, share_width, 1)
    for shift in range(1, hid_count):
        block = (hid_index + shift) % hid_count
        outgoing = lax.dynamic_slice_in_dim(partial_out, block * share_width, share_width, 1)
        pairs = [(index, (index + shift) % hid_count) for index in range(hid_count)]
        incoming = lax.ppermute(outgoing.astype(jnp.bfloat16), "hid", pairs)
        expert_sum = expert_sum + incoming.astype(jnp.float32)
    hidden_out = (middle_share.astype(jnp.float32) + expert_sum).astype(jnp.bfloat16)
    return (hidden_out, kv_pages)


def solution(mesh):
    in_specs = (
        P("req", "hid"),
        P("req", None),
        P("req", None),
        P("req", None, "hid", None),
        P("req", None),
        P(),
        P(None, "hid"),
        P(None, "hid"),
        P("hid", None),
        P(),
        P("req", None),
        P("req", None),
        P("req", None, None, "hid"),
        P("req", "hid", None),
    )
    out_specs = (P("req", "hid"), P("req", None, "hid", None))
    return jax.shard_map(shards, mesh=mesh, in_specs=in_specs, out_specs=out_specs, check_vma=False)
```

```python
import functools

import jax
import jax.numpy as jnp
from jax import lax
from jax.sharding import PartitionSpec as P
from jax.experimental import pallas as pl
from jax.experimental.pallas import tpu as pltpu

PAGE = 128


EPSILON = 1e-06
THETA = 10000.0


def rms_scale(row_data, gain_row):
    floats = row_data.astype(jnp.float32)
    mean_square = jnp.mean(floats * floats, axis=-1, keepdims=True)
    return (floats * lax.rsqrt(mean_square + EPSILON) * gain_row).astype(jnp.bfloat16)


def rotate(features, positions):
    half_dim = features.shape[-1] // 2
    frequency = THETA ** (-2.0 * jnp.arange(half_dim, dtype=jnp.float32) / features.shape[-1])
    angles = positions.astype(jnp.float32)[:, None] * frequency[None, :]
    cosine = jnp.cos(angles)[:, None, :]
    sine_part = jnp.sin(angles)[:, None, :]
    front_half = features[..., :half_dim]
    second = features[..., half_dim:]
    return jnp.concatenate(
        [front_half * cosine - second * sine_part, second * cosine + front_half * sine_part],
        axis=-1,
    )


def positions_of(segment_row, offset):
    earlier = jnp.sum((segment_row[None, :] < segment_row[:, None]).astype(jnp.int32), axis=1)
    token_index = jnp.arange(segment_row.shape[0], dtype=jnp.int32)
    return token_index - earlier + offset


def slots_of(route_rows, experts):
    flat_routes = route_rows.reshape(-1)
    onehot = (flat_routes[:, None] == jnp.arange(experts, dtype=jnp.int32)[None, :]).astype(
        jnp.int32
    )
    before = jnp.cumsum(onehot, axis=0) - onehot
    return (flat_routes, jnp.sum(before * onehot, axis=1))


def expert_rows(received, gate_up, down_proj):
    local_experts = down_proj.shape[0]
    slot_count = received.shape[1]
    model_width = received.shape[2]
    grouped = received.reshape(-1, local_experts, slot_count, model_width)
    gate_proj = jnp.einsum(
        "recd,edf->recf", grouped, gate_up[:, 0], preferred_element_type=jnp.float32
    )
    up_proj = jnp.einsum(
        "recd,edf->recf", grouped, gate_up[:, 1], preferred_element_type=jnp.float32
    )
    hidden = (jax.nn.silu(gate_proj) * up_proj).astype(jnp.bfloat16)
    produced = jnp.einsum("recf,efd->recd", hidden, down_proj, preferred_element_type=jnp.float32)
    return produced.reshape(-1, slot_count, model_width)


def shifted_copies(block, axis_name):
    count = lax.axis_size(axis_name)
    copies = [block]
    for shift in range(1, count):
        pairs = [(index, (index + shift) % count) for index in range(count)]
        copies.append(lax.ppermute(block, axis_name, pairs))
    return copies


def gather_in_order(block, axis_name, axis):
    count = lax.axis_size(axis_name)
    copies = jnp.stack(shifted_copies(block, axis_name))
    order = (lax.axis_index(axis_name) - jnp.arange(count, dtype=jnp.int32)) % count
    picked = jnp.take(copies, order, axis=0)
    return jnp.concatenate([picked[index] for index in range(count)], axis=axis)


def attention_body(group_ref, bound_ref, q_ref, k_ref, v_ref, segq_ref, segk_ref, prefix_ref, out_ref):
    block = pl.program_id(1)
    seg = pl.program_id(2)
    seg_count = pl.num_programs(2)
    rows = q_ref.shape[2]
    tokens = k_ref.shape[1]
    head_dim = q_ref.shape[3]

    @pl.when(seg == 0)
    def _():
        out_ref[...] = jnp.zeros_like(out_ref)

    first = bound_ref[seg]
    last = bound_ref[seg + seg_count]
    active = (first < (block + 1) * rows) & (last > block * rows)

    @pl.when(active)
    def _():
        seg_q = segq_ref[...]
        seg_k = segk_ref[...]
        t_idx = block * rows + lax.broadcasted_iota(jnp.int32, (rows, tokens), 0)
        u_idx = lax.broadcasted_iota(jnp.int32, (rows, tokens), 1)
        visible = (seg_q == seg_k) & (u_idx <= t_idx)
        keys = k_ref[0]
        values = v_ref[0]
        prefix = prefix_ref[0, 0]
        prefix_keys = prefix[:, :head_dim]
        prefix_values = prefix[:, head_dim:]
        scale = head_dim ** (-0.5)
        mine = seg_q == seg
        contract = (((1,), (1,)), ((), ()))
        for group in range(q_ref.shape[1]):
            query = q_ref[0, group]
            local = lax.dot_general(query, keys, contract, preferred_element_type=jnp.float32) * scale
            local = jnp.where(visible, local, -jnp.inf)
            cached = (
                lax.dot_general(query, prefix_keys, contract, preferred_element_type=jnp.float32)
                * scale
            )
            top = jnp.maximum(
                jnp.max(local, axis=1, keepdims=True), jnp.max(cached, axis=1, keepdims=True)
            )
            local_num = jnp.exp(local - top)
            cached_num = jnp.exp(cached - top)
            total = jnp.sum(local_num, axis=1, keepdims=True) + jnp.sum(
                cached_num, axis=1, keepdims=True
            )
            summed = jnp.dot(
                local_num.astype(jnp.bfloat16), values, preferred_element_type=jnp.float32
            ) + jnp.dot(
                cached_num.astype(jnp.bfloat16), prefix_values, preferred_element_type=jnp.float32
            )
            out_ref[0, group] = jnp.where(mine, summed / total, out_ref[0, group])


def attend(grouped_query, key_rows, value_rows, segment_row, group_row, prefix_heads, interpret=False):
    tok_count, kv_heads, q_groups, head_dim = grouped_query.shape
    seg_count = group_row.shape[0]
    prefix_len = prefix_heads.shape[2]
    rows = min(128, tok_count)
    labels = jnp.arange(seg_count, dtype=jnp.int32)
    first = jnp.sum((segment_row[None, :] < labels[:, None]).astype(jnp.int32), axis=1)
    last = jnp.sum((segment_row[None, :] <= labels[:, None]).astype(jnp.int32), axis=1)
    bounds = jnp.concatenate([first, last])
    query_heads = grouped_query.transpose(1, 2, 0, 3)
    key_heads = key_rows.transpose(1, 0, 2)
    value_heads = value_rows.transpose(1, 0, 2)
    seg_col = segment_row.reshape(tok_count, 1)
    seg_line = segment_row.reshape(1, tok_count)
    grid_spec = pltpu.PrefetchScalarGridSpec(
        num_scalar_prefetch=2,
        grid=(kv_heads, tok_count // rows, seg_count),
        in_specs=[
            pl.BlockSpec((1, q_groups, rows, head_dim), lambda h, b, s, gr, bd: (h, 0, b, 0)),
            pl.BlockSpec((1, tok_count, head_dim), lambda h, b, s, gr, bd: (h, 0, 0)),
            pl.BlockSpec((1, tok_count, head_dim), lambda h, b, s, gr, bd: (h, 0, 0)),
            pl.BlockSpec((rows, 1), lambda h, b, s, gr, bd: (b, 0)),
            pl.BlockSpec((1, tok_count), lambda h, b, s, gr, bd: (0, 0)),
            pl.BlockSpec(
                (1, 1, prefix_len, 2 * head_dim), lambda h, b, s, gr, bd: (gr[s], h, 0, 0)
            ),
        ],
        out_specs=pl.BlockSpec((1, q_groups, rows, head_dim), lambda h, b, s, gr, bd: (h, 0, b, 0)),
    )
    out = pl.pallas_call(
        attention_body,
        grid_spec=grid_spec,
        out_shape=jax.ShapeDtypeStruct((kv_heads, q_groups, tok_count, head_dim), jnp.float32),
        compiler_params=pltpu.CompilerParams(
            dimension_semantics=("arbitrary", "arbitrary", "arbitrary")
        ),
        interpret=interpret,
    )(group_row, bounds, query_heads, key_heads, value_heads, seg_col, seg_line, prefix_heads)
    return out.transpose(2, 0, 1, 3).reshape(tok_count, -1).astype(jnp.bfloat16)


def owner_body(local_groups, me_ref, group_ref, bound_ref, q_ref, segq_ref, prefix_ref, o_ref, lse_ref):
    row = pl.program_id(1)
    block = pl.program_id(2)
    seg = pl.program_id(3)
    seg_count = pl.num_programs(3)
    rows = q_ref.shape[2]
    head_dim = q_ref.shape[3]

    @pl.when(seg == 0)
    def _():
        o_ref[...] = jnp.zeros_like(o_ref)
        lse_ref[...] = jnp.zeros_like(lse_ref)

    group = group_ref[row * seg_count + seg]
    first = bound_ref[row * 2 * seg_count + seg]
    last = bound_ref[row * 2 * seg_count + seg_count + seg]
    active = (
        (group // local_groups == me_ref[0]) & (first < (block + 1) * rows) & (last > block * rows)
    )

    @pl.when(active)
    def _():
        prefix = prefix_ref[0, 0]
        prefix_keys = prefix[:, :head_dim]
        prefix_values = prefix[:, head_dim:]
        mine = segq_ref[...] == seg
        contract = (((1,), (1,)), ((), ()))
        for q_group in range(q_ref.shape[1]):
            scores = (
                lax.dot_general(
                    q_ref[0, q_group], prefix_keys, contract, preferred_element_type=jnp.float32
                )
                * head_dim ** (-0.5)
            )
            top = jnp.max(scores, axis=1, keepdims=True)
            numerators = jnp.exp(scores - top)
            total = jnp.sum(numerators, axis=1, keepdims=True)
            summed = jnp.dot(
                numerators.astype(jnp.bfloat16), prefix_values, preferred_element_type=jnp.float32
            )
            o_ref[0, q_group] = jnp.where(mine, summed / total, o_ref[0, q_group])
            lse_ref[0, q_group] = jnp.where(mine, top + jnp.log(total), lse_ref[0, q_group])


def prefix_partials(query_all, segments_all, groups_all, prefix_local, me):
    kv_heads, q_groups, all_tokens, head_dim = query_all.shape
    row_count, tok_count = segments_all.shape
    seg_count = groups_all.shape[1]
    prefix_len = prefix_local.shape[2]
    rows = min(128, tok_count)
    blocks = tok_count // rows
    local_groups = prefix_local.shape[0]
    labels = jnp.arange(seg_count, dtype=jnp.int32)
    first = jnp.sum((segments_all[:, None, :] < labels[None, :, None]).astype(jnp.int32), axis=2)
    last = jnp.sum((segments_all[:, None, :] <= labels[None, :, None]).astype(jnp.int32), axis=2)
    bounds = jnp.concatenate([first, last], axis=1).reshape(-1)
    seg_col = segments_all.reshape(all_tokens, 1)
    grid_spec = pltpu.PrefetchScalarGridSpec(
        num_scalar_prefetch=3,
        grid=(kv_heads, row_count, blocks, seg_count),
        in_specs=[
            pl.BlockSpec(
                (1, q_groups, rows, head_dim),
                lambda h, r, b, s, me, gr, bd: (h, 0, r * blocks + b, 0),
            ),
            pl.BlockSpec((rows, 1), lambda h, r, b, s, me, gr, bd: (r * blocks + b, 0)),
            pl.BlockSpec(
                (1, 1, prefix_len, 2 * head_dim),
                lambda h, r, b, s, me, gr, bd: (gr[r * seg_count + s] % local_groups, h, 0, 0),
            ),
        ],
        out_specs=[
            pl.BlockSpec(
                (1, q_groups, rows, head_dim),
                lambda h, r, b, s, me, gr, bd: (h, 0, r * blocks + b, 0),
            ),
            pl.BlockSpec(
                (1, q_groups, rows, 1), lambda h, r, b, s, me, gr, bd: (h, 0, r * blocks + b, 0)
            ),
        ],
    )
    return pl.pallas_call(
        functools.partial(owner_body, local_groups),
        grid_spec=grid_spec,
        out_shape=(
            jax.ShapeDtypeStruct((kv_heads, q_groups, all_tokens, head_dim), jnp.float32),
            jax.ShapeDtypeStruct((kv_heads, q_groups, all_tokens, 1), jnp.float32),
        ),
        compiler_params=pltpu.CompilerParams(
            dimension_semantics=("arbitrary", "arbitrary", "arbitrary", "arbitrary")
        ),
    )(me.reshape(1), groups_all.reshape(-1), bounds, query_all, seg_col, prefix_local)


def shards(
    hidden_in,
    segments,
    prefix_group,
    prefix_cache,
    page_table,
    norm_gain,
    w_query,
    w_keyval,
    w_out,
    moe_gain,
    routes,
    gates,
    w_gate_up,
    w_down,
):
    req_count = lax.axis_size("req")
    whole = gather_in_order(hidden_in, "hid", 1)
    tok_count = whole.shape[0]
    model_width = whole.shape[1]
    segment_row = segments[0]
    prefix_len = prefix_cache.shape[1]
    kv_heads = prefix_cache.shape[2]
    head_dim = prefix_cache.shape[3] // 2
    score_scale = head_dim ** (-0.5)
    normed = rms_scale(whole, norm_gain)
    position = positions_of(segment_row, prefix_len)
    projected = jnp.dot(normed, w_query, preferred_element_type=jnp.float32).reshape(
        tok_count, -1, head_dim
    )
    queries = rotate(projected, position).astype(jnp.bfloat16)
    q_groups = queries.shape[1] // kv_heads
    grouped_query = queries.reshape(tok_count, kv_heads, q_groups, head_dim)
    key_value = jnp.dot(normed, w_keyval, preferred_element_type=jnp.float32).reshape(
        tok_count, kv_heads, 2 * head_dim
    )
    key_rows = rotate(key_value[..., :head_dim], position).astype(jnp.bfloat16)
    value_rows = key_value[..., head_dim:].astype(jnp.bfloat16)
    pages = jnp.concatenate([key_rows, value_rows], axis=-1).reshape(
        -1, PAGE, kv_heads, 2 * head_dim
    )
    kv_pages = jnp.zeros_like(pages).at[page_table[0]].set(pages)
    query_heads = grouped_query.transpose(1, 2, 0, 3)
    query_all = lax.all_gather(query_heads, "req", axis=2, tiled=True)
    segments_all = lax.all_gather(segments, "req", axis=0, tiled=True)
    groups_all = lax.all_gather(prefix_group, "req", axis=0, tiled=True)
    query_all, w_gate_up, w_down = lax.optimization_barrier((query_all, w_gate_up, w_down))
    cached_out, cached_lse = prefix_partials(
        query_all, segments_all, groups_all, prefix_cache.transpose(0, 2, 1, 3),
        lax.axis_index("req"),
    )
    row_split = (kv_heads, q_groups, req_count, tok_count)
    cached_out = lax.all_to_all(
        cached_out.astype(jnp.bfloat16).reshape(row_split + (head_dim,)),
        "req", split_axis=2, concat_axis=2, tiled=True,
    )
    cached_lse = lax.all_to_all(
        cached_lse.reshape(row_split + (1,)), "req", split_axis=2, concat_axis=2, tiled=True
    )
    cached_out = jnp.sum(cached_out.astype(jnp.float32), axis=2)
    cached_lse = jnp.sum(cached_lse, axis=2)
    token_index = jnp.arange(tok_count, dtype=jnp.int32)
    visible = (segment_row[None, :] == segment_row[:, None]) & (
        token_index[None, :] <= token_index[:, None]
    )
    local_scores = (
        jnp.einsum("tkgd,skd->kgts", grouped_query, key_rows, preferred_element_type=jnp.float32)
        * score_scale
    )
    local_scores = jnp.where(visible[None, None], local_scores, -jnp.inf)
    local_max = jnp.max(local_scores, axis=-1, keepdims=True)
    local_num = jnp.exp(local_scores - local_max)
    local_total = jnp.sum(local_num, axis=-1, keepdims=True)
    local_out = jnp.einsum(
        "kgts,skd->kgtd", local_num.astype(jnp.bfloat16), value_rows,
        preferred_element_type=jnp.float32,
    ) / local_total
    local_lse = local_max + jnp.log(local_total)
    joint_lse = jnp.logaddexp(local_lse, cached_lse)
    merged = jnp.exp(local_lse - joint_lse) * local_out + jnp.exp(cached_lse - joint_lse) * cached_out
    attention = merged.transpose(2, 0, 1, 3).reshape(tok_count, -1).astype(jnp.bfloat16)
    share_width = hidden_in.shape[1]
    whole_attention = jnp.concatenate(shifted_copies(attention, "hid"), axis=1)
    whole_w_out = jnp.concatenate(shifted_copies(w_out, "hid"), axis=0)
    projected_out = jnp.dot(whole_attention, whole_w_out, preferred_element_type=jnp.float32)
    middle = (whole.astype(jnp.float32) + projected_out).astype(jnp.bfloat16)
    middle_share = lax.dynamic_slice_in_dim(
        middle, lax.axis_index("hid") * share_width, share_width, 1
    )
    normed_moe = rms_scale(middle, moe_gain)
    all_gate_up = lax.all_gather(w_gate_up, "req", axis=0, tiled=True)
    all_down = lax.all_gather(w_down, "req", axis=0, tiled=True)
    experts = all_down.shape[0]
    expert_ids = jnp.arange(experts, dtype=jnp.int32)
    combine = jnp.sum(
        jnp.where(routes[:, :, None] == expert_ids[None, None, :], gates[:, :, None], 0.0), axis=1
    )
    gate_proj = jnp.einsum(
        "td,edf->tef", normed_moe, all_gate_up[:, 0], preferred_element_type=jnp.float32
    )
    up_proj = jnp.einsum(
        "td,edf->tef", normed_moe, all_gate_up[:, 1], preferred_element_type=jnp.float32
    )
    hidden = (jax.nn.silu(gate_proj) * up_proj * combine[:, :, None]).astype(jnp.bfloat16)
    partial_out = jnp.einsum(
        "tef,efd->td", hidden, all_down, preferred_element_type=jnp.float32
    )
    hid_count = lax.axis_size("hid")
    hid_index = lax.axis_index("hid")
    expert_sum = lax.dynamic_slice_in_dim(partial_out, hid_index * share_width, share_width, 1)
    for shift in range(1, hid_count):
        block = (hid_index + shift) % hid_count
        outgoing = lax.dynamic_slice_in_dim(partial_out, block * share_width, share_width, 1)
        pairs = [(index, (index + shift) % hid_count) for index in range(hid_count)]
        incoming = lax.ppermute(outgoing.astype(jnp.bfloat16), "hid", pairs)
        expert_sum = expert_sum + incoming.astype(jnp.float32)
    hidden_out = (middle_share.astype(jnp.float32) + expert_sum).astype(jnp.bfloat16)
    return (hidden_out, kv_pages)


def solution(mesh):
    in_specs = (
        P("req", "hid"),
        P("req", None),
        P("req", None),
        P("req", None, "hid", None),
        P("req", None),
        P(),
        P(None, "hid"),
        P(None, "hid"),
        P("hid", None),
        P(),
        P("req", None),
        P("req", None),
        P("req", None, None, "hid"),
        P("req", "hid", None),
    )
    out_specs = (P("req", "hid"), P("req", None, "hid", None))
    return jax.shard_map(shards, mesh=mesh, in_specs=in_specs, out_specs=out_specs, check_vma=False)
```

```python
import functools

import jax
import jax.numpy as jnp
from jax import lax
from jax.sharding import PartitionSpec as P
from jax.experimental import pallas as pl
from jax.experimental.pallas import tpu as pltpu

PAGE = 128


EPSILON = 1e-06
THETA = 10000.0


def rms_scale(row_data, gain_row):
    floats = row_data.astype(jnp.float32)
    mean_square = jnp.mean(floats * floats, axis=-1, keepdims=True)
    return (floats * lax.rsqrt(mean_square + EPSILON) * gain_row).astype(jnp.bfloat16)


def rotate(features, positions):
    half_dim = features.shape[-1] // 2
    frequency = THETA ** (-2.0 * jnp.arange(half_dim, dtype=jnp.float32) / features.shape[-1])
    angles = positions.astype(jnp.float32)[:, None] * frequency[None, :]
    cosine = jnp.cos(angles)[:, None, :]
    sine_part = jnp.sin(angles)[:, None, :]
    front_half = features[..., :half_dim]
    second = features[..., half_dim:]
    return jnp.concatenate(
        [front_half * cosine - second * sine_part, second * cosine + front_half * sine_part],
        axis=-1,
    )


def positions_of(segment_row, offset):
    earlier = jnp.sum((segment_row[None, :] < segment_row[:, None]).astype(jnp.int32), axis=1)
    token_index = jnp.arange(segment_row.shape[0], dtype=jnp.int32)
    return token_index - earlier + offset


def slots_of(route_rows, experts):
    flat_routes = route_rows.reshape(-1)
    onehot = (flat_routes[:, None] == jnp.arange(experts, dtype=jnp.int32)[None, :]).astype(
        jnp.int32
    )
    before = jnp.cumsum(onehot, axis=0) - onehot
    return (flat_routes, jnp.sum(before * onehot, axis=1))


def expert_rows(received, gate_up, down_proj):
    local_experts = down_proj.shape[0]
    slot_count = received.shape[1]
    model_width = received.shape[2]
    grouped = received.reshape(-1, local_experts, slot_count, model_width)
    gate_proj = jnp.einsum(
        "recd,edf->recf", grouped, gate_up[:, 0], preferred_element_type=jnp.float32
    )
    up_proj = jnp.einsum(
        "recd,edf->recf", grouped, gate_up[:, 1], preferred_element_type=jnp.float32
    )
    hidden = (jax.nn.silu(gate_proj) * up_proj).astype(jnp.bfloat16)
    produced = jnp.einsum("recf,efd->recd", hidden, down_proj, preferred_element_type=jnp.float32)
    return produced.reshape(-1, slot_count, model_width)


def shifted_copies(block, axis_name):
    count = lax.axis_size(axis_name)
    copies = [block]
    for shift in range(1, count):
        pairs = [(index, (index + shift) % count) for index in range(count)]
        copies.append(lax.ppermute(block, axis_name, pairs))
    return copies


def gather_in_order(block, axis_name, axis):
    count = lax.axis_size(axis_name)
    copies = jnp.stack(shifted_copies(block, axis_name))
    order = (lax.axis_index(axis_name) - jnp.arange(count, dtype=jnp.int32)) % count
    picked = jnp.take(copies, order, axis=0)
    return jnp.concatenate([picked[index] for index in range(count)], axis=axis)


def attention_body(group_ref, bound_ref, q_ref, k_ref, v_ref, segq_ref, segk_ref, prefix_ref, out_ref):
    block = pl.program_id(1)
    seg = pl.program_id(2)
    seg_count = pl.num_programs(2)
    rows = q_ref.shape[2]
    tokens = k_ref.shape[1]
    head_dim = q_ref.shape[3]

    @pl.when(seg == 0)
    def _():
        out_ref[...] = jnp.zeros_like(out_ref)

    first = bound_ref[seg]
    last = bound_ref[seg + seg_count]
    active = (first < (block + 1) * rows) & (last > block * rows)

    @pl.when(active)
    def _():
        seg_q = segq_ref[...]
        seg_k = segk_ref[...]
        t_idx = block * rows + lax.broadcasted_iota(jnp.int32, (rows, tokens), 0)
        u_idx = lax.broadcasted_iota(jnp.int32, (rows, tokens), 1)
        visible = (seg_q == seg_k) & (u_idx <= t_idx)
        keys = k_ref[0]
        values = v_ref[0]
        prefix = prefix_ref[0, 0]
        prefix_keys = prefix[:, :head_dim]
        prefix_values = prefix[:, head_dim:]
        scale = head_dim ** (-0.5)
        mine = seg_q == seg
        contract = (((1,), (1,)), ((), ()))
        for group in range(q_ref.shape[1]):
            query = q_ref[0, group]
            local = lax.dot_general(query, keys, contract, preferred_element_type=jnp.float32) * scale
            local = jnp.where(visible, local, -jnp.inf)
            cached = (
                lax.dot_general(query, prefix_keys, contract, preferred_element_type=jnp.float32)
                * scale
            )
            top = jnp.maximum(
                jnp.max(local, axis=1, keepdims=True), jnp.max(cached, axis=1, keepdims=True)
            )
            local_num = jnp.exp(local - top)
            cached_num = jnp.exp(cached - top)
            total = jnp.sum(local_num, axis=1, keepdims=True) + jnp.sum(
                cached_num, axis=1, keepdims=True
            )
            summed = jnp.dot(
                local_num.astype(jnp.bfloat16), values, preferred_element_type=jnp.float32
            ) + jnp.dot(
                cached_num.astype(jnp.bfloat16), prefix_values, preferred_element_type=jnp.float32
            )
            out_ref[0, group] = jnp.where(mine, summed / total, out_ref[0, group])


def attend(grouped_query, key_rows, value_rows, segment_row, group_row, prefix_heads, interpret=False):
    tok_count, kv_heads, q_groups, head_dim = grouped_query.shape
    seg_count = group_row.shape[0]
    prefix_len = prefix_heads.shape[2]
    rows = min(128, tok_count)
    labels = jnp.arange(seg_count, dtype=jnp.int32)
    first = jnp.sum((segment_row[None, :] < labels[:, None]).astype(jnp.int32), axis=1)
    last = jnp.sum((segment_row[None, :] <= labels[:, None]).astype(jnp.int32), axis=1)
    bounds = jnp.concatenate([first, last])
    query_heads = grouped_query.transpose(1, 2, 0, 3)
    key_heads = key_rows.transpose(1, 0, 2)
    value_heads = value_rows.transpose(1, 0, 2)
    seg_col = segment_row.reshape(tok_count, 1)
    seg_line = segment_row.reshape(1, tok_count)
    grid_spec = pltpu.PrefetchScalarGridSpec(
        num_scalar_prefetch=2,
        grid=(kv_heads, tok_count // rows, seg_count),
        in_specs=[
            pl.BlockSpec((1, q_groups, rows, head_dim), lambda h, b, s, gr, bd: (h, 0, b, 0)),
            pl.BlockSpec((1, tok_count, head_dim), lambda h, b, s, gr, bd: (h, 0, 0)),
            pl.BlockSpec((1, tok_count, head_dim), lambda h, b, s, gr, bd: (h, 0, 0)),
            pl.BlockSpec((rows, 1), lambda h, b, s, gr, bd: (b, 0)),
            pl.BlockSpec((1, tok_count), lambda h, b, s, gr, bd: (0, 0)),
            pl.BlockSpec(
                (1, 1, prefix_len, 2 * head_dim), lambda h, b, s, gr, bd: (gr[s], h, 0, 0)
            ),
        ],
        out_specs=pl.BlockSpec((1, q_groups, rows, head_dim), lambda h, b, s, gr, bd: (h, 0, b, 0)),
    )
    out = pl.pallas_call(
        attention_body,
        grid_spec=grid_spec,
        out_shape=jax.ShapeDtypeStruct((kv_heads, q_groups, tok_count, head_dim), jnp.float32),
        compiler_params=pltpu.CompilerParams(
            dimension_semantics=("arbitrary", "arbitrary", "arbitrary")
        ),
        interpret=interpret,
    )(group_row, bounds, query_heads, key_heads, value_heads, seg_col, seg_line, prefix_heads)
    return out.transpose(2, 0, 1, 3).reshape(tok_count, -1).astype(jnp.bfloat16)


def owner_body(local_groups, seg_count, me_ref, group_ref, bound_ref, q_ref, segq_ref, prefix_ref, o_ref, lse_ref):
    head = pl.program_id(0)
    row = pl.program_id(1)
    block = pl.program_id(2)
    rows = q_ref.shape[2]
    head_dim = q_ref.shape[3]
    o_ref[...] = jnp.zeros_like(o_ref)
    lse_ref[...] = jnp.zeros_like(lse_ref)
    contract = (((1,), (1,)), ((), ()))
    for seg in range(seg_count):
        group = group_ref[row * seg_count + seg]
        first = bound_ref[row * 2 * seg_count + seg]
        last = bound_ref[row * 2 * seg_count + seg_count + seg]
        active = (
            (group // local_groups == me_ref[0])
            & (first < (block + 1) * rows)
            & (last > block * rows)
        )

        @pl.when(active)
        def _():
            prefix = prefix_ref[group % local_groups, head]
            prefix_keys = prefix[:, :head_dim]
            prefix_values = prefix[:, head_dim:]
            mine = segq_ref[...] == seg
            for q_group in range(q_ref.shape[1]):
                scores = (
                    lax.dot_general(
                        q_ref[0, q_group], prefix_keys, contract,
                        preferred_element_type=jnp.float32,
                    )
                    * head_dim ** (-0.5)
                )
                top = jnp.max(scores, axis=1, keepdims=True)
                numerators = jnp.exp(scores - top)
                total = jnp.sum(numerators, axis=1, keepdims=True)
                summed = jnp.dot(
                    numerators.astype(jnp.bfloat16), prefix_values,
                    preferred_element_type=jnp.float32,
                )
                o_ref[0, q_group] = jnp.where(mine, summed / total, o_ref[0, q_group])
                lse_ref[0, q_group] = jnp.where(mine, top + jnp.log(total), lse_ref[0, q_group])


def prefix_partials(query_all, segments_all, groups_all, prefix_local, me):
    kv_heads, q_groups, all_tokens, head_dim = query_all.shape
    row_count, tok_count = segments_all.shape
    seg_count = groups_all.shape[1]
    rows = min(128, tok_count)
    blocks = tok_count // rows
    local_groups = prefix_local.shape[0]
    labels = jnp.arange(seg_count, dtype=jnp.int32)
    first = jnp.sum((segments_all[:, None, :] < labels[None, :, None]).astype(jnp.int32), axis=2)
    last = jnp.sum((segments_all[:, None, :] <= labels[None, :, None]).astype(jnp.int32), axis=2)
    bounds = jnp.concatenate([first, last], axis=1).reshape(-1)
    seg_col = segments_all.reshape(all_tokens, 1)
    grid_spec = pltpu.PrefetchScalarGridSpec(
        num_scalar_prefetch=3,
        grid=(kv_heads, row_count, blocks),
        in_specs=[
            pl.BlockSpec(
                (1, q_groups, rows, head_dim), lambda h, r, b, me, gr, bd: (h, 0, r * blocks + b, 0)
            ),
            pl.BlockSpec((rows, 1), lambda h, r, b, me, gr, bd: (r * blocks + b, 0)),
            pl.BlockSpec(prefix_local.shape, lambda h, r, b, me, gr, bd: (0, 0, 0, 0)),
        ],
        out_specs=[
            pl.BlockSpec(
                (1, q_groups, rows, head_dim), lambda h, r, b, me, gr, bd: (h, 0, r * blocks + b, 0)
            ),
            pl.BlockSpec(
                (1, q_groups, rows, 1), lambda h, r, b, me, gr, bd: (h, 0, r * blocks + b, 0)
            ),
        ],
    )
    return pl.pallas_call(
        functools.partial(owner_body, local_groups, seg_count),
        grid_spec=grid_spec,
        out_shape=(
            jax.ShapeDtypeStruct((kv_heads, q_groups, all_tokens, head_dim), jnp.float32),
            jax.ShapeDtypeStruct((kv_heads, q_groups, all_tokens, 1), jnp.float32),
        ),
        compiler_params=pltpu.CompilerParams(
            dimension_semantics=("arbitrary", "arbitrary", "arbitrary")
        ),
    )(me.reshape(1), groups_all.reshape(-1), bounds, query_all, seg_col, prefix_local)


def shards(
    hidden_in,
    segments,
    prefix_group,
    prefix_cache,
    page_table,
    norm_gain,
    w_query,
    w_keyval,
    w_out,
    moe_gain,
    routes,
    gates,
    w_gate_up,
    w_down,
):
    req_count = lax.axis_size("req")
    whole = gather_in_order(hidden_in, "hid", 1)
    tok_count = whole.shape[0]
    model_width = whole.shape[1]
    segment_row = segments[0]
    prefix_len = prefix_cache.shape[1]
    kv_heads = prefix_cache.shape[2]
    head_dim = prefix_cache.shape[3] // 2
    score_scale = head_dim ** (-0.5)
    normed = rms_scale(whole, norm_gain)
    position = positions_of(segment_row, prefix_len)
    projected = jnp.dot(normed, w_query, preferred_element_type=jnp.float32).reshape(
        tok_count, -1, head_dim
    )
    queries = rotate(projected, position).astype(jnp.bfloat16)
    q_groups = queries.shape[1] // kv_heads
    grouped_query = queries.reshape(tok_count, kv_heads, q_groups, head_dim)
    key_value = jnp.dot(normed, w_keyval, preferred_element_type=jnp.float32).reshape(
        tok_count, kv_heads, 2 * head_dim
    )
    key_rows = rotate(key_value[..., :head_dim], position).astype(jnp.bfloat16)
    value_rows = key_value[..., head_dim:].astype(jnp.bfloat16)
    pages = jnp.concatenate([key_rows, value_rows], axis=-1).reshape(
        -1, PAGE, kv_heads, 2 * head_dim
    )
    kv_pages = jnp.zeros_like(pages).at[page_table[0]].set(pages)
    query_all = lax.all_gather(grouped_query, "req", axis=0, tiled=True).transpose(1, 2, 0, 3)
    row_tables = lax.all_gather(
        jnp.concatenate([segments, prefix_group], axis=1), "req", axis=0, tiled=True
    )
    segments_all = row_tables[:, : segments.shape[1]]
    groups_all = row_tables[:, segments.shape[1] :]
    query_all, w_gate_up, w_down = lax.optimization_barrier((query_all, w_gate_up, w_down))
    cached_out, cached_lse = prefix_partials(
        query_all, segments_all, groups_all, prefix_cache.transpose(0, 2, 1, 3),
        lax.axis_index("req"),
    )
    row_split = (kv_heads, q_groups, req_count, tok_count)
    cached_out = lax.all_to_all(
        cached_out.astype(jnp.bfloat16).reshape(row_split + (head_dim,)),
        "req", split_axis=2, concat_axis=2, tiled=True,
    )
    cached_lse = lax.all_to_all(
        cached_lse.reshape(row_split + (1,)), "req", split_axis=2, concat_axis=2, tiled=True
    )
    cached_out = jnp.sum(cached_out.astype(jnp.float32), axis=2)
    cached_lse = jnp.sum(cached_lse, axis=2)
    token_index = jnp.arange(tok_count, dtype=jnp.int32)
    visible = (segment_row[None, :] == segment_row[:, None]) & (
        token_index[None, :] <= token_index[:, None]
    )
    local_scores = (
        jnp.einsum("tkgd,skd->kgts", grouped_query, key_rows, preferred_element_type=jnp.float32)
        * score_scale
    )
    local_scores = jnp.where(visible[None, None], local_scores, -jnp.inf)
    local_max = jnp.max(local_scores, axis=-1, keepdims=True)
    local_num = jnp.exp(local_scores - local_max)
    local_total = jnp.sum(local_num, axis=-1, keepdims=True)
    local_out = jnp.einsum(
        "kgts,skd->kgtd", local_num.astype(jnp.bfloat16), value_rows,
        preferred_element_type=jnp.float32,
    ) / local_total
    local_lse = local_max + jnp.log(local_total)
    joint_lse = jnp.logaddexp(local_lse, cached_lse)
    merged = jnp.exp(local_lse - joint_lse) * local_out + jnp.exp(cached_lse - joint_lse) * cached_out
    attention = merged.transpose(2, 0, 1, 3).reshape(tok_count, -1).astype(jnp.bfloat16)
    share_width = hidden_in.shape[1]
    whole_attention = jnp.concatenate(shifted_copies(attention, "hid"), axis=1)
    whole_w_out = jnp.concatenate(shifted_copies(w_out, "hid"), axis=0)
    projected_out = jnp.dot(whole_attention, whole_w_out, preferred_element_type=jnp.float32)
    middle = (whole.astype(jnp.float32) + projected_out).astype(jnp.bfloat16)
    middle_share = lax.dynamic_slice_in_dim(
        middle, lax.axis_index("hid") * share_width, share_width, 1
    )
    normed_moe = rms_scale(middle, moe_gain)
    all_gate_up = lax.all_gather(w_gate_up, "req", axis=0, tiled=True)
    all_down = lax.all_gather(w_down, "req", axis=0, tiled=True)
    experts = all_down.shape[0]
    expert_ids = jnp.arange(experts, dtype=jnp.int32)
    combine = jnp.sum(
        jnp.where(routes[:, :, None] == expert_ids[None, None, :], gates[:, :, None], 0.0), axis=1
    )
    gate_proj = jnp.einsum(
        "td,edf->tef", normed_moe, all_gate_up[:, 0], preferred_element_type=jnp.float32
    )
    up_proj = jnp.einsum(
        "td,edf->tef", normed_moe, all_gate_up[:, 1], preferred_element_type=jnp.float32
    )
    hidden = (jax.nn.silu(gate_proj) * up_proj * combine[:, :, None]).astype(jnp.bfloat16)
    partial_out = jnp.einsum(
        "tef,efd->td", hidden, all_down, preferred_element_type=jnp.float32
    )
    hid_count = lax.axis_size("hid")
    hid_index = lax.axis_index("hid")
    expert_sum = lax.dynamic_slice_in_dim(partial_out, hid_index * share_width, share_width, 1)
    for shift in range(1, hid_count):
        block = (hid_index + shift) % hid_count
        outgoing = lax.dynamic_slice_in_dim(partial_out, block * share_width, share_width, 1)
        pairs = [(index, (index + shift) % hid_count) for index in range(hid_count)]
        incoming = lax.ppermute(outgoing.astype(jnp.bfloat16), "hid", pairs)
        expert_sum = expert_sum + incoming.astype(jnp.float32)
    hidden_out = (middle_share.astype(jnp.float32) + expert_sum).astype(jnp.bfloat16)
    return (hidden_out, kv_pages)


def solution(mesh):
    in_specs = (
        P("req", "hid"),
        P("req", None),
        P("req", None),
        P("req", None, "hid", None),
        P("req", None),
        P(),
        P(None, "hid"),
        P(None, "hid"),
        P("hid", None),
        P(),
        P("req", None),
        P("req", None),
        P("req", None, None, "hid"),
        P("req", "hid", None),
    )
    out_specs = (P("req", "hid"), P("req", None, "hid", None))
    return jax.shard_map(shards, mesh=mesh, in_specs=in_specs, out_specs=out_specs, check_vma=False)
```

```python
import functools

import jax
import jax.numpy as jnp
from jax import lax
from jax.sharding import PartitionSpec as P
from jax.experimental import pallas as pl
from jax.experimental.pallas import tpu as pltpu

PAGE = 128


EPSILON = 1e-06
THETA = 10000.0


def rms_scale(row_data, gain_row):
    floats = row_data.astype(jnp.float32)
    mean_square = jnp.mean(floats * floats, axis=-1, keepdims=True)
    return (floats * lax.rsqrt(mean_square + EPSILON) * gain_row).astype(jnp.bfloat16)


def rotate(features, positions):
    half_dim = features.shape[-1] // 2
    frequency = THETA ** (-2.0 * jnp.arange(half_dim, dtype=jnp.float32) / features.shape[-1])
    angles = positions.astype(jnp.float32)[:, None] * frequency[None, :]
    cosine = jnp.cos(angles)[:, None, :]
    sine_part = jnp.sin(angles)[:, None, :]
    front_half = features[..., :half_dim]
    second = features[..., half_dim:]
    return jnp.concatenate(
        [front_half * cosine - second * sine_part, second * cosine + front_half * sine_part],
        axis=-1,
    )


def positions_of(segment_row, offset):
    earlier = jnp.sum((segment_row[None, :] < segment_row[:, None]).astype(jnp.int32), axis=1)
    token_index = jnp.arange(segment_row.shape[0], dtype=jnp.int32)
    return token_index - earlier + offset


def slots_of(route_rows, experts):
    flat_routes = route_rows.reshape(-1)
    onehot = (flat_routes[:, None] == jnp.arange(experts, dtype=jnp.int32)[None, :]).astype(
        jnp.int32
    )
    before = jnp.cumsum(onehot, axis=0) - onehot
    return (flat_routes, jnp.sum(before * onehot, axis=1))


def expert_rows(received, gate_up, down_proj):
    local_experts = down_proj.shape[0]
    slot_count = received.shape[1]
    model_width = received.shape[2]
    grouped = received.reshape(-1, local_experts, slot_count, model_width)
    gate_proj = jnp.einsum(
        "recd,edf->recf", grouped, gate_up[:, 0], preferred_element_type=jnp.float32
    )
    up_proj = jnp.einsum(
        "recd,edf->recf", grouped, gate_up[:, 1], preferred_element_type=jnp.float32
    )
    hidden = (jax.nn.silu(gate_proj) * up_proj).astype(jnp.bfloat16)
    produced = jnp.einsum("recf,efd->recd", hidden, down_proj, preferred_element_type=jnp.float32)
    return produced.reshape(-1, slot_count, model_width)


def shifted_copies(block, axis_name):
    count = lax.axis_size(axis_name)
    copies = [block]
    for shift in range(1, count):
        pairs = [(index, (index + shift) % count) for index in range(count)]
        copies.append(lax.ppermute(block, axis_name, pairs))
    return copies


def gather_in_order(block, axis_name, axis):
    count = lax.axis_size(axis_name)
    copies = jnp.stack(shifted_copies(block, axis_name))
    order = (lax.axis_index(axis_name) - jnp.arange(count, dtype=jnp.int32)) % count
    picked = jnp.take(copies, order, axis=0)
    return jnp.concatenate([picked[index] for index in range(count)], axis=axis)


def attention_body(group_ref, bound_ref, q_ref, k_ref, v_ref, segq_ref, segk_ref, prefix_ref, out_ref):
    block = pl.program_id(1)
    seg = pl.program_id(2)
    seg_count = pl.num_programs(2)
    rows = q_ref.shape[2]
    tokens = k_ref.shape[1]
    head_dim = q_ref.shape[3]

    @pl.when(seg == 0)
    def _():
        out_ref[...] = jnp.zeros_like(out_ref)

    first = bound_ref[seg]
    last = bound_ref[seg + seg_count]
    active = (first < (block + 1) * rows) & (last > block * rows)

    @pl.when(active)
    def _():
        seg_q = segq_ref[...]
        seg_k = segk_ref[...]
        t_idx = block * rows + lax.broadcasted_iota(jnp.int32, (rows, tokens), 0)
        u_idx = lax.broadcasted_iota(jnp.int32, (rows, tokens), 1)
        visible = (seg_q == seg_k) & (u_idx <= t_idx)
        keys = k_ref[0]
        values = v_ref[0]
        prefix = prefix_ref[0, 0]
        prefix_keys = prefix[:, :head_dim]
        prefix_values = prefix[:, head_dim:]
        scale = head_dim ** (-0.5)
        mine = seg_q == seg
        contract = (((1,), (1,)), ((), ()))
        for group in range(q_ref.shape[1]):
            query = q_ref[0, group]
            local = lax.dot_general(query, keys, contract, preferred_element_type=jnp.float32) * scale
            local = jnp.where(visible, local, -jnp.inf)
            cached = (
                lax.dot_general(query, prefix_keys, contract, preferred_element_type=jnp.float32)
                * scale
            )
            top = jnp.maximum(
                jnp.max(local, axis=1, keepdims=True), jnp.max(cached, axis=1, keepdims=True)
            )
            local_num = jnp.exp(local - top)
            cached_num = jnp.exp(cached - top)
            total = jnp.sum(local_num, axis=1, keepdims=True) + jnp.sum(
                cached_num, axis=1, keepdims=True
            )
            summed = jnp.dot(
                local_num.astype(jnp.bfloat16), values, preferred_element_type=jnp.float32
            ) + jnp.dot(
                cached_num.astype(jnp.bfloat16), prefix_values, preferred_element_type=jnp.float32
            )
            out_ref[0, group] = jnp.where(mine, summed / total, out_ref[0, group])


def attend(grouped_query, key_rows, value_rows, segment_row, group_row, prefix_heads, interpret=False):
    tok_count, kv_heads, q_groups, head_dim = grouped_query.shape
    seg_count = group_row.shape[0]
    prefix_len = prefix_heads.shape[2]
    rows = min(128, tok_count)
    labels = jnp.arange(seg_count, dtype=jnp.int32)
    first = jnp.sum((segment_row[None, :] < labels[:, None]).astype(jnp.int32), axis=1)
    last = jnp.sum((segment_row[None, :] <= labels[:, None]).astype(jnp.int32), axis=1)
    bounds = jnp.concatenate([first, last])
    query_heads = grouped_query.transpose(1, 2, 0, 3)
    key_heads = key_rows.transpose(1, 0, 2)
    value_heads = value_rows.transpose(1, 0, 2)
    seg_col = segment_row.reshape(tok_count, 1)
    seg_line = segment_row.reshape(1, tok_count)
    grid_spec = pltpu.PrefetchScalarGridSpec(
        num_scalar_prefetch=2,
        grid=(kv_heads, tok_count // rows, seg_count),
        in_specs=[
            pl.BlockSpec((1, q_groups, rows, head_dim), lambda h, b, s, gr, bd: (h, 0, b, 0)),
            pl.BlockSpec((1, tok_count, head_dim), lambda h, b, s, gr, bd: (h, 0, 0)),
            pl.BlockSpec((1, tok_count, head_dim), lambda h, b, s, gr, bd: (h, 0, 0)),
            pl.BlockSpec((rows, 1), lambda h, b, s, gr, bd: (b, 0)),
            pl.BlockSpec((1, tok_count), lambda h, b, s, gr, bd: (0, 0)),
            pl.BlockSpec(
                (1, 1, prefix_len, 2 * head_dim), lambda h, b, s, gr, bd: (gr[s], h, 0, 0)
            ),
        ],
        out_specs=pl.BlockSpec((1, q_groups, rows, head_dim), lambda h, b, s, gr, bd: (h, 0, b, 0)),
    )
    out = pl.pallas_call(
        attention_body,
        grid_spec=grid_spec,
        out_shape=jax.ShapeDtypeStruct((kv_heads, q_groups, tok_count, head_dim), jnp.float32),
        compiler_params=pltpu.CompilerParams(
            dimension_semantics=("arbitrary", "arbitrary", "arbitrary")
        ),
        interpret=interpret,
    )(group_row, bounds, query_heads, key_heads, value_heads, seg_col, seg_line, prefix_heads)
    return out.transpose(2, 0, 1, 3).reshape(tok_count, -1).astype(jnp.bfloat16)


def owner_body(local_groups, seg_count, me_ref, group_ref, bound_ref, q_ref, segq_ref, prefix_ref, o_ref, lse_ref):
    head = pl.program_id(0)
    row = pl.program_id(1)
    block = pl.program_id(2)
    rows = q_ref.shape[2]
    head_dim = q_ref.shape[3]
    o_ref[...] = jnp.zeros_like(o_ref)
    lse_ref[...] = jnp.zeros_like(lse_ref)
    contract = (((1,), (1,)), ((), ()))
    for seg in range(seg_count):
        group = group_ref[row * seg_count + seg]
        first = bound_ref[row * 2 * seg_count + seg]
        last = bound_ref[row * 2 * seg_count + seg_count + seg]
        active = (
            (group // local_groups == me_ref[0])
            & (first < (block + 1) * rows)
            & (last > block * rows)
        )

        @pl.when(active)
        def _():
            prefix = prefix_ref[group % local_groups, head]
            prefix_keys = prefix[:, :head_dim]
            prefix_values = prefix[:, head_dim:]
            mine = segq_ref[...] == seg
            for q_group in range(q_ref.shape[1]):
                scores = (
                    lax.dot_general(
                        q_ref[0, q_group], prefix_keys, contract,
                        preferred_element_type=jnp.float32,
                    )
                    * head_dim ** (-0.5)
                )
                top = jnp.max(scores, axis=1, keepdims=True)
                numerators = jnp.exp(scores - top)
                total = jnp.sum(numerators, axis=1, keepdims=True)
                summed = jnp.dot(
                    numerators.astype(jnp.bfloat16), prefix_values,
                    preferred_element_type=jnp.float32,
                )
                o_ref[0, q_group] = jnp.where(mine, summed / total, o_ref[0, q_group])
                lse_ref[0, q_group] = jnp.where(mine, top + jnp.log(total), lse_ref[0, q_group])


def prefix_partials(query_all, segments_all, groups_all, prefix_local, me):
    kv_heads, q_groups, all_tokens, head_dim = query_all.shape
    row_count, tok_count = segments_all.shape
    seg_count = groups_all.shape[1]
    rows = min(128, tok_count)
    blocks = tok_count // rows
    local_groups = prefix_local.shape[0]
    labels = jnp.arange(seg_count, dtype=jnp.int32)
    first = jnp.sum((segments_all[:, None, :] < labels[None, :, None]).astype(jnp.int32), axis=2)
    last = jnp.sum((segments_all[:, None, :] <= labels[None, :, None]).astype(jnp.int32), axis=2)
    bounds = jnp.concatenate([first, last], axis=1).reshape(-1)
    seg_col = segments_all.reshape(all_tokens, 1)
    grid_spec = pltpu.PrefetchScalarGridSpec(
        num_scalar_prefetch=3,
        grid=(kv_heads, row_count, blocks),
        in_specs=[
            pl.BlockSpec(
                (1, q_groups, rows, head_dim), lambda h, r, b, me, gr, bd: (h, 0, r * blocks + b, 0)
            ),
            pl.BlockSpec((rows, 1), lambda h, r, b, me, gr, bd: (r * blocks + b, 0)),
            pl.BlockSpec(prefix_local.shape, lambda h, r, b, me, gr, bd: (0, 0, 0, 0)),
        ],
        out_specs=[
            pl.BlockSpec(
                (1, q_groups, rows, head_dim), lambda h, r, b, me, gr, bd: (h, 0, r * blocks + b, 0)
            ),
            pl.BlockSpec(
                (1, q_groups, rows, 1), lambda h, r, b, me, gr, bd: (h, 0, r * blocks + b, 0)
            ),
        ],
    )
    return pl.pallas_call(
        functools.partial(owner_body, local_groups, seg_count),
        grid_spec=grid_spec,
        out_shape=(
            jax.ShapeDtypeStruct((kv_heads, q_groups, all_tokens, head_dim), jnp.float32),
            jax.ShapeDtypeStruct((kv_heads, q_groups, all_tokens, 1), jnp.float32),
        ),
        compiler_params=pltpu.CompilerParams(
            dimension_semantics=("arbitrary", "arbitrary", "arbitrary")
        ),
    )(me.reshape(1), groups_all.reshape(-1), bounds, query_all, seg_col, prefix_local)


def shards(
    hidden_in,
    segments,
    prefix_group,
    prefix_cache,
    page_table,
    norm_gain,
    w_query,
    w_keyval,
    w_out,
    moe_gain,
    routes,
    gates,
    w_gate_up,
    w_down,
):
    req_count = lax.axis_size("req")
    whole = gather_in_order(hidden_in, "hid", 1)
    tok_count = whole.shape[0]
    model_width = whole.shape[1]
    segment_row = segments[0]
    prefix_len = prefix_cache.shape[1]
    kv_heads = prefix_cache.shape[2]
    head_dim = prefix_cache.shape[3] // 2
    score_scale = head_dim ** (-0.5)
    normed = rms_scale(whole, norm_gain)
    position = positions_of(segment_row, prefix_len)
    projected = jnp.dot(normed, w_query, preferred_element_type=jnp.float32).reshape(
        tok_count, -1, head_dim
    )
    queries = rotate(projected, position).astype(jnp.bfloat16)
    q_groups = queries.shape[1] // kv_heads
    grouped_query = queries.reshape(tok_count, kv_heads, q_groups, head_dim)
    key_value = jnp.dot(normed, w_keyval, preferred_element_type=jnp.float32).reshape(
        tok_count, kv_heads, 2 * head_dim
    )
    key_rows = rotate(key_value[..., :head_dim], position).astype(jnp.bfloat16)
    value_rows = key_value[..., head_dim:].astype(jnp.bfloat16)
    pages = jnp.concatenate([key_rows, value_rows], axis=-1).reshape(
        -1, PAGE, kv_heads, 2 * head_dim
    )
    kv_pages = jnp.zeros_like(pages).at[page_table[0]].set(pages)
    query_all = gather_in_order(grouped_query, "req", 0).transpose(1, 2, 0, 3)
    row_tables = lax.all_gather(
        jnp.concatenate([segments, prefix_group], axis=1), "req", axis=0, tiled=True
    )
    segments_all = row_tables[:, : segments.shape[1]]
    groups_all = row_tables[:, segments.shape[1] :]
    cached_out, cached_lse = prefix_partials(
        query_all, segments_all, groups_all, prefix_cache.transpose(0, 2, 1, 3),
        lax.axis_index("req"),
    )
    row_split = (kv_heads, q_groups, req_count, tok_count)
    cached_out = lax.all_to_all(
        cached_out.astype(jnp.bfloat16).reshape(row_split + (head_dim,)),
        "req", split_axis=2, concat_axis=2, tiled=True,
    )
    cached_lse = lax.all_to_all(
        cached_lse.reshape(row_split + (1,)), "req", split_axis=2, concat_axis=2, tiled=True
    )
    cached_out = jnp.sum(cached_out.astype(jnp.float32), axis=2)
    cached_lse = jnp.sum(cached_lse, axis=2)
    token_index = jnp.arange(tok_count, dtype=jnp.int32)
    visible = (segment_row[None, :] == segment_row[:, None]) & (
        token_index[None, :] <= token_index[:, None]
    )
    local_scores = (
        jnp.einsum("tkgd,skd->kgts", grouped_query, key_rows, preferred_element_type=jnp.float32)
        * score_scale
    )
    local_scores = jnp.where(visible[None, None], local_scores, -jnp.inf)
    local_max = jnp.max(local_scores, axis=-1, keepdims=True)
    local_num = jnp.exp(local_scores - local_max)
    local_total = jnp.sum(local_num, axis=-1, keepdims=True)
    local_out = jnp.einsum(
        "kgts,skd->kgtd", local_num.astype(jnp.bfloat16), value_rows,
        preferred_element_type=jnp.float32,
    ) / local_total
    local_lse = local_max + jnp.log(local_total)
    joint_lse = jnp.logaddexp(local_lse, cached_lse)
    merged = jnp.exp(local_lse - joint_lse) * local_out + jnp.exp(cached_lse - joint_lse) * cached_out
    attention = merged.transpose(2, 0, 1, 3).reshape(tok_count, -1).astype(jnp.bfloat16)
    share_width = hidden_in.shape[1]
    whole_attention = jnp.concatenate(shifted_copies(attention, "hid"), axis=1)
    whole_w_out = jnp.concatenate(shifted_copies(w_out, "hid"), axis=0)
    projected_out = jnp.dot(whole_attention, whole_w_out, preferred_element_type=jnp.float32)
    middle = (whole.astype(jnp.float32) + projected_out).astype(jnp.bfloat16)
    middle_share = lax.dynamic_slice_in_dim(
        middle, lax.axis_index("hid") * share_width, share_width, 1
    )
    normed_moe = rms_scale(middle, moe_gain)
    all_gate_up = lax.all_gather(w_gate_up, "req", axis=0, tiled=True)
    all_down = lax.all_gather(w_down, "req", axis=0, tiled=True)
    experts = all_down.shape[0]
    expert_ids = jnp.arange(experts, dtype=jnp.int32)
    combine = jnp.sum(
        jnp.where(routes[:, :, None] == expert_ids[None, None, :], gates[:, :, None], 0.0), axis=1
    )
    gate_proj = jnp.einsum(
        "td,edf->tef", normed_moe, all_gate_up[:, 0], preferred_element_type=jnp.float32
    )
    up_proj = jnp.einsum(
        "td,edf->tef", normed_moe, all_gate_up[:, 1], preferred_element_type=jnp.float32
    )
    hidden = (jax.nn.silu(gate_proj) * up_proj * combine[:, :, None]).astype(jnp.bfloat16)
    partial_out = jnp.einsum(
        "tef,efd->td", hidden, all_down, preferred_element_type=jnp.float32
    )
    hid_count = lax.axis_size("hid")
    hid_index = lax.axis_index("hid")
    expert_sum = lax.dynamic_slice_in_dim(partial_out, hid_index * share_width, share_width, 1)
    for shift in range(1, hid_count):
        block = (hid_index + shift) % hid_count
        outgoing = lax.dynamic_slice_in_dim(partial_out, block * share_width, share_width, 1)
        pairs = [(index, (index + shift) % hid_count) for index in range(hid_count)]
        incoming = lax.ppermute(outgoing.astype(jnp.bfloat16), "hid", pairs)
        expert_sum = expert_sum + incoming.astype(jnp.float32)
    hidden_out = (middle_share.astype(jnp.float32) + expert_sum).astype(jnp.bfloat16)
    return (hidden_out, kv_pages)


def solution(mesh):
    in_specs = (
        P("req", "hid"),
        P("req", None),
        P("req", None),
        P("req", None, "hid", None),
        P("req", None),
        P(),
        P(None, "hid"),
        P(None, "hid"),
        P("hid", None),
        P(),
        P("req", None),
        P("req", None),
        P("req", None, None, "hid"),
        P("req", "hid", None),
    )
    out_specs = (P("req", "hid"), P("req", None, "hid", None))
    return jax.shard_map(shards, mesh=mesh, in_specs=in_specs, out_specs=out_specs, check_vma=False)
```

```python
import jax
import jax.numpy as jnp
from jax import lax
from jax.sharding import PartitionSpec as P
from jax.experimental import pallas as pl
from jax.experimental.pallas import tpu as pltpu

PAGE = 128


EPSILON = 1e-06
THETA = 10000.0


def rms_scale(row_data, gain_row):
    floats = row_data.astype(jnp.float32)
    mean_square = jnp.mean(floats * floats, axis=-1, keepdims=True)
    return (floats * lax.rsqrt(mean_square + EPSILON) * gain_row).astype(jnp.bfloat16)


def rotate(features, positions):
    half_dim = features.shape[-1] // 2
    frequency = THETA ** (-2.0 * jnp.arange(half_dim, dtype=jnp.float32) / features.shape[-1])
    angles = positions.astype(jnp.float32)[:, None] * frequency[None, :]
    cosine = jnp.cos(angles)[:, None, :]
    sine_part = jnp.sin(angles)[:, None, :]
    front_half = features[..., :half_dim]
    second = features[..., half_dim:]
    return jnp.concatenate(
        [front_half * cosine - second * sine_part, second * cosine + front_half * sine_part],
        axis=-1,
    )


def positions_of(segment_row, offset):
    earlier = jnp.sum((segment_row[None, :] < segment_row[:, None]).astype(jnp.int32), axis=1)
    token_index = jnp.arange(segment_row.shape[0], dtype=jnp.int32)
    return token_index - earlier + offset


def slots_of(route_rows, experts):
    flat_routes = route_rows.reshape(-1)
    onehot = (flat_routes[:, None] == jnp.arange(experts, dtype=jnp.int32)[None, :]).astype(
        jnp.int32
    )
    before = jnp.cumsum(onehot, axis=0) - onehot
    return (flat_routes, jnp.sum(before * onehot, axis=1))


def expert_rows(received, gate_up, down_proj):
    local_experts = down_proj.shape[0]
    slot_count = received.shape[1]
    model_width = received.shape[2]
    grouped = received.reshape(-1, local_experts, slot_count, model_width)
    gate_proj = jnp.einsum(
        "recd,edf->recf", grouped, gate_up[:, 0], preferred_element_type=jnp.float32
    )
    up_proj = jnp.einsum(
        "recd,edf->recf", grouped, gate_up[:, 1], preferred_element_type=jnp.float32
    )
    hidden = (jax.nn.silu(gate_proj) * up_proj).astype(jnp.bfloat16)
    produced = jnp.einsum("recf,efd->recd", hidden, down_proj, preferred_element_type=jnp.float32)
    return produced.reshape(-1, slot_count, model_width)


def shifted_copies(block, axis_name):
    count = lax.axis_size(axis_name)
    copies = [block]
    for shift in range(1, count):
        pairs = [(index, (index + shift) % count) for index in range(count)]
        copies.append(lax.ppermute(block, axis_name, pairs))
    return copies


def gather_in_order(block, axis_name, axis):
    count = lax.axis_size(axis_name)
    copies = jnp.stack(shifted_copies(block, axis_name))
    order = (lax.axis_index(axis_name) - jnp.arange(count, dtype=jnp.int32)) % count
    picked = jnp.take(copies, order, axis=0)
    return jnp.concatenate([picked[index] for index in range(count)], axis=axis)


def chip_gather(block, axis_name):
    count = lax.axis_size(axis_name)
    me = lax.axis_index(axis_name)
    if count < 2 or count & (count - 1):
        copies = shifted_copies(block, axis_name)
        sources = [(me - shift) % count for shift in range(count)]
        return jnp.concatenate(copies, axis=0), sources
    near, near_from = [block], [me]
    for mask in range(2, count, 2):
        near.append(lax.ppermute(block, axis_name, [(i, i ^ mask) for i in range(count)]))
        near_from.append(jnp.bitwise_xor(me, mask))
    stack = jnp.concatenate(near, axis=0)
    far = lax.ppermute(stack, axis_name, [(i, i ^ 1) for i in range(count)])
    sources = near_from + [jnp.bitwise_xor(source, 1) for source in near_from]
    return jnp.concatenate([stack, far], axis=0), sources


def attention_body(group_ref, bound_ref, q_ref, k_ref, v_ref, segq_ref, segk_ref, prefix_ref, out_ref):
    block = pl.program_id(1)
    seg = pl.program_id(2)
    seg_count = pl.num_programs(2)
    rows = q_ref.shape[2]
    tokens = k_ref.shape[1]
    head_dim = q_ref.shape[3]

    @pl.when(seg == 0)
    def _():
        out_ref[...] = jnp.zeros_like(out_ref)

    first = bound_ref[seg]
    last = bound_ref[seg + seg_count]
    active = (first < (block + 1) * rows) & (last > block * rows)

    @pl.when(active)
    def _():
        seg_q = segq_ref[...]
        seg_k = segk_ref[...]
        t_idx = block * rows + lax.broadcasted_iota(jnp.int32, (rows, tokens), 0)
        u_idx = lax.broadcasted_iota(jnp.int32, (rows, tokens), 1)
        visible = (seg_q == seg_k) & (u_idx <= t_idx)
        keys = k_ref[0]
        values = v_ref[0]
        prefix = prefix_ref[0, 0]
        prefix_keys = prefix[:, :head_dim]
        prefix_values = prefix[:, head_dim:]
        scale = head_dim ** (-0.5)
        mine = seg_q == seg
        contract = (((1,), (1,)), ((), ()))
        for group in range(q_ref.shape[1]):
            query = q_ref[0, group]
            local = lax.dot_general(query, keys, contract, preferred_element_type=jnp.float32) * scale
            local = jnp.where(visible, local, -jnp.inf)
            cached = (
                lax.dot_general(query, prefix_keys, contract, preferred_element_type=jnp.float32)
                * scale
            )
            top = jnp.maximum(
                jnp.max(local, axis=1, keepdims=True), jnp.max(cached, axis=1, keepdims=True)
            )
            local_num = jnp.exp(local - top)
            cached_num = jnp.exp(cached - top)
            total = jnp.sum(local_num, axis=1, keepdims=True) + jnp.sum(
                cached_num, axis=1, keepdims=True
            )
            summed = jnp.dot(
                local_num.astype(jnp.bfloat16), values, preferred_element_type=jnp.float32
            ) + jnp.dot(
                cached_num.astype(jnp.bfloat16), prefix_values, preferred_element_type=jnp.float32
            )
            out_ref[0, group] = jnp.where(mine, summed / total, out_ref[0, group])


def attend(grouped_query, key_rows, value_rows, segment_row, group_row, prefix_heads, interpret=False):
    tok_count, kv_heads, q_groups, head_dim = grouped_query.shape
    seg_count = group_row.shape[0]
    prefix_len = prefix_heads.shape[2]
    rows = min(128, tok_count)
    labels = jnp.arange(seg_count, dtype=jnp.int32)
    first = jnp.sum((segment_row[None, :] < labels[:, None]).astype(jnp.int32), axis=1)
    last = jnp.sum((segment_row[None, :] <= labels[:, None]).astype(jnp.int32), axis=1)
    bounds = jnp.concatenate([first, last])
    query_heads = grouped_query.transpose(1, 2, 0, 3)
    key_heads = key_rows.transpose(1, 0, 2)
    value_heads = value_rows.transpose(1, 0, 2)
    seg_col = segment_row.reshape(tok_count, 1)
    seg_line = segment_row.reshape(1, tok_count)
    grid_spec = pltpu.PrefetchScalarGridSpec(
        num_scalar_prefetch=2,
        grid=(kv_heads, tok_count // rows, seg_count),
        in_specs=[
            pl.BlockSpec((1, q_groups, rows, head_dim), lambda h, b, s, gr, bd: (h, 0, b, 0)),
            pl.BlockSpec((1, tok_count, head_dim), lambda h, b, s, gr, bd: (h, 0, 0)),
            pl.BlockSpec((1, tok_count, head_dim), lambda h, b, s, gr, bd: (h, 0, 0)),
            pl.BlockSpec((rows, 1), lambda h, b, s, gr, bd: (b, 0)),
            pl.BlockSpec((1, tok_count), lambda h, b, s, gr, bd: (0, 0)),
            pl.BlockSpec(
                (1, 1, prefix_len, 2 * head_dim), lambda h, b, s, gr, bd: (gr[s], h, 0, 0)
            ),
        ],
        out_specs=pl.BlockSpec((1, q_groups, rows, head_dim), lambda h, b, s, gr, bd: (h, 0, b, 0)),
    )
    out = pl.pallas_call(
        attention_body,
        grid_spec=grid_spec,
        out_shape=jax.ShapeDtypeStruct((kv_heads, q_groups, tok_count, head_dim), jnp.float32),
        compiler_params=pltpu.CompilerParams(
            dimension_semantics=("arbitrary", "arbitrary", "arbitrary")
        ),
        interpret=interpret,
    )(group_row, bounds, query_heads, key_heads, value_heads, seg_col, seg_line, prefix_heads)
    return out.transpose(2, 0, 1, 3).reshape(tok_count, -1).astype(jnp.bfloat16)


def shards(
    hidden_in,
    segments,
    prefix_group,
    prefix_cache,
    page_table,
    norm_gain,
    w_query,
    w_keyval,
    w_out,
    moe_gain,
    routes,
    gates,
    w_gate_up,
    w_down,
):
    req_count = lax.axis_size("req")
    whole = gather_in_order(hidden_in, "hid", 1)
    tok_count = whole.shape[0]
    model_width = whole.shape[1]
    segment_row = segments[0]
    prefix_len = prefix_cache.shape[1]
    kv_heads = prefix_cache.shape[2]
    head_dim = prefix_cache.shape[3] // 2
    score_scale = head_dim ** (-0.5)
    normed = rms_scale(whole, norm_gain)
    position = positions_of(segment_row, prefix_len)
    projected = jnp.dot(normed, w_query, preferred_element_type=jnp.float32).reshape(
        tok_count, -1, head_dim
    )
    queries = rotate(projected, position).astype(jnp.bfloat16)
    q_groups = queries.shape[1] // kv_heads
    grouped_query = queries.reshape(tok_count, kv_heads, q_groups, head_dim)
    key_value = jnp.dot(normed, w_keyval, preferred_element_type=jnp.float32).reshape(
        tok_count, kv_heads, 2 * head_dim
    )
    key_rows = rotate(key_value[..., :head_dim], position).astype(jnp.bfloat16)
    value_rows = key_value[..., head_dim:].astype(jnp.bfloat16)
    pages = jnp.concatenate([key_rows, value_rows], axis=-1).reshape(
        -1, PAGE, kv_heads, 2 * head_dim
    )
    kv_pages = jnp.zeros_like(pages).at[page_table[0]].set(pages)
    gathered, prefix_from = chip_gather(prefix_cache, "req")
    local_groups = prefix_cache.shape[0]
    group_owner = prefix_group[0] // local_groups
    owner_slot = sum(
        jnp.where(group_owner == source, position, 0) for position, source in enumerate(prefix_from)
    )
    group_place = owner_slot * local_groups + prefix_group[0] % local_groups
    gathered, w_gate_up, w_down = lax.optimization_barrier((gathered, w_gate_up, w_down))
    attention = attend(
        grouped_query, key_rows, value_rows, segment_row, group_place,
        gathered.transpose(0, 2, 1, 3),
    )
    share_width = hidden_in.shape[1]
    whole_attention = jnp.concatenate(shifted_copies(attention, "hid"), axis=1)
    whole_w_out = jnp.concatenate(shifted_copies(w_out, "hid"), axis=0)
    projected_out = jnp.dot(whole_attention, whole_w_out, preferred_element_type=jnp.float32)
    middle = (whole.astype(jnp.float32) + projected_out).astype(jnp.bfloat16)
    middle_share = lax.dynamic_slice_in_dim(
        middle, lax.axis_index("hid") * share_width, share_width, 1
    )
    normed_moe = rms_scale(middle, moe_gain)
    local_experts = w_down.shape[0]
    all_gate_up, weight_from = chip_gather(w_gate_up, "req")
    all_down, _ = chip_gather(w_down, "req")
    expert_ids = jnp.concatenate(
        [source * local_experts + jnp.arange(local_experts, dtype=jnp.int32) for source in weight_from]
    )
    combine = jnp.sum(
        jnp.where(routes[:, :, None] == expert_ids[None, None, :], gates[:, :, None], 0.0), axis=1
    )
    gate_proj = jnp.einsum(
        "td,edf->tef", normed_moe, all_gate_up[:, 0], preferred_element_type=jnp.float32
    )
    up_proj = jnp.einsum(
        "td,edf->tef", normed_moe, all_gate_up[:, 1], preferred_element_type=jnp.float32
    )
    hidden = (jax.nn.silu(gate_proj) * up_proj * combine[:, :, None]).astype(jnp.bfloat16)
    partial_out = jnp.einsum(
        "tef,efd->td", hidden, all_down, preferred_element_type=jnp.float32
    )
    hid_count = lax.axis_size("hid")
    hid_index = lax.axis_index("hid")
    expert_sum = lax.dynamic_slice_in_dim(partial_out, hid_index * share_width, share_width, 1)
    for shift in range(1, hid_count):
        block = (hid_index + shift) % hid_count
        outgoing = lax.dynamic_slice_in_dim(partial_out, block * share_width, share_width, 1)
        pairs = [(index, (index + shift) % hid_count) for index in range(hid_count)]
        incoming = lax.ppermute(outgoing.astype(jnp.bfloat16), "hid", pairs)
        expert_sum = expert_sum + incoming.astype(jnp.float32)
    hidden_out = (middle_share.astype(jnp.float32) + expert_sum).astype(jnp.bfloat16)
    return (hidden_out, kv_pages)


def solution(mesh):
    in_specs = (
        P("req", "hid"),
        P("req", None),
        P("req", None),
        P("req", None, "hid", None),
        P("req", None),
        P(),
        P(None, "hid"),
        P(None, "hid"),
        P("hid", None),
        P(),
        P("req", None),
        P("req", None),
        P("req", None, None, "hid"),
        P("req", "hid", None),
    )
    out_specs = (P("req", "hid"), P("req", None, "hid", None))
    return jax.shard_map(shards, mesh=mesh, in_specs=in_specs, out_specs=out_specs, check_vma=False)
```

```python
import jax
import jax.numpy as jnp
from jax import lax
from jax.sharding import PartitionSpec as P
from jax.experimental import pallas as pl
from jax.experimental.pallas import tpu as pltpu

PAGE = 128


EPSILON = 1e-06
THETA = 10000.0


def rms_scale(row_data, gain_row):
    floats = row_data.astype(jnp.float32)
    mean_square = jnp.mean(floats * floats, axis=-1, keepdims=True)
    return (floats * lax.rsqrt(mean_square + EPSILON) * gain_row).astype(jnp.bfloat16)


def rotate(features, positions):
    half_dim = features.shape[-1] // 2
    frequency = THETA ** (-2.0 * jnp.arange(half_dim, dtype=jnp.float32) / features.shape[-1])
    angles = positions.astype(jnp.float32)[:, None] * frequency[None, :]
    cosine = jnp.cos(angles)[:, None, :]
    sine_part = jnp.sin(angles)[:, None, :]
    front_half = features[..., :half_dim]
    second = features[..., half_dim:]
    return jnp.concatenate(
        [front_half * cosine - second * sine_part, second * cosine + front_half * sine_part],
        axis=-1,
    )


def positions_of(segment_row, offset):
    earlier = jnp.sum((segment_row[None, :] < segment_row[:, None]).astype(jnp.int32), axis=1)
    token_index = jnp.arange(segment_row.shape[0], dtype=jnp.int32)
    return token_index - earlier + offset


def slots_of(route_rows, experts):
    flat_routes = route_rows.reshape(-1)
    onehot = (flat_routes[:, None] == jnp.arange(experts, dtype=jnp.int32)[None, :]).astype(
        jnp.int32
    )
    before = jnp.cumsum(onehot, axis=0) - onehot
    return (flat_routes, jnp.sum(before * onehot, axis=1))


def expert_rows(received, gate_up, down_proj):
    local_experts = down_proj.shape[0]
    slot_count = received.shape[1]
    model_width = received.shape[2]
    grouped = received.reshape(-1, local_experts, slot_count, model_width)
    gate_proj = jnp.einsum(
        "recd,edf->recf", grouped, gate_up[:, 0], preferred_element_type=jnp.float32
    )
    up_proj = jnp.einsum(
        "recd,edf->recf", grouped, gate_up[:, 1], preferred_element_type=jnp.float32
    )
    hidden = (jax.nn.silu(gate_proj) * up_proj).astype(jnp.bfloat16)
    produced = jnp.einsum("recf,efd->recd", hidden, down_proj, preferred_element_type=jnp.float32)
    return produced.reshape(-1, slot_count, model_width)


def shifted_copies(block, axis_name):
    count = lax.axis_size(axis_name)
    copies = [block]
    for shift in range(1, count):
        pairs = [(index, (index + shift) % count) for index in range(count)]
        copies.append(lax.ppermute(block, axis_name, pairs))
    return copies


def gather_in_order(block, axis_name, axis):
    count = lax.axis_size(axis_name)
    copies = jnp.stack(shifted_copies(block, axis_name))
    order = (lax.axis_index(axis_name) - jnp.arange(count, dtype=jnp.int32)) % count
    picked = jnp.take(copies, order, axis=0)
    return jnp.concatenate([picked[index] for index in range(count)], axis=axis)


def attention_body(group_ref, bound_ref, q_ref, k_ref, v_ref, segq_ref, segk_ref, prefix_ref, out_ref):
    block = pl.program_id(1)
    seg = pl.program_id(2)
    seg_count = pl.num_programs(2)
    rows = q_ref.shape[2]
    tokens = k_ref.shape[1]
    head_dim = q_ref.shape[3]

    @pl.when(seg == 0)
    def _():
        out_ref[...] = jnp.zeros_like(out_ref)

    first = bound_ref[seg]
    last = bound_ref[seg + seg_count]
    active = (first < (block + 1) * rows) & (last > block * rows)

    @pl.when(active)
    def _():
        seg_q = segq_ref[...]
        seg_k = segk_ref[...]
        t_idx = block * rows + lax.broadcasted_iota(jnp.int32, (rows, tokens), 0)
        u_idx = lax.broadcasted_iota(jnp.int32, (rows, tokens), 1)
        visible = (seg_q == seg_k) & (u_idx <= t_idx)
        keys = k_ref[0]
        values = v_ref[0]
        prefix = prefix_ref[0, 0]
        prefix_keys = prefix[:, :head_dim]
        prefix_values = prefix[:, head_dim:]
        scale = head_dim ** (-0.5)
        mine = seg_q == seg
        contract = (((1,), (1,)), ((), ()))
        for group in range(q_ref.shape[1]):
            query = q_ref[0, group]
            local = lax.dot_general(query, keys, contract, preferred_element_type=jnp.float32) * scale
            local = jnp.where(visible, local, -jnp.inf)
            cached = (
                lax.dot_general(query, prefix_keys, contract, preferred_element_type=jnp.float32)
                * scale
            )
            top = jnp.maximum(
                jnp.max(local, axis=1, keepdims=True), jnp.max(cached, axis=1, keepdims=True)
            )
            local_num = jnp.exp(local - top)
            cached_num = jnp.exp(cached - top)
            total = jnp.sum(local_num, axis=1, keepdims=True) + jnp.sum(
                cached_num, axis=1, keepdims=True
            )
            summed = jnp.dot(
                local_num.astype(jnp.bfloat16), values, preferred_element_type=jnp.float32
            ) + jnp.dot(
                cached_num.astype(jnp.bfloat16), prefix_values, preferred_element_type=jnp.float32
            )
            out_ref[0, group] = jnp.where(mine, summed / total, out_ref[0, group])


def attend(grouped_query, key_rows, value_rows, segment_row, group_row, prefix_heads, interpret=False):
    tok_count, kv_heads, q_groups, head_dim = grouped_query.shape
    seg_count = group_row.shape[0]
    prefix_len = prefix_heads.shape[2]
    rows = min(128, tok_count)
    labels = jnp.arange(seg_count, dtype=jnp.int32)
    first = jnp.sum((segment_row[None, :] < labels[:, None]).astype(jnp.int32), axis=1)
    last = jnp.sum((segment_row[None, :] <= labels[:, None]).astype(jnp.int32), axis=1)
    bounds = jnp.concatenate([first, last])
    query_heads = grouped_query.transpose(1, 2, 0, 3)
    key_heads = key_rows.transpose(1, 0, 2)
    value_heads = value_rows.transpose(1, 0, 2)
    seg_col = segment_row.reshape(tok_count, 1)
    seg_line = segment_row.reshape(1, tok_count)
    grid_spec = pltpu.PrefetchScalarGridSpec(
        num_scalar_prefetch=2,
        grid=(kv_heads, tok_count // rows, seg_count),
        in_specs=[
            pl.BlockSpec((1, q_groups, rows, head_dim), lambda h, b, s, gr, bd: (h, 0, b, 0)),
            pl.BlockSpec((1, tok_count, head_dim), lambda h, b, s, gr, bd: (h, 0, 0)),
            pl.BlockSpec((1, tok_count, head_dim), lambda h, b, s, gr, bd: (h, 0, 0)),
            pl.BlockSpec((rows, 1), lambda h, b, s, gr, bd: (b, 0)),
            pl.BlockSpec((1, tok_count), lambda h, b, s, gr, bd: (0, 0)),
            pl.BlockSpec(
                (1, 1, prefix_len, 2 * head_dim), lambda h, b, s, gr, bd: (gr[s], h, 0, 0)
            ),
        ],
        out_specs=pl.BlockSpec((1, q_groups, rows, head_dim), lambda h, b, s, gr, bd: (h, 0, b, 0)),
    )
    out = pl.pallas_call(
        attention_body,
        grid_spec=grid_spec,
        out_shape=jax.ShapeDtypeStruct((kv_heads, q_groups, tok_count, head_dim), jnp.float32),
        compiler_params=pltpu.CompilerParams(
            dimension_semantics=("arbitrary", "arbitrary", "arbitrary")
        ),
        interpret=interpret,
    )(group_row, bounds, query_heads, key_heads, value_heads, seg_col, seg_line, prefix_heads)
    return out.transpose(2, 0, 1, 3).reshape(tok_count, -1).astype(jnp.bfloat16)


def shards(
    hidden_in,
    segments,
    prefix_group,
    prefix_cache,
    page_table,
    norm_gain,
    w_query,
    w_keyval,
    w_out,
    moe_gain,
    routes,
    gates,
    w_gate_up,
    w_down,
):
    req_count = lax.axis_size("req")
    whole = gather_in_order(hidden_in, "hid", 1)
    tok_count = whole.shape[0]
    model_width = whole.shape[1]
    segment_row = segments[0]
    prefix_len = prefix_cache.shape[1]
    kv_heads = prefix_cache.shape[2]
    head_dim = prefix_cache.shape[3] // 2
    score_scale = head_dim ** (-0.5)
    normed = rms_scale(whole, norm_gain)
    position = positions_of(segment_row, prefix_len)
    projected = jnp.dot(normed, w_query, preferred_element_type=jnp.float32).reshape(
        tok_count, -1, head_dim
    )
    queries = rotate(projected, position).astype(jnp.bfloat16)
    queries, w_gate_up, w_down = lax.optimization_barrier((queries, w_gate_up, w_down))
    q_groups = queries.shape[1] // kv_heads
    grouped_query = queries.reshape(tok_count, kv_heads, q_groups, head_dim)
    key_value = jnp.dot(normed, w_keyval, preferred_element_type=jnp.float32).reshape(
        tok_count, kv_heads, 2 * head_dim
    )
    key_rows = rotate(key_value[..., :head_dim], position).astype(jnp.bfloat16)
    value_rows = key_value[..., head_dim:].astype(jnp.bfloat16)
    pages = jnp.concatenate([key_rows, value_rows], axis=-1).reshape(
        -1, PAGE, kv_heads, 2 * head_dim
    )
    kv_pages = jnp.zeros_like(pages).at[page_table[0]].set(pages)
    gathered = lax.all_gather(prefix_cache, "req", axis=0, tiled=True)
    attention = attend(
        grouped_query, key_rows, value_rows, segment_row, prefix_group[0],
        gathered.transpose(0, 2, 1, 3),
    )
    share_width = hidden_in.shape[1]
    whole_attention = jnp.concatenate(shifted_copies(attention, "hid"), axis=1)
    whole_w_out = jnp.concatenate(shifted_copies(w_out, "hid"), axis=0)
    projected_out = jnp.dot(whole_attention, whole_w_out, preferred_element_type=jnp.float32)
    middle = (whole.astype(jnp.float32) + projected_out).astype(jnp.bfloat16)
    middle_share = lax.dynamic_slice_in_dim(
        middle, lax.axis_index("hid") * share_width, share_width, 1
    )
    normed_moe = rms_scale(middle, moe_gain)
    local_experts = w_down.shape[0]
    gate_up_size = w_gate_up[0].size
    packed = jnp.concatenate(
        [w_gate_up.reshape(local_experts, -1), w_down.reshape(local_experts, -1)], axis=1
    )
    packed = lax.all_gather(packed, "req", axis=0, tiled=True)
    experts = packed.shape[0]
    all_gate_up = packed[:, :gate_up_size].reshape((experts,) + w_gate_up.shape[1:])
    all_down = packed[:, gate_up_size:].reshape((experts,) + w_down.shape[1:])
    expert_ids = jnp.arange(experts, dtype=jnp.int32)
    combine = jnp.sum(
        jnp.where(routes[:, :, None] == expert_ids[None, None, :], gates[:, :, None], 0.0), axis=1
    )
    gate_proj = jnp.einsum(
        "td,edf->tef", normed_moe, all_gate_up[:, 0], preferred_element_type=jnp.float32
    )
    up_proj = jnp.einsum(
        "td,edf->tef", normed_moe, all_gate_up[:, 1], preferred_element_type=jnp.float32
    )
    hidden = (jax.nn.silu(gate_proj) * up_proj * combine[:, :, None]).astype(jnp.bfloat16)
    partial_out = jnp.einsum(
        "tef,efd->td", hidden, all_down, preferred_element_type=jnp.float32
    )
    hid_count = lax.axis_size("hid")
    hid_index = lax.axis_index("hid")
    expert_sum = lax.dynamic_slice_in_dim(partial_out, hid_index * share_width, share_width, 1)
    for shift in range(1, hid_count):
        block = (hid_index + shift) % hid_count
        outgoing = lax.dynamic_slice_in_dim(partial_out, block * share_width, share_width, 1)
        pairs = [(index, (index + shift) % hid_count) for index in range(hid_count)]
        incoming = lax.ppermute(outgoing.astype(jnp.bfloat16), "hid", pairs)
        expert_sum = expert_sum + incoming.astype(jnp.float32)
    hidden_out = (middle_share.astype(jnp.float32) + expert_sum).astype(jnp.bfloat16)
    return (hidden_out, kv_pages)


def solution(mesh):
    in_specs = (
        P("req", "hid"),
        P("req", None),
        P("req", None),
        P("req", None, "hid", None),
        P("req", None),
        P(),
        P(None, "hid"),
        P(None, "hid"),
        P("hid", None),
        P(),
        P("req", None),
        P("req", None),
        P("req", None, None, "hid"),
        P("req", "hid", None),
    )
    out_specs = (P("req", "hid"), P("req", None, "hid", None))
    return jax.shard_map(shards, mesh=mesh, in_specs=in_specs, out_specs=out_specs, check_vma=False)
```

```python
import jax
import jax.numpy as jnp
from jax import lax
from jax.sharding import PartitionSpec as P
from jax.experimental import pallas as pl
from jax.experimental.pallas import tpu as pltpu

PAGE = 128


EPSILON = 1e-06
THETA = 10000.0


def rms_scale(row_data, gain_row):
    floats = row_data.astype(jnp.float32)
    mean_square = jnp.mean(floats * floats, axis=-1, keepdims=True)
    return (floats * lax.rsqrt(mean_square + EPSILON) * gain_row).astype(jnp.bfloat16)


def rotate(features, positions):
    half_dim = features.shape[-1] // 2
    frequency = THETA ** (-2.0 * jnp.arange(half_dim, dtype=jnp.float32) / features.shape[-1])
    angles = positions.astype(jnp.float32)[:, None] * frequency[None, :]
    cosine = jnp.cos(angles)[:, None, :]
    sine_part = jnp.sin(angles)[:, None, :]
    front_half = features[..., :half_dim]
    second = features[..., half_dim:]
    return jnp.concatenate(
        [front_half * cosine - second * sine_part, second * cosine + front_half * sine_part],
        axis=-1,
    )


def positions_of(segment_row, offset):
    earlier = jnp.sum((segment_row[None, :] < segment_row[:, None]).astype(jnp.int32), axis=1)
    token_index = jnp.arange(segment_row.shape[0], dtype=jnp.int32)
    return token_index - earlier + offset


def slots_of(route_rows, experts):
    flat_routes = route_rows.reshape(-1)
    onehot = (flat_routes[:, None] == jnp.arange(experts, dtype=jnp.int32)[None, :]).astype(
        jnp.int32
    )
    before = jnp.cumsum(onehot, axis=0) - onehot
    return (flat_routes, jnp.sum(before * onehot, axis=1))


def expert_rows(received, gate_up, down_proj):
    local_experts = down_proj.shape[0]
    slot_count = received.shape[1]
    model_width = received.shape[2]
    grouped = received.reshape(-1, local_experts, slot_count, model_width)
    gate_proj = jnp.einsum(
        "recd,edf->recf", grouped, gate_up[:, 0], preferred_element_type=jnp.float32
    )
    up_proj = jnp.einsum(
        "recd,edf->recf", grouped, gate_up[:, 1], preferred_element_type=jnp.float32
    )
    hidden = (jax.nn.silu(gate_proj) * up_proj).astype(jnp.bfloat16)
    produced = jnp.einsum("recf,efd->recd", hidden, down_proj, preferred_element_type=jnp.float32)
    return produced.reshape(-1, slot_count, model_width)


def shifted_copies(block, axis_name):
    count = lax.axis_size(axis_name)
    copies = [block]
    for shift in range(1, count):
        pairs = [(index, (index + shift) % count) for index in range(count)]
        copies.append(lax.ppermute(block, axis_name, pairs))
    return copies


def gather_in_order(block, axis_name, axis):
    count = lax.axis_size(axis_name)
    copies = jnp.stack(shifted_copies(block, axis_name))
    order = (lax.axis_index(axis_name) - jnp.arange(count, dtype=jnp.int32)) % count
    picked = jnp.take(copies, order, axis=0)
    return jnp.concatenate([picked[index] for index in range(count)], axis=axis)


def attention_body(group_ref, bound_ref, q_ref, k_ref, v_ref, segq_ref, segk_ref, prefix_ref, out_ref):
    block = pl.program_id(1)
    seg = pl.program_id(2)
    seg_count = pl.num_programs(2)
    rows = q_ref.shape[2]
    tokens = k_ref.shape[1]
    head_dim = q_ref.shape[3]

    @pl.when(seg == 0)
    def _():
        out_ref[...] = jnp.zeros_like(out_ref)

    first = bound_ref[seg]
    last = bound_ref[seg + seg_count]
    active = (first < (block + 1) * rows) & (last > block * rows)

    @pl.when(active)
    def _():
        seg_q = segq_ref[...]
        seg_k = segk_ref[...]
        t_idx = block * rows + lax.broadcasted_iota(jnp.int32, (rows, tokens), 0)
        u_idx = lax.broadcasted_iota(jnp.int32, (rows, tokens), 1)
        visible = (seg_q == seg_k) & (u_idx <= t_idx)
        keys = k_ref[0]
        values = v_ref[0]
        prefix = prefix_ref[0, 0]
        prefix_keys = prefix[:, :head_dim]
        prefix_values = prefix[:, head_dim:]
        scale = head_dim ** (-0.5)
        mine = seg_q == seg
        contract = (((1,), (1,)), ((), ()))
        for group in range(q_ref.shape[1]):
            query = q_ref[0, group]
            local = lax.dot_general(query, keys, contract, preferred_element_type=jnp.float32) * scale
            local = jnp.where(visible, local, -jnp.inf)
            cached = (
                lax.dot_general(query, prefix_keys, contract, preferred_element_type=jnp.float32)
                * scale
            )
            top = jnp.maximum(
                jnp.max(local, axis=1, keepdims=True), jnp.max(cached, axis=1, keepdims=True)
            )
            local_num = jnp.exp(local - top)
            cached_num = jnp.exp(cached - top)
            total = jnp.sum(local_num, axis=1, keepdims=True) + jnp.sum(
                cached_num, axis=1, keepdims=True
            )
            summed = jnp.dot(
                local_num.astype(jnp.bfloat16), values, preferred_element_type=jnp.float32
            ) + jnp.dot(
                cached_num.astype(jnp.bfloat16), prefix_values, preferred_element_type=jnp.float32
            )
            out_ref[0, group] = jnp.where(mine, summed / total, out_ref[0, group])


def attend(grouped_query, key_rows, value_rows, segment_row, group_row, prefix_heads, interpret=False):
    tok_count, kv_heads, q_groups, head_dim = grouped_query.shape
    seg_count = group_row.shape[0]
    prefix_len = prefix_heads.shape[2]
    rows = min(128, tok_count)
    labels = jnp.arange(seg_count, dtype=jnp.int32)
    first = jnp.sum((segment_row[None, :] < labels[:, None]).astype(jnp.int32), axis=1)
    last = jnp.sum((segment_row[None, :] <= labels[:, None]).astype(jnp.int32), axis=1)
    bounds = jnp.concatenate([first, last])
    query_heads = grouped_query.transpose(1, 2, 0, 3)
    key_heads = key_rows.transpose(1, 0, 2)
    value_heads = value_rows.transpose(1, 0, 2)
    seg_col = segment_row.reshape(tok_count, 1)
    seg_line = segment_row.reshape(1, tok_count)
    grid_spec = pltpu.PrefetchScalarGridSpec(
        num_scalar_prefetch=2,
        grid=(kv_heads, tok_count // rows, seg_count),
        in_specs=[
            pl.BlockSpec((1, q_groups, rows, head_dim), lambda h, b, s, gr, bd: (h, 0, b, 0)),
            pl.BlockSpec((1, tok_count, head_dim), lambda h, b, s, gr, bd: (h, 0, 0)),
            pl.BlockSpec((1, tok_count, head_dim), lambda h, b, s, gr, bd: (h, 0, 0)),
            pl.BlockSpec((rows, 1), lambda h, b, s, gr, bd: (b, 0)),
            pl.BlockSpec((1, tok_count), lambda h, b, s, gr, bd: (0, 0)),
            pl.BlockSpec(
                (1, 1, prefix_len, 2 * head_dim), lambda h, b, s, gr, bd: (gr[s], h, 0, 0)
            ),
        ],
        out_specs=pl.BlockSpec((1, q_groups, rows, head_dim), lambda h, b, s, gr, bd: (h, 0, b, 0)),
    )
    out = pl.pallas_call(
        attention_body,
        grid_spec=grid_spec,
        out_shape=jax.ShapeDtypeStruct((kv_heads, q_groups, tok_count, head_dim), jnp.float32),
        compiler_params=pltpu.CompilerParams(
            dimension_semantics=("arbitrary", "arbitrary", "arbitrary")
        ),
        interpret=interpret,
    )(group_row, bounds, query_heads, key_heads, value_heads, seg_col, seg_line, prefix_heads)
    return out.transpose(2, 0, 1, 3).reshape(tok_count, -1).astype(jnp.bfloat16)


def shards(
    hidden_in,
    segments,
    prefix_group,
    prefix_cache,
    page_table,
    norm_gain,
    w_query,
    w_keyval,
    w_out,
    moe_gain,
    routes,
    gates,
    w_gate_up,
    w_down,
):
    req_count = lax.axis_size("req")
    whole = gather_in_order(hidden_in, "hid", 1)
    tok_count = whole.shape[0]
    model_width = whole.shape[1]
    segment_row = segments[0]
    prefix_len = prefix_cache.shape[1]
    kv_heads = prefix_cache.shape[2]
    head_dim = prefix_cache.shape[3] // 2
    score_scale = head_dim ** (-0.5)
    normed = rms_scale(whole, norm_gain)
    position = positions_of(segment_row, prefix_len)
    projected = jnp.dot(normed, w_query, preferred_element_type=jnp.float32).reshape(
        tok_count, -1, head_dim
    )
    queries = rotate(projected, position).astype(jnp.bfloat16)
    queries, w_gate_up, w_down = lax.optimization_barrier((queries, w_gate_up, w_down))
    q_groups = queries.shape[1] // kv_heads
    grouped_query = queries.reshape(tok_count, kv_heads, q_groups, head_dim)
    key_value = jnp.dot(normed, w_keyval, preferred_element_type=jnp.float32).reshape(
        tok_count, kv_heads, 2 * head_dim
    )
    key_rows = rotate(key_value[..., :head_dim], position).astype(jnp.bfloat16)
    value_rows = key_value[..., head_dim:].astype(jnp.bfloat16)
    pages = jnp.concatenate([key_rows, value_rows], axis=-1).reshape(
        -1, PAGE, kv_heads, 2 * head_dim
    )
    kv_pages = jnp.zeros_like(pages).at[page_table[0]].set(pages)
    gathered = lax.all_gather(prefix_cache, "req", axis=0, tiled=True)
    attention = attend(
        grouped_query, key_rows, value_rows, segment_row, prefix_group[0],
        gathered.transpose(0, 2, 1, 3),
    )
    share_width = hidden_in.shape[1]
    whole_attention = jnp.concatenate(shifted_copies(attention, "hid"), axis=1)
    whole_w_out = jnp.concatenate(shifted_copies(w_out, "hid"), axis=0)
    projected_out = jnp.dot(whole_attention, whole_w_out, preferred_element_type=jnp.float32)
    middle = (whole.astype(jnp.float32) + projected_out).astype(jnp.bfloat16)
    middle_share = lax.dynamic_slice_in_dim(
        middle, lax.axis_index("hid") * share_width, share_width, 1
    )
    normed_moe = rms_scale(middle, moe_gain)
    local_experts, hidden_units, model_cols = w_down.shape
    lane_width = w_gate_up.shape[-1]
    down_view = w_down.reshape(local_experts, 1, -1, lane_width)
    packed = lax.all_gather(
        jnp.concatenate([w_gate_up, down_view], axis=1), "req", axis=0, tiled=True
    )
    experts = packed.shape[0]
    all_gate_up = packed[:, :2]
    all_down = packed[:, 2].reshape(experts, hidden_units, model_cols // lane_width, lane_width)
    expert_ids = jnp.arange(experts, dtype=jnp.int32)
    combine = jnp.sum(
        jnp.where(routes[:, :, None] == expert_ids[None, None, :], gates[:, :, None], 0.0), axis=1
    )
    gate_proj = jnp.einsum(
        "td,edf->tef", normed_moe, all_gate_up[:, 0], preferred_element_type=jnp.float32
    )
    up_proj = jnp.einsum(
        "td,edf->tef", normed_moe, all_gate_up[:, 1], preferred_element_type=jnp.float32
    )
    hidden = (jax.nn.silu(gate_proj) * up_proj * combine[:, :, None]).astype(jnp.bfloat16)
    partial_out = jnp.einsum(
        "tef,efhl->thl", hidden, all_down, preferred_element_type=jnp.float32
    ).reshape(tok_count, model_width)
    hid_count = lax.axis_size("hid")
    hid_index = lax.axis_index("hid")
    expert_sum = lax.dynamic_slice_in_dim(partial_out, hid_index * share_width, share_width, 1)
    for shift in range(1, hid_count):
        block = (hid_index + shift) % hid_count
        outgoing = lax.dynamic_slice_in_dim(partial_out, block * share_width, share_width, 1)
        pairs = [(index, (index + shift) % hid_count) for index in range(hid_count)]
        incoming = lax.ppermute(outgoing.astype(jnp.bfloat16), "hid", pairs)
        expert_sum = expert_sum + incoming.astype(jnp.float32)
    hidden_out = (middle_share.astype(jnp.float32) + expert_sum).astype(jnp.bfloat16)
    return (hidden_out, kv_pages)


def solution(mesh):
    in_specs = (
        P("req", "hid"),
        P("req", None),
        P("req", None),
        P("req", None, "hid", None),
        P("req", None),
        P(),
        P(None, "hid"),
        P(None, "hid"),
        P("hid", None),
        P(),
        P("req", None),
        P("req", None),
        P("req", None, None, "hid"),
        P("req", "hid", None),
    )
    out_specs = (P("req", "hid"), P("req", None, "hid", None))
    return jax.shard_map(shards, mesh=mesh, in_specs=in_specs, out_specs=out_specs, check_vma=False)
```

```python
import jax
import jax.numpy as jnp
from jax import lax
from jax.sharding import PartitionSpec as P
from jax.experimental import pallas as pl
from jax.experimental.pallas import tpu as pltpu

PAGE = 128


EPSILON = 1e-06
THETA = 10000.0


def rms_scale(row_data, gain_row):
    floats = row_data.astype(jnp.float32)
    mean_square = jnp.mean(floats * floats, axis=-1, keepdims=True)
    return (floats * lax.rsqrt(mean_square + EPSILON) * gain_row).astype(jnp.bfloat16)


def rotate(features, positions):
    half_dim = features.shape[-1] // 2
    frequency = THETA ** (-2.0 * jnp.arange(half_dim, dtype=jnp.float32) / features.shape[-1])
    angles = positions.astype(jnp.float32)[:, None] * frequency[None, :]
    cosine = jnp.cos(angles)[:, None, :]
    sine_part = jnp.sin(angles)[:, None, :]
    front_half = features[..., :half_dim]
    second = features[..., half_dim:]
    return jnp.concatenate(
        [front_half * cosine - second * sine_part, second * cosine + front_half * sine_part],
        axis=-1,
    )


def positions_of(segment_row, offset):
    earlier = jnp.sum((segment_row[None, :] < segment_row[:, None]).astype(jnp.int32), axis=1)
    token_index = jnp.arange(segment_row.shape[0], dtype=jnp.int32)
    return token_index - earlier + offset


def slots_of(route_rows, experts):
    flat_routes = route_rows.reshape(-1)
    onehot = (flat_routes[:, None] == jnp.arange(experts, dtype=jnp.int32)[None, :]).astype(
        jnp.int32
    )
    before = jnp.cumsum(onehot, axis=0) - onehot
    return (flat_routes, jnp.sum(before * onehot, axis=1))


def expert_rows(received, gate_up, down_proj):
    local_experts = down_proj.shape[0]
    slot_count = received.shape[1]
    model_width = received.shape[2]
    grouped = received.reshape(-1, local_experts, slot_count, model_width)
    gate_proj = jnp.einsum(
        "recd,edf->recf", grouped, gate_up[:, 0], preferred_element_type=jnp.float32
    )
    up_proj = jnp.einsum(
        "recd,edf->recf", grouped, gate_up[:, 1], preferred_element_type=jnp.float32
    )
    hidden = (jax.nn.silu(gate_proj) * up_proj).astype(jnp.bfloat16)
    produced = jnp.einsum("recf,efd->recd", hidden, down_proj, preferred_element_type=jnp.float32)
    return produced.reshape(-1, slot_count, model_width)


def shifted_copies(block, axis_name):
    count = lax.axis_size(axis_name)
    copies = [block]
    for shift in range(1, count):
        pairs = [(index, (index + shift) % count) for index in range(count)]
        copies.append(lax.ppermute(block, axis_name, pairs))
    return copies


def gather_in_order(block, axis_name, axis):
    count = lax.axis_size(axis_name)
    copies = jnp.stack(shifted_copies(block, axis_name))
    order = (lax.axis_index(axis_name) - jnp.arange(count, dtype=jnp.int32)) % count
    picked = jnp.take(copies, order, axis=0)
    return jnp.concatenate([picked[index] for index in range(count)], axis=axis)


def attention_body(group_ref, bound_ref, q_ref, k_ref, v_ref, segq_ref, segk_ref, prefix_ref, out_ref):
    block = pl.program_id(1)
    seg = pl.program_id(2)
    seg_count = pl.num_programs(2)
    rows = q_ref.shape[2]
    tokens = k_ref.shape[1]
    head_dim = q_ref.shape[3]

    @pl.when(seg == 0)
    def _():
        out_ref[...] = jnp.zeros_like(out_ref)

    first = bound_ref[seg]
    last = bound_ref[seg + seg_count]
    active = (first < (block + 1) * rows) & (last > block * rows)

    @pl.when(active)
    def _():
        seg_q = segq_ref[...]
        seg_k = segk_ref[...]
        t_idx = block * rows + lax.broadcasted_iota(jnp.int32, (rows, tokens), 0)
        u_idx = lax.broadcasted_iota(jnp.int32, (rows, tokens), 1)
        visible = (seg_q == seg_k) & (u_idx <= t_idx)
        keys = k_ref[0]
        values = v_ref[0]
        prefix = prefix_ref[0, 0]
        prefix_keys = prefix[:, :head_dim]
        prefix_values = prefix[:, head_dim:]
        scale = head_dim ** (-0.5)
        mine = seg_q == seg
        contract = (((1,), (1,)), ((), ()))
        for group in range(q_ref.shape[1]):
            query = q_ref[0, group]
            local = lax.dot_general(query, keys, contract, preferred_element_type=jnp.float32) * scale
            local = jnp.where(visible, local, -jnp.inf)
            cached = (
                lax.dot_general(query, prefix_keys, contract, preferred_element_type=jnp.float32)
                * scale
            )
            top = jnp.maximum(
                jnp.max(local, axis=1, keepdims=True), jnp.max(cached, axis=1, keepdims=True)
            )
            local_num = jnp.exp(local - top)
            cached_num = jnp.exp(cached - top)
            total = jnp.sum(local_num, axis=1, keepdims=True) + jnp.sum(
                cached_num, axis=1, keepdims=True
            )
            summed = jnp.dot(
                local_num.astype(jnp.bfloat16), values, preferred_element_type=jnp.float32
            ) + jnp.dot(
                cached_num.astype(jnp.bfloat16), prefix_values, preferred_element_type=jnp.float32
            )
            out_ref[0, group] = jnp.where(mine, summed / total, out_ref[0, group])


def attend(grouped_query, key_rows, value_rows, segment_row, group_row, prefix_heads, interpret=False):
    tok_count, kv_heads, q_groups, head_dim = grouped_query.shape
    seg_count = group_row.shape[0]
    prefix_len = prefix_heads.shape[2]
    rows = min(128, tok_count)
    labels = jnp.arange(seg_count, dtype=jnp.int32)
    first = jnp.sum((segment_row[None, :] < labels[:, None]).astype(jnp.int32), axis=1)
    last = jnp.sum((segment_row[None, :] <= labels[:, None]).astype(jnp.int32), axis=1)
    bounds = jnp.concatenate([first, last])
    query_heads = grouped_query.transpose(1, 2, 0, 3)
    key_heads = key_rows.transpose(1, 0, 2)
    value_heads = value_rows.transpose(1, 0, 2)
    seg_col = segment_row.reshape(tok_count, 1)
    seg_line = segment_row.reshape(1, tok_count)
    grid_spec = pltpu.PrefetchScalarGridSpec(
        num_scalar_prefetch=2,
        grid=(kv_heads, tok_count // rows, seg_count),
        in_specs=[
            pl.BlockSpec((1, q_groups, rows, head_dim), lambda h, b, s, gr, bd: (h, 0, b, 0)),
            pl.BlockSpec((1, tok_count, head_dim), lambda h, b, s, gr, bd: (h, 0, 0)),
            pl.BlockSpec((1, tok_count, head_dim), lambda h, b, s, gr, bd: (h, 0, 0)),
            pl.BlockSpec((rows, 1), lambda h, b, s, gr, bd: (b, 0)),
            pl.BlockSpec((1, tok_count), lambda h, b, s, gr, bd: (0, 0)),
            pl.BlockSpec(
                (1, 1, prefix_len, 2 * head_dim), lambda h, b, s, gr, bd: (gr[s], h, 0, 0)
            ),
        ],
        out_specs=pl.BlockSpec((1, q_groups, rows, head_dim), lambda h, b, s, gr, bd: (h, 0, b, 0)),
    )
    out = pl.pallas_call(
        attention_body,
        grid_spec=grid_spec,
        out_shape=jax.ShapeDtypeStruct((kv_heads, q_groups, tok_count, head_dim), jnp.float32),
        compiler_params=pltpu.CompilerParams(
            dimension_semantics=("arbitrary", "arbitrary", "arbitrary")
        ),
        interpret=interpret,
    )(group_row, bounds, query_heads, key_heads, value_heads, seg_col, seg_line, prefix_heads)
    return out.transpose(2, 0, 1, 3).reshape(tok_count, -1).astype(jnp.bfloat16)


def down_body(hidden_ref, weight_ref, out_ref):
    total = jnp.zeros(out_ref.shape[1:], jnp.float32)
    for expert in range(hidden_ref.shape[0]):
        total = total + jnp.dot(
            hidden_ref[expert], weight_ref[0, expert], preferred_element_type=jnp.float32
        )
    out_ref[0] = total


def down_project(hidden, packed):
    experts, tok_count, units = hidden.shape
    lanes = packed.shape[3]
    col_blocks = packed.shape[2] // units
    return pl.pallas_call(
        down_body,
        grid=(col_blocks,),
        in_specs=[
            pl.BlockSpec((experts, tok_count, units), lambda c: (0, 0, 0)),
            pl.BlockSpec((1, experts, units, lanes), lambda c: (2, 0, c, 0)),
        ],
        out_specs=pl.BlockSpec((1, tok_count, lanes), lambda c: (c, 0, 0)),
        out_shape=jax.ShapeDtypeStruct((col_blocks, tok_count, lanes), jnp.float32),
        compiler_params=pltpu.CompilerParams(dimension_semantics=("arbitrary",)),
    )(hidden, packed)


def shards(
    hidden_in,
    segments,
    prefix_group,
    prefix_cache,
    page_table,
    norm_gain,
    w_query,
    w_keyval,
    w_out,
    moe_gain,
    routes,
    gates,
    w_gate_up,
    w_down,
):
    req_count = lax.axis_size("req")
    whole = gather_in_order(hidden_in, "hid", 1)
    tok_count = whole.shape[0]
    model_width = whole.shape[1]
    segment_row = segments[0]
    prefix_len = prefix_cache.shape[1]
    kv_heads = prefix_cache.shape[2]
    head_dim = prefix_cache.shape[3] // 2
    score_scale = head_dim ** (-0.5)
    normed = rms_scale(whole, norm_gain)
    position = positions_of(segment_row, prefix_len)
    projected = jnp.dot(normed, w_query, preferred_element_type=jnp.float32).reshape(
        tok_count, -1, head_dim
    )
    queries = rotate(projected, position).astype(jnp.bfloat16)
    queries, w_gate_up, w_down = lax.optimization_barrier((queries, w_gate_up, w_down))
    q_groups = queries.shape[1] // kv_heads
    grouped_query = queries.reshape(tok_count, kv_heads, q_groups, head_dim)
    key_value = jnp.dot(normed, w_keyval, preferred_element_type=jnp.float32).reshape(
        tok_count, kv_heads, 2 * head_dim
    )
    key_rows = rotate(key_value[..., :head_dim], position).astype(jnp.bfloat16)
    value_rows = key_value[..., head_dim:].astype(jnp.bfloat16)
    pages = jnp.concatenate([key_rows, value_rows], axis=-1).reshape(
        -1, PAGE, kv_heads, 2 * head_dim
    )
    kv_pages = jnp.zeros_like(pages).at[page_table[0]].set(pages)
    gathered = lax.all_gather(prefix_cache, "req", axis=0, tiled=True)
    attention = attend(
        grouped_query, key_rows, value_rows, segment_row, prefix_group[0],
        gathered.transpose(0, 2, 1, 3),
    )
    share_width = hidden_in.shape[1]
    whole_attention = jnp.concatenate(shifted_copies(attention, "hid"), axis=1)
    whole_w_out = jnp.concatenate(shifted_copies(w_out, "hid"), axis=0)
    projected_out = jnp.dot(whole_attention, whole_w_out, preferred_element_type=jnp.float32)
    middle = (whole.astype(jnp.float32) + projected_out).astype(jnp.bfloat16)
    middle_share = lax.dynamic_slice_in_dim(
        middle, lax.axis_index("hid") * share_width, share_width, 1
    )
    normed_moe = rms_scale(middle, moe_gain)
    local_experts, hidden_units, model_cols = w_down.shape
    lane_width = w_gate_up.shape[-1]
    down_view = (
        w_down.reshape(local_experts, hidden_units, model_cols // lane_width, lane_width)
        .transpose(0, 2, 1, 3)
        .reshape(local_experts, 1, -1, lane_width)
    )
    packed = jnp.concatenate([w_gate_up, down_view], axis=1).transpose(1, 0, 2, 3)
    packed = lax.all_gather(packed, "req", axis=1, tiled=True)
    experts = packed.shape[1]
    expert_ids = jnp.arange(experts, dtype=jnp.int32)
    combine = jnp.sum(
        jnp.where(routes[:, :, None] == expert_ids[None, None, :], gates[:, :, None], 0.0), axis=1
    )
    gate_proj = jnp.einsum(
        "td,edf->etf", normed_moe, packed[0], preferred_element_type=jnp.float32
    )
    up_proj = jnp.einsum(
        "td,edf->etf", normed_moe, packed[1], preferred_element_type=jnp.float32
    )
    hidden = (jax.nn.silu(gate_proj) * up_proj * combine.T[:, :, None]).astype(jnp.bfloat16)
    partial_out = down_project(hidden, packed).transpose(1, 0, 2).reshape(tok_count, model_width)
    hid_count = lax.axis_size("hid")
    hid_index = lax.axis_index("hid")
    expert_sum = lax.dynamic_slice_in_dim(partial_out, hid_index * share_width, share_width, 1)
    for shift in range(1, hid_count):
        block = (hid_index + shift) % hid_count
        outgoing = lax.dynamic_slice_in_dim(partial_out, block * share_width, share_width, 1)
        pairs = [(index, (index + shift) % hid_count) for index in range(hid_count)]
        incoming = lax.ppermute(outgoing.astype(jnp.bfloat16), "hid", pairs)
        expert_sum = expert_sum + incoming.astype(jnp.float32)
    hidden_out = (middle_share.astype(jnp.float32) + expert_sum).astype(jnp.bfloat16)
    return (hidden_out, kv_pages)


def solution(mesh):
    in_specs = (
        P("req", "hid"),
        P("req", None),
        P("req", None),
        P("req", None, "hid", None),
        P("req", None),
        P(),
        P(None, "hid"),
        P(None, "hid"),
        P("hid", None),
        P(),
        P("req", None),
        P("req", None),
        P("req", None, None, "hid"),
        P("req", "hid", None),
    )
    out_specs = (P("req", "hid"), P("req", None, "hid", None))
    return jax.shard_map(shards, mesh=mesh, in_specs=in_specs, out_specs=out_specs, check_vma=False)
```

```python
import functools

import jax
import jax.numpy as jnp
from jax import lax
from jax.sharding import PartitionSpec as P
from jax.experimental import pallas as pl
from jax.experimental.pallas import tpu as pltpu

PAGE = 128


EPSILON = 1e-06
THETA = 10000.0


def rms_scale(row_data, gain_row):
    floats = row_data.astype(jnp.float32)
    mean_square = jnp.mean(floats * floats, axis=-1, keepdims=True)
    return (floats * lax.rsqrt(mean_square + EPSILON) * gain_row).astype(jnp.bfloat16)


def rotate(features, positions):
    half_dim = features.shape[-1] // 2
    frequency = THETA ** (-2.0 * jnp.arange(half_dim, dtype=jnp.float32) / features.shape[-1])
    angles = positions.astype(jnp.float32)[:, None] * frequency[None, :]
    cosine = jnp.cos(angles)[:, None, :]
    sine_part = jnp.sin(angles)[:, None, :]
    front_half = features[..., :half_dim]
    second = features[..., half_dim:]
    return jnp.concatenate(
        [front_half * cosine - second * sine_part, second * cosine + front_half * sine_part],
        axis=-1,
    )


def positions_of(segment_row, offset):
    earlier = jnp.sum((segment_row[None, :] < segment_row[:, None]).astype(jnp.int32), axis=1)
    token_index = jnp.arange(segment_row.shape[0], dtype=jnp.int32)
    return token_index - earlier + offset


def slots_of(route_rows, experts):
    flat_routes = route_rows.reshape(-1)
    onehot = (flat_routes[:, None] == jnp.arange(experts, dtype=jnp.int32)[None, :]).astype(
        jnp.int32
    )
    before = jnp.cumsum(onehot, axis=0) - onehot
    return (flat_routes, jnp.sum(before * onehot, axis=1))


def expert_rows(received, gate_up, down_proj):
    local_experts = down_proj.shape[0]
    slot_count = received.shape[1]
    model_width = received.shape[2]
    grouped = received.reshape(-1, local_experts, slot_count, model_width)
    gate_proj = jnp.einsum(
        "recd,edf->recf", grouped, gate_up[:, 0], preferred_element_type=jnp.float32
    )
    up_proj = jnp.einsum(
        "recd,edf->recf", grouped, gate_up[:, 1], preferred_element_type=jnp.float32
    )
    hidden = (jax.nn.silu(gate_proj) * up_proj).astype(jnp.bfloat16)
    produced = jnp.einsum("recf,efd->recd", hidden, down_proj, preferred_element_type=jnp.float32)
    return produced.reshape(-1, slot_count, model_width)


def shifted_copies(block, axis_name):
    count = lax.axis_size(axis_name)
    copies = [block]
    for shift in range(1, count):
        pairs = [(index, (index + shift) % count) for index in range(count)]
        copies.append(lax.ppermute(block, axis_name, pairs))
    return copies


def gather_in_order(block, axis_name, axis):
    count = lax.axis_size(axis_name)
    copies = jnp.stack(shifted_copies(block, axis_name))
    order = (lax.axis_index(axis_name) - jnp.arange(count, dtype=jnp.int32)) % count
    picked = jnp.take(copies, order, axis=0)
    return jnp.concatenate([picked[index] for index in range(count)], axis=axis)


def attention_body(group_ref, bound_ref, q_ref, k_ref, v_ref, segq_ref, segk_ref, prefix_ref, out_ref):
    block = pl.program_id(1)
    seg = pl.program_id(2)
    seg_count = pl.num_programs(2)
    rows = q_ref.shape[2]
    tokens = k_ref.shape[1]
    head_dim = q_ref.shape[3]

    @pl.when(seg == 0)
    def _():
        out_ref[...] = jnp.zeros_like(out_ref)

    first = bound_ref[seg]
    last = bound_ref[seg + seg_count]
    active = (first < (block + 1) * rows) & (last > block * rows)

    @pl.when(active)
    def _():
        seg_q = segq_ref[...]
        seg_k = segk_ref[...]
        t_idx = block * rows + lax.broadcasted_iota(jnp.int32, (rows, tokens), 0)
        u_idx = lax.broadcasted_iota(jnp.int32, (rows, tokens), 1)
        visible = (seg_q == seg_k) & (u_idx <= t_idx)
        keys = k_ref[0]
        values = v_ref[0]
        prefix = prefix_ref[0, 0]
        prefix_keys = prefix[:, :head_dim]
        prefix_values = prefix[:, head_dim:]
        scale = head_dim ** (-0.5)
        mine = seg_q == seg
        contract = (((1,), (1,)), ((), ()))
        for group in range(q_ref.shape[1]):
            query = q_ref[0, group]
            local = lax.dot_general(query, keys, contract, preferred_element_type=jnp.float32) * scale
            local = jnp.where(visible, local, -jnp.inf)
            cached = (
                lax.dot_general(query, prefix_keys, contract, preferred_element_type=jnp.float32)
                * scale
            )
            top = jnp.maximum(
                jnp.max(local, axis=1, keepdims=True), jnp.max(cached, axis=1, keepdims=True)
            )
            local_num = jnp.exp(local - top)
            cached_num = jnp.exp(cached - top)
            total = jnp.sum(local_num, axis=1, keepdims=True) + jnp.sum(
                cached_num, axis=1, keepdims=True
            )
            summed = jnp.dot(
                local_num.astype(jnp.bfloat16), values, preferred_element_type=jnp.float32
            ) + jnp.dot(
                cached_num.astype(jnp.bfloat16), prefix_values, preferred_element_type=jnp.float32
            )
            out_ref[0, group] = jnp.where(mine, summed / total, out_ref[0, group])


def attend(grouped_query, key_rows, value_rows, segment_row, group_row, prefix_heads, interpret=False):
    tok_count, kv_heads, q_groups, head_dim = grouped_query.shape
    seg_count = group_row.shape[0]
    prefix_len = prefix_heads.shape[2]
    rows = min(128, tok_count)
    labels = jnp.arange(seg_count, dtype=jnp.int32)
    first = jnp.sum((segment_row[None, :] < labels[:, None]).astype(jnp.int32), axis=1)
    last = jnp.sum((segment_row[None, :] <= labels[:, None]).astype(jnp.int32), axis=1)
    bounds = jnp.concatenate([first, last])
    query_heads = grouped_query.transpose(1, 2, 0, 3)
    key_heads = key_rows.transpose(1, 0, 2)
    value_heads = value_rows.transpose(1, 0, 2)
    seg_col = segment_row.reshape(tok_count, 1)
    seg_line = segment_row.reshape(1, tok_count)
    grid_spec = pltpu.PrefetchScalarGridSpec(
        num_scalar_prefetch=2,
        grid=(kv_heads, tok_count // rows, seg_count),
        in_specs=[
            pl.BlockSpec((1, q_groups, rows, head_dim), lambda h, b, s, gr, bd: (h, 0, b, 0)),
            pl.BlockSpec((1, tok_count, head_dim), lambda h, b, s, gr, bd: (h, 0, 0)),
            pl.BlockSpec((1, tok_count, head_dim), lambda h, b, s, gr, bd: (h, 0, 0)),
            pl.BlockSpec((rows, 1), lambda h, b, s, gr, bd: (b, 0)),
            pl.BlockSpec((1, tok_count), lambda h, b, s, gr, bd: (0, 0)),
            pl.BlockSpec(
                (1, 1, prefix_len, 2 * head_dim), lambda h, b, s, gr, bd: (gr[s], h, 0, 0)
            ),
        ],
        out_specs=pl.BlockSpec((1, q_groups, rows, head_dim), lambda h, b, s, gr, bd: (h, 0, b, 0)),
    )
    out = pl.pallas_call(
        attention_body,
        grid_spec=grid_spec,
        out_shape=jax.ShapeDtypeStruct((kv_heads, q_groups, tok_count, head_dim), jnp.float32),
        compiler_params=pltpu.CompilerParams(
            dimension_semantics=("arbitrary", "arbitrary", "arbitrary")
        ),
        interpret=interpret,
    )(group_row, bounds, query_heads, key_heads, value_heads, seg_col, seg_line, prefix_heads)
    return out.transpose(2, 0, 1, 3).reshape(tok_count, -1).astype(jnp.bfloat16)


def down_body(hidden_ref, weight_ref, out_ref):
    total = jnp.zeros(out_ref.shape[1:], jnp.float32)
    for expert in range(hidden_ref.shape[0]):
        total = total + jnp.dot(
            hidden_ref[expert], weight_ref[0, expert], preferred_element_type=jnp.float32
        )
    out_ref[0] = total


def down_project(hidden, packed):
    experts, tok_count, units = hidden.shape
    lanes = packed.shape[3]
    col_blocks = packed.shape[2] // units
    return pl.pallas_call(
        down_body,
        grid=(col_blocks,),
        in_specs=[
            pl.BlockSpec((experts, tok_count, units), lambda c: (0, 0, 0)),
            pl.BlockSpec((1, experts, units, lanes), lambda c: (2, 0, c, 0)),
        ],
        out_specs=pl.BlockSpec((1, tok_count, lanes), lambda c: (c, 0, 0)),
        out_shape=jax.ShapeDtypeStruct((col_blocks, tok_count, lanes), jnp.float32),
        compiler_params=pltpu.CompilerParams(dimension_semantics=("arbitrary",)),
    )(hidden, packed)


def shards(
    req_axes,
    hidden_in,
    segments,
    prefix_group,
    prefix_cache,
    page_table,
    norm_gain,
    w_query,
    w_keyval,
    w_out,
    moe_gain,
    routes,
    gates,
    w_gate_up,
    w_down,
):
    req_count = lax.axis_size(req_axes)
    whole = gather_in_order(hidden_in, "hid", 1)
    tok_count = whole.shape[0]
    model_width = whole.shape[1]
    segment_row = segments[0]
    prefix_len = prefix_cache.shape[1]
    kv_heads = prefix_cache.shape[2]
    head_dim = prefix_cache.shape[3] // 2
    score_scale = head_dim ** (-0.5)
    normed = rms_scale(whole, norm_gain)
    position = positions_of(segment_row, prefix_len)
    projected = jnp.dot(normed, w_query, preferred_element_type=jnp.float32).reshape(
        tok_count, -1, head_dim
    )
    queries = rotate(projected, position).astype(jnp.bfloat16)
    queries, w_gate_up, w_down = lax.optimization_barrier((queries, w_gate_up, w_down))
    q_groups = queries.shape[1] // kv_heads
    grouped_query = queries.reshape(tok_count, kv_heads, q_groups, head_dim)
    key_value = jnp.dot(normed, w_keyval, preferred_element_type=jnp.float32).reshape(
        tok_count, kv_heads, 2 * head_dim
    )
    key_rows = rotate(key_value[..., :head_dim], position).astype(jnp.bfloat16)
    value_rows = key_value[..., head_dim:].astype(jnp.bfloat16)
    pages = jnp.concatenate([key_rows, value_rows], axis=-1).reshape(
        -1, PAGE, kv_heads, 2 * head_dim
    )
    kv_pages = jnp.zeros_like(pages).at[page_table[0]].set(pages)
    gathered, prefix_from = staged_gather(prefix_cache, req_axes, 0)
    local_groups = prefix_cache.shape[0]
    group_owner = prefix_group[0] // local_groups
    group_place = (
        jnp.sum(jnp.where(group_owner[:, None] == prefix_from[None, :], jnp.arange(prefix_from.shape[0])[None, :], 0), axis=1)
        * local_groups
        + prefix_group[0] % local_groups
    )
    attention = attend(
        grouped_query, key_rows, value_rows, segment_row, group_place,
        gathered.transpose(0, 2, 1, 3),
    )
    share_width = hidden_in.shape[1]
    whole_attention = jnp.concatenate(shifted_copies(attention, "hid"), axis=1)
    whole_w_out = jnp.concatenate(shifted_copies(w_out, "hid"), axis=0)
    projected_out = jnp.dot(whole_attention, whole_w_out, preferred_element_type=jnp.float32)
    middle = (whole.astype(jnp.float32) + projected_out).astype(jnp.bfloat16)
    middle_share = lax.dynamic_slice_in_dim(
        middle, lax.axis_index("hid") * share_width, share_width, 1
    )
    normed_moe = rms_scale(middle, moe_gain)
    local_experts, hidden_units, model_cols = w_down.shape
    lane_width = w_gate_up.shape[-1]
    down_view = (
        w_down.reshape(local_experts, hidden_units, model_cols // lane_width, lane_width)
        .transpose(0, 2, 1, 3)
        .reshape(local_experts, 1, -1, lane_width)
    )
    packed = jnp.concatenate([w_gate_up, down_view], axis=1).transpose(1, 0, 2, 3)
    packed, weight_from = staged_gather(packed, req_axes, 1)
    expert_ids = (
        weight_from[:, None] * local_experts + jnp.arange(local_experts, dtype=jnp.int32)[None, :]
    ).reshape(-1)
    combine = jnp.sum(
        jnp.where(routes[:, :, None] == expert_ids[None, None, :], gates[:, :, None], 0.0), axis=1
    )
    gate_proj = jnp.einsum(
        "td,edf->etf", normed_moe, packed[0], preferred_element_type=jnp.float32
    )
    up_proj = jnp.einsum(
        "td,edf->etf", normed_moe, packed[1], preferred_element_type=jnp.float32
    )
    hidden = (jax.nn.silu(gate_proj) * up_proj * combine.T[:, :, None]).astype(jnp.bfloat16)
    partial_out = down_project(hidden, packed).transpose(1, 0, 2).reshape(tok_count, model_width)
    hid_count = lax.axis_size("hid")
    hid_index = lax.axis_index("hid")
    expert_sum = lax.dynamic_slice_in_dim(partial_out, hid_index * share_width, share_width, 1)
    for shift in range(1, hid_count):
        block = (hid_index + shift) % hid_count
        outgoing = lax.dynamic_slice_in_dim(partial_out, block * share_width, share_width, 1)
        pairs = [(index, (index + shift) % hid_count) for index in range(hid_count)]
        incoming = lax.ppermute(outgoing.astype(jnp.bfloat16), "hid", pairs)
        expert_sum = expert_sum + incoming.astype(jnp.float32)
    hidden_out = (middle_share.astype(jnp.float32) + expert_sum).astype(jnp.bfloat16)
    return (hidden_out, kv_pages)


def staged_gather(block, req_axes, axis):
    if isinstance(req_axes, str):
        count = lax.axis_size(req_axes)
        return lax.all_gather(block, req_axes, axis=axis, tiled=True), jnp.arange(count)
    chips = lax.axis_size(req_axes[0])
    cores = lax.axis_size(req_axes[1])
    near = lax.all_gather(block, req_axes[0], axis=axis, tiled=True)
    whole = lax.all_gather(near, req_axes[1], axis=axis, tiled=True)
    order = jnp.arange(chips * cores, dtype=jnp.int32)
    return whole, (order % chips) * cores + order // chips


def req_layout(mesh):
    devices = mesh.devices
    rows = devices.shape[0]
    if rows % 2 or devices.ndim != 2:
        return mesh, "req"
    for pair in range(0, rows, 2):
        for col in range(devices.shape[1]):
            first, second = devices[pair, col], devices[pair + 1, col]
            same_chip = getattr(first, "coords", None) == getattr(second, "coords", None)
            if getattr(first, "coords", None) is None or not same_chip:
                return mesh, "req"
    shaped = devices.reshape(rows // 2, 2, devices.shape[1])
    return jax.sharding.Mesh(shaped, ("chip", "core", "hid")), ("chip", "core")


def solution(mesh):
    mesh, req_axes = req_layout(mesh)
    in_specs = (
        P(req_axes, "hid"),
        P(req_axes, None),
        P(req_axes, None),
        P(req_axes, None, "hid", None),
        P(req_axes, None),
        P(),
        P(None, "hid"),
        P(None, "hid"),
        P("hid", None),
        P(),
        P(req_axes, None),
        P(req_axes, None),
        P(req_axes, None, None, "hid"),
        P(req_axes, "hid", None),
    )
    out_specs = (P(req_axes, "hid"), P(req_axes, None, "hid", None))
    return jax.shard_map(functools.partial(shards, req_axes), mesh=mesh, in_specs=in_specs, out_specs=out_specs, check_vma=False)
```

```python
import functools

import jax
import jax.numpy as jnp
from jax import lax
from jax.sharding import PartitionSpec as P
from jax.experimental import pallas as pl
from jax.experimental.pallas import tpu as pltpu

PAGE = 128


EPSILON = 1e-06
THETA = 10000.0


def rms_scale(row_data, gain_row):
    floats = row_data.astype(jnp.float32)
    mean_square = jnp.mean(floats * floats, axis=-1, keepdims=True)
    return (floats * lax.rsqrt(mean_square + EPSILON) * gain_row).astype(jnp.bfloat16)


def rotate(features, positions):
    half_dim = features.shape[-1] // 2
    frequency = THETA ** (-2.0 * jnp.arange(half_dim, dtype=jnp.float32) / features.shape[-1])
    angles = positions.astype(jnp.float32)[:, None] * frequency[None, :]
    cosine = jnp.cos(angles)[:, None, :]
    sine_part = jnp.sin(angles)[:, None, :]
    front_half = features[..., :half_dim]
    second = features[..., half_dim:]
    return jnp.concatenate(
        [front_half * cosine - second * sine_part, second * cosine + front_half * sine_part],
        axis=-1,
    )


def positions_of(segment_row, offset):
    earlier = jnp.sum((segment_row[None, :] < segment_row[:, None]).astype(jnp.int32), axis=1)
    token_index = jnp.arange(segment_row.shape[0], dtype=jnp.int32)
    return token_index - earlier + offset


def slots_of(route_rows, experts):
    flat_routes = route_rows.reshape(-1)
    onehot = (flat_routes[:, None] == jnp.arange(experts, dtype=jnp.int32)[None, :]).astype(
        jnp.int32
    )
    before = jnp.cumsum(onehot, axis=0) - onehot
    return (flat_routes, jnp.sum(before * onehot, axis=1))


def expert_rows(received, gate_up, down_proj):
    local_experts = down_proj.shape[0]
    slot_count = received.shape[1]
    model_width = received.shape[2]
    grouped = received.reshape(-1, local_experts, slot_count, model_width)
    gate_proj = jnp.einsum(
        "recd,edf->recf", grouped, gate_up[:, 0], preferred_element_type=jnp.float32
    )
    up_proj = jnp.einsum(
        "recd,edf->recf", grouped, gate_up[:, 1], preferred_element_type=jnp.float32
    )
    hidden = (jax.nn.silu(gate_proj) * up_proj).astype(jnp.bfloat16)
    produced = jnp.einsum("recf,efd->recd", hidden, down_proj, preferred_element_type=jnp.float32)
    return produced.reshape(-1, slot_count, model_width)


def shifted_copies(block, axis_name):
    count = lax.axis_size(axis_name)
    copies = [block]
    for shift in range(1, count):
        pairs = [(index, (index + shift) % count) for index in range(count)]
        copies.append(lax.ppermute(block, axis_name, pairs))
    return copies


def gather_in_order(block, axis_name, axis):
    count = lax.axis_size(axis_name)
    copies = jnp.stack(shifted_copies(block, axis_name))
    order = (lax.axis_index(axis_name) - jnp.arange(count, dtype=jnp.int32)) % count
    picked = jnp.take(copies, order, axis=0)
    return jnp.concatenate([picked[index] for index in range(count)], axis=axis)


def chip_gather(block, axis_name):
    count = lax.axis_size(axis_name)
    me = lax.axis_index(axis_name)
    if count < 2 or count & (count - 1):
        copies = shifted_copies(block, axis_name)
        sources = [(me - shift) % count for shift in range(count)]
        return jnp.concatenate(copies, axis=0), sources
    near, near_from = [block], [me]
    for mask in range(2, count, 2):
        near.append(lax.ppermute(block, axis_name, [(i, i ^ mask) for i in range(count)]))
        near_from.append(jnp.bitwise_xor(me, mask))
    stack = jnp.concatenate(near, axis=0)
    far = lax.ppermute(stack, axis_name, [(i, i ^ 1) for i in range(count)])
    sources = near_from + [jnp.bitwise_xor(source, 1) for source in near_from]
    return jnp.concatenate([stack, far], axis=0), sources


def attention_body(group_ref, bound_ref, q_ref, k_ref, v_ref, segq_ref, segk_ref, prefix_ref, out_ref):
    block = pl.program_id(1)
    seg = pl.program_id(2)
    seg_count = pl.num_programs(2)
    rows = q_ref.shape[2]
    tokens = k_ref.shape[1]
    head_dim = q_ref.shape[3]

    @pl.when(seg == 0)
    def _():
        out_ref[...] = jnp.zeros_like(out_ref)

    first = bound_ref[seg]
    last = bound_ref[seg + seg_count]
    active = (first < (block + 1) * rows) & (last > block * rows)

    @pl.when(active)
    def _():
        seg_q = segq_ref[...]
        seg_k = segk_ref[...]
        t_idx = block * rows + lax.broadcasted_iota(jnp.int32, (rows, tokens), 0)
        u_idx = lax.broadcasted_iota(jnp.int32, (rows, tokens), 1)
        visible = (seg_q == seg_k) & (u_idx <= t_idx)
        keys = k_ref[0]
        values = v_ref[0]
        prefix = prefix_ref[0, 0]
        prefix_keys = prefix[:, :head_dim]
        prefix_values = prefix[:, head_dim:]
        scale = head_dim ** (-0.5)
        mine = seg_q == seg
        contract = (((1,), (1,)), ((), ()))
        for group in range(q_ref.shape[1]):
            query = q_ref[0, group]
            local = lax.dot_general(query, keys, contract, preferred_element_type=jnp.float32) * scale
            local = jnp.where(visible, local, -jnp.inf)
            cached = (
                lax.dot_general(query, prefix_keys, contract, preferred_element_type=jnp.float32)
                * scale
            )
            top = jnp.maximum(
                jnp.max(local, axis=1, keepdims=True), jnp.max(cached, axis=1, keepdims=True)
            )
            local_num = jnp.exp(local - top)
            cached_num = jnp.exp(cached - top)
            total = jnp.sum(local_num, axis=1, keepdims=True) + jnp.sum(
                cached_num, axis=1, keepdims=True
            )
            summed = jnp.dot(
                local_num.astype(jnp.bfloat16), values, preferred_element_type=jnp.float32
            ) + jnp.dot(
                cached_num.astype(jnp.bfloat16), prefix_values, preferred_element_type=jnp.float32
            )
            out_ref[0, group] = jnp.where(mine, summed / total, out_ref[0, group])


def attend(grouped_query, key_rows, value_rows, segment_row, group_row, prefix_heads, interpret=False):
    tok_count, kv_heads, q_groups, head_dim = grouped_query.shape
    seg_count = group_row.shape[0]
    prefix_len = prefix_heads.shape[2]
    rows = min(128, tok_count)
    labels = jnp.arange(seg_count, dtype=jnp.int32)
    first = jnp.sum((segment_row[None, :] < labels[:, None]).astype(jnp.int32), axis=1)
    last = jnp.sum((segment_row[None, :] <= labels[:, None]).astype(jnp.int32), axis=1)
    bounds = jnp.concatenate([first, last])
    query_heads = grouped_query.transpose(1, 2, 0, 3)
    key_heads = key_rows.transpose(1, 0, 2)
    value_heads = value_rows.transpose(1, 0, 2)
    seg_col = segment_row.reshape(tok_count, 1)
    seg_line = segment_row.reshape(1, tok_count)
    grid_spec = pltpu.PrefetchScalarGridSpec(
        num_scalar_prefetch=2,
        grid=(kv_heads, tok_count // rows, seg_count),
        in_specs=[
            pl.BlockSpec((1, q_groups, rows, head_dim), lambda h, b, s, gr, bd: (h, 0, b, 0)),
            pl.BlockSpec((1, tok_count, head_dim), lambda h, b, s, gr, bd: (h, 0, 0)),
            pl.BlockSpec((1, tok_count, head_dim), lambda h, b, s, gr, bd: (h, 0, 0)),
            pl.BlockSpec((rows, 1), lambda h, b, s, gr, bd: (b, 0)),
            pl.BlockSpec((1, tok_count), lambda h, b, s, gr, bd: (0, 0)),
            pl.BlockSpec(
                (1, 1, prefix_len, 2 * head_dim), lambda h, b, s, gr, bd: (gr[s], h, 0, 0)
            ),
        ],
        out_specs=pl.BlockSpec((1, q_groups, rows, head_dim), lambda h, b, s, gr, bd: (h, 0, b, 0)),
    )
    out = pl.pallas_call(
        attention_body,
        grid_spec=grid_spec,
        out_shape=jax.ShapeDtypeStruct((kv_heads, q_groups, tok_count, head_dim), jnp.float32),
        compiler_params=pltpu.CompilerParams(
            dimension_semantics=("arbitrary", "arbitrary", "arbitrary")
        ),
        interpret=interpret,
    )(group_row, bounds, query_heads, key_heads, value_heads, seg_col, seg_line, prefix_heads)
    return out.transpose(2, 0, 1, 3).reshape(tok_count, -1).astype(jnp.bfloat16)


def down_body(hidden_ref, weight_ref, out_ref):
    total = jnp.zeros(out_ref.shape[1:], jnp.float32)
    for expert in range(hidden_ref.shape[0]):
        total = total + jnp.dot(
            hidden_ref[expert], weight_ref[0, expert], preferred_element_type=jnp.float32
        )
    out_ref[0] = total


def down_project(hidden, packed):
    experts, tok_count, units = hidden.shape
    lanes = packed.shape[3]
    col_blocks = packed.shape[2] // units
    return pl.pallas_call(
        down_body,
        grid=(col_blocks,),
        in_specs=[
            pl.BlockSpec((experts, tok_count, units), lambda c: (0, 0, 0)),
            pl.BlockSpec((1, experts, units, lanes), lambda c: (2, 0, c, 0)),
        ],
        out_specs=pl.BlockSpec((1, tok_count, lanes), lambda c: (c, 0, 0)),
        out_shape=jax.ShapeDtypeStruct((col_blocks, tok_count, lanes), jnp.float32),
        compiler_params=pltpu.CompilerParams(dimension_semantics=("arbitrary",)),
    )(hidden, packed)


def shards(
    hidden_in,
    segments,
    prefix_group,
    prefix_cache,
    page_table,
    norm_gain,
    w_query,
    w_keyval,
    w_out,
    moe_gain,
    routes,
    gates,
    w_gate_up,
    w_down,
):
    req_count = lax.axis_size("req")
    whole = gather_in_order(hidden_in, "hid", 1)
    tok_count = whole.shape[0]
    model_width = whole.shape[1]
    segment_row = segments[0]
    prefix_len = prefix_cache.shape[1]
    kv_heads = prefix_cache.shape[2]
    head_dim = prefix_cache.shape[3] // 2
    score_scale = head_dim ** (-0.5)
    normed = rms_scale(whole, norm_gain)
    position = positions_of(segment_row, prefix_len)
    projected = jnp.dot(normed, w_query, preferred_element_type=jnp.float32).reshape(
        tok_count, -1, head_dim
    )
    queries = rotate(projected, position).astype(jnp.bfloat16)
    q_groups = queries.shape[1] // kv_heads
    grouped_query = queries.reshape(tok_count, kv_heads, q_groups, head_dim)
    key_value = jnp.dot(normed, w_keyval, preferred_element_type=jnp.float32).reshape(
        tok_count, kv_heads, 2 * head_dim
    )
    key_rows = rotate(key_value[..., :head_dim], position).astype(jnp.bfloat16)
    value_rows = key_value[..., head_dim:].astype(jnp.bfloat16)
    pages = jnp.concatenate([key_rows, value_rows], axis=-1).reshape(
        -1, PAGE, kv_heads, 2 * head_dim
    )
    kv_pages = jnp.zeros_like(pages).at[page_table[0]].set(pages)
    gathered, prefix_from = chip_gather(prefix_cache, "req")
    local_groups = prefix_cache.shape[0]
    group_owner = prefix_group[0] // local_groups
    owner_slot = sum(
        jnp.where(group_owner == source, position, 0) for position, source in enumerate(prefix_from)
    )
    group_place = owner_slot * local_groups + prefix_group[0] % local_groups
    attention = attend(
        grouped_query, key_rows, value_rows, segment_row, group_place,
        gathered.transpose(0, 2, 1, 3),
    )
    share_width = hidden_in.shape[1]
    whole_attention = jnp.concatenate(shifted_copies(attention, "hid"), axis=1)
    whole_w_out = jnp.concatenate(shifted_copies(w_out, "hid"), axis=0)
    projected_out = jnp.dot(whole_attention, whole_w_out, preferred_element_type=jnp.float32)
    middle = (whole.astype(jnp.float32) + projected_out).astype(jnp.bfloat16)
    middle_share = lax.dynamic_slice_in_dim(
        middle, lax.axis_index("hid") * share_width, share_width, 1
    )
    normed_moe = rms_scale(middle, moe_gain)
    local_experts, hidden_units, model_cols = w_down.shape
    lane_width = w_gate_up.shape[-1]
    down_view = (
        w_down.reshape(local_experts, hidden_units, model_cols // lane_width, lane_width)
        .transpose(0, 2, 1, 3)
        .reshape(local_experts, 1, -1, lane_width)
    )
    packed = jnp.concatenate([w_gate_up, down_view], axis=1).transpose(1, 0, 2, 3)
    packed = lax.all_gather(packed, "req", axis=1, tiled=True)
    experts = packed.shape[1]
    expert_ids = jnp.arange(experts, dtype=jnp.int32)
    combine = jnp.sum(
        jnp.where(routes[:, :, None] == expert_ids[None, None, :], gates[:, :, None], 0.0), axis=1
    )
    gate_proj = jnp.einsum(
        "td,edf->etf", normed_moe, packed[0], preferred_element_type=jnp.float32
    )
    up_proj = jnp.einsum(
        "td,edf->etf", normed_moe, packed[1], preferred_element_type=jnp.float32
    )
    hidden = (jax.nn.silu(gate_proj) * up_proj * combine.T[:, :, None]).astype(jnp.bfloat16)
    partial_out = down_project(hidden, packed).transpose(1, 0, 2).reshape(tok_count, model_width)
    hid_count = lax.axis_size("hid")
    hid_index = lax.axis_index("hid")
    expert_sum = lax.dynamic_slice_in_dim(partial_out, hid_index * share_width, share_width, 1)
    for shift in range(1, hid_count):
        block = (hid_index + shift) % hid_count
        outgoing = lax.dynamic_slice_in_dim(partial_out, block * share_width, share_width, 1)
        pairs = [(index, (index + shift) % hid_count) for index in range(hid_count)]
        incoming = lax.ppermute(outgoing.astype(jnp.bfloat16), "hid", pairs)
        expert_sum = expert_sum + incoming.astype(jnp.float32)
    hidden_out = (middle_share.astype(jnp.float32) + expert_sum).astype(jnp.bfloat16)
    return (hidden_out, kv_pages)


def solution(mesh):
    in_specs = (
        P("req", "hid"),
        P("req", None),
        P("req", None),
        P("req", None, "hid", None),
        P("req", None),
        P(),
        P(None, "hid"),
        P(None, "hid"),
        P("hid", None),
        P(),
        P("req", None),
        P("req", None),
        P("req", None, None, "hid"),
        P("req", "hid", None),
    )
    out_specs = (P("req", "hid"), P("req", None, "hid", None))
    return jax.shard_map(shards, mesh=mesh, in_specs=in_specs, out_specs=out_specs, check_vma=False)
```

```python
import functools

import jax
import jax.numpy as jnp
from jax import lax
from jax.sharding import PartitionSpec as P
from jax.experimental import pallas as pl
from jax.experimental.pallas import tpu as pltpu

PAGE = 128


EPSILON = 1e-06
THETA = 10000.0


def rms_scale(row_data, gain_row):
    floats = row_data.astype(jnp.float32)
    mean_square = jnp.mean(floats * floats, axis=-1, keepdims=True)
    return (floats * lax.rsqrt(mean_square + EPSILON) * gain_row).astype(jnp.bfloat16)


def rotate(features, positions):
    half_dim = features.shape[-1] // 2
    frequency = THETA ** (-2.0 * jnp.arange(half_dim, dtype=jnp.float32) / features.shape[-1])
    angles = positions.astype(jnp.float32)[:, None] * frequency[None, :]
    cosine = jnp.cos(angles)[:, None, :]
    sine_part = jnp.sin(angles)[:, None, :]
    front_half = features[..., :half_dim]
    second = features[..., half_dim:]
    return jnp.concatenate(
        [front_half * cosine - second * sine_part, second * cosine + front_half * sine_part],
        axis=-1,
    )


def positions_of(segment_row, offset):
    earlier = jnp.sum((segment_row[None, :] < segment_row[:, None]).astype(jnp.int32), axis=1)
    token_index = jnp.arange(segment_row.shape[0], dtype=jnp.int32)
    return token_index - earlier + offset


def slots_of(route_rows, experts):
    flat_routes = route_rows.reshape(-1)
    onehot = (flat_routes[:, None] == jnp.arange(experts, dtype=jnp.int32)[None, :]).astype(
        jnp.int32
    )
    before = jnp.cumsum(onehot, axis=0) - onehot
    return (flat_routes, jnp.sum(before * onehot, axis=1))


def expert_rows(received, gate_up, down_proj):
    local_experts = down_proj.shape[0]
    slot_count = received.shape[1]
    model_width = received.shape[2]
    grouped = received.reshape(-1, local_experts, slot_count, model_width)
    gate_proj = jnp.einsum(
        "recd,edf->recf", grouped, gate_up[:, 0], preferred_element_type=jnp.float32
    )
    up_proj = jnp.einsum(
        "recd,edf->recf", grouped, gate_up[:, 1], preferred_element_type=jnp.float32
    )
    hidden = (jax.nn.silu(gate_proj) * up_proj).astype(jnp.bfloat16)
    produced = jnp.einsum("recf,efd->recd", hidden, down_proj, preferred_element_type=jnp.float32)
    return produced.reshape(-1, slot_count, model_width)


def shifted_copies(block, axis_name):
    count = lax.axis_size(axis_name)
    copies = [block]
    for shift in range(1, count):
        pairs = [(index, (index + shift) % count) for index in range(count)]
        copies.append(lax.ppermute(block, axis_name, pairs))
    return copies


def gather_in_order(block, axis_name, axis):
    count = lax.axis_size(axis_name)
    copies = jnp.stack(shifted_copies(block, axis_name))
    order = (lax.axis_index(axis_name) - jnp.arange(count, dtype=jnp.int32)) % count
    picked = jnp.take(copies, order, axis=0)
    return jnp.concatenate([picked[index] for index in range(count)], axis=axis)


def attention_body(group_ref, bound_ref, q_ref, k_ref, v_ref, segq_ref, segk_ref, prefix_ref, out_ref):
    block = pl.program_id(1)
    seg = pl.program_id(2)
    seg_count = pl.num_programs(2)
    rows = q_ref.shape[2]
    tokens = k_ref.shape[1]
    head_dim = q_ref.shape[3]

    @pl.when(seg == 0)
    def _():
        out_ref[...] = jnp.zeros_like(out_ref)

    first = bound_ref[seg]
    last = bound_ref[seg + seg_count]
    active = (first < (block + 1) * rows) & (last > block * rows)

    @pl.when(active)
    def _():
        seg_q = segq_ref[...]
        seg_k = segk_ref[...]
        t_idx = block * rows + lax.broadcasted_iota(jnp.int32, (rows, tokens), 0)
        u_idx = lax.broadcasted_iota(jnp.int32, (rows, tokens), 1)
        visible = (seg_q == seg_k) & (u_idx <= t_idx)
        keys = k_ref[0]
        values = v_ref[0]
        prefix = prefix_ref[0, 0]
        prefix_keys = prefix[:, :head_dim]
        prefix_values = prefix[:, head_dim:]
        scale = head_dim ** (-0.5)
        mine = seg_q == seg
        contract = (((1,), (1,)), ((), ()))
        for group in range(q_ref.shape[1]):
            query = q_ref[0, group]
            local = lax.dot_general(query, keys, contract, preferred_element_type=jnp.float32) * scale
            local = jnp.where(visible, local, -jnp.inf)
            cached = (
                lax.dot_general(query, prefix_keys, contract, preferred_element_type=jnp.float32)
                * scale
            )
            top = jnp.maximum(
                jnp.max(local, axis=1, keepdims=True), jnp.max(cached, axis=1, keepdims=True)
            )
            local_num = jnp.exp(local - top)
            cached_num = jnp.exp(cached - top)
            total = jnp.sum(local_num, axis=1, keepdims=True) + jnp.sum(
                cached_num, axis=1, keepdims=True
            )
            summed = jnp.dot(
                local_num.astype(jnp.bfloat16), values, preferred_element_type=jnp.float32
            ) + jnp.dot(
                cached_num.astype(jnp.bfloat16), prefix_values, preferred_element_type=jnp.float32
            )
            out_ref[0, group] = jnp.where(mine, summed / total, out_ref[0, group])


def attend(grouped_query, key_rows, value_rows, segment_row, group_row, prefix_heads, interpret=False):
    tok_count, kv_heads, q_groups, head_dim = grouped_query.shape
    seg_count = group_row.shape[0]
    prefix_len = prefix_heads.shape[2]
    rows = min(128, tok_count)
    labels = jnp.arange(seg_count, dtype=jnp.int32)
    first = jnp.sum((segment_row[None, :] < labels[:, None]).astype(jnp.int32), axis=1)
    last = jnp.sum((segment_row[None, :] <= labels[:, None]).astype(jnp.int32), axis=1)
    bounds = jnp.concatenate([first, last])
    query_heads = grouped_query.transpose(1, 2, 0, 3)
    key_heads = key_rows.transpose(1, 0, 2)
    value_heads = value_rows.transpose(1, 0, 2)
    seg_col = segment_row.reshape(tok_count, 1)
    seg_line = segment_row.reshape(1, tok_count)
    grid_spec = pltpu.PrefetchScalarGridSpec(
        num_scalar_prefetch=2,
        grid=(kv_heads, tok_count // rows, seg_count),
        in_specs=[
            pl.BlockSpec((1, q_groups, rows, head_dim), lambda h, b, s, gr, bd: (h, 0, b, 0)),
            pl.BlockSpec((1, tok_count, head_dim), lambda h, b, s, gr, bd: (h, 0, 0)),
            pl.BlockSpec((1, tok_count, head_dim), lambda h, b, s, gr, bd: (h, 0, 0)),
            pl.BlockSpec((rows, 1), lambda h, b, s, gr, bd: (b, 0)),
            pl.BlockSpec((1, tok_count), lambda h, b, s, gr, bd: (0, 0)),
            pl.BlockSpec(
                (1, 1, prefix_len, 2 * head_dim), lambda h, b, s, gr, bd: (gr[s], h, 0, 0)
            ),
        ],
        out_specs=pl.BlockSpec((1, q_groups, rows, head_dim), lambda h, b, s, gr, bd: (h, 0, b, 0)),
    )
    out = pl.pallas_call(
        attention_body,
        grid_spec=grid_spec,
        out_shape=jax.ShapeDtypeStruct((kv_heads, q_groups, tok_count, head_dim), jnp.float32),
        compiler_params=pltpu.CompilerParams(
            dimension_semantics=("arbitrary", "arbitrary", "arbitrary")
        ),
        interpret=interpret,
    )(group_row, bounds, query_heads, key_heads, value_heads, seg_col, seg_line, prefix_heads)
    return out.transpose(2, 0, 1, 3).reshape(tok_count, -1).astype(jnp.bfloat16)


def expert_body(normed_ref, combine_ref, weight_ref, down_ref, out_ref, hidden_ref):
    experts = hidden_ref.shape[0]

    @pl.when(pl.program_id(0) == 0)
    def _():
        rows = normed_ref[...]
        for expert in range(experts):
            gate_proj = jnp.dot(rows, weight_ref[0, expert], preferred_element_type=jnp.float32)
            up_proj = jnp.dot(rows, weight_ref[1, expert], preferred_element_type=jnp.float32)
            activated = gate_proj / (1.0 + jnp.exp(-gate_proj))
            hidden_ref[expert] = (activated * up_proj * combine_ref[expert]).astype(jnp.bfloat16)

    total = jnp.zeros(out_ref.shape[1:], jnp.float32)
    for expert in range(experts):
        total = total + jnp.dot(
            hidden_ref[expert], down_ref[0, expert], preferred_element_type=jnp.float32
        )
    out_ref[0] = total


def expert_project(normed_moe, combine, packed):
    tok_count, model_width = normed_moe.shape
    experts, lanes = packed.shape[1], packed.shape[3]
    units = lanes
    col_blocks = packed.shape[2] // units
    return pl.pallas_call(
        expert_body,
        grid=(col_blocks,),
        in_specs=[
            pl.BlockSpec((tok_count, model_width), lambda c: (0, 0)),
            pl.BlockSpec((experts, tok_count, 1), lambda c: (0, 0, 0)),
            pl.BlockSpec((2, experts, model_width, lanes), lambda c: (0, 0, 0, 0)),
            pl.BlockSpec((1, experts, units, lanes), lambda c: (2, 0, c, 0)),
        ],
        out_specs=pl.BlockSpec((1, tok_count, lanes), lambda c: (c, 0, 0)),
        out_shape=jax.ShapeDtypeStruct((col_blocks, tok_count, lanes), jnp.float32),
        scratch_shapes=[pltpu.VMEM((experts, tok_count, units), jnp.bfloat16)],
        compiler_params=pltpu.CompilerParams(dimension_semantics=("arbitrary",)),
    )(normed_moe, combine, packed, packed)


def shards(
    hidden_in,
    segments,
    prefix_group,
    prefix_cache,
    page_table,
    norm_gain,
    w_query,
    w_keyval,
    w_out,
    moe_gain,
    routes,
    gates,
    w_gate_up,
    w_down,
):
    req_count = lax.axis_size("req")
    whole = gather_in_order(hidden_in, "hid", 1)
    tok_count = whole.shape[0]
    model_width = whole.shape[1]
    segment_row = segments[0]
    prefix_len = prefix_cache.shape[1]
    kv_heads = prefix_cache.shape[2]
    head_dim = prefix_cache.shape[3] // 2
    score_scale = head_dim ** (-0.5)
    normed = rms_scale(whole, norm_gain)
    position = positions_of(segment_row, prefix_len)
    projected = jnp.dot(normed, w_query, preferred_element_type=jnp.float32).reshape(
        tok_count, -1, head_dim
    )
    queries = rotate(projected, position).astype(jnp.bfloat16)
    queries, w_gate_up, w_down = lax.optimization_barrier((queries, w_gate_up, w_down))
    q_groups = queries.shape[1] // kv_heads
    grouped_query = queries.reshape(tok_count, kv_heads, q_groups, head_dim)
    key_value = jnp.dot(normed, w_keyval, preferred_element_type=jnp.float32).reshape(
        tok_count, kv_heads, 2 * head_dim
    )
    key_rows = rotate(key_value[..., :head_dim], position).astype(jnp.bfloat16)
    value_rows = key_value[..., head_dim:].astype(jnp.bfloat16)
    pages = jnp.concatenate([key_rows, value_rows], axis=-1).reshape(
        -1, PAGE, kv_heads, 2 * head_dim
    )
    kv_pages = jnp.zeros_like(pages).at[page_table[0]].set(pages)
    gathered = lax.all_gather(prefix_cache, "req", axis=0, tiled=True)
    attention = attend(
        grouped_query, key_rows, value_rows, segment_row, prefix_group[0],
        gathered.transpose(0, 2, 1, 3),
    )
    share_width = hidden_in.shape[1]
    whole_attention = jnp.concatenate(shifted_copies(attention, "hid"), axis=1)
    whole_w_out = jnp.concatenate(shifted_copies(w_out, "hid"), axis=0)
    projected_out = jnp.dot(whole_attention, whole_w_out, preferred_element_type=jnp.float32)
    middle = (whole.astype(jnp.float32) + projected_out).astype(jnp.bfloat16)
    middle_share = lax.dynamic_slice_in_dim(
        middle, lax.axis_index("hid") * share_width, share_width, 1
    )
    normed_moe = rms_scale(middle, moe_gain)
    local_experts, hidden_units, model_cols = w_down.shape
    lane_width = w_gate_up.shape[-1]
    down_view = (
        w_down.reshape(local_experts, hidden_units, model_cols // lane_width, lane_width)
        .transpose(0, 2, 1, 3)
        .reshape(local_experts, 1, -1, lane_width)
    )
    packed = jnp.concatenate([w_gate_up, down_view], axis=1).transpose(1, 0, 2, 3)
    packed = lax.all_gather(packed, "req", axis=1, tiled=True)
    experts = packed.shape[1]
    expert_ids = jnp.arange(experts, dtype=jnp.int32)
    combine = jnp.sum(
        jnp.where(routes[:, :, None] == expert_ids[None, None, :], gates[:, :, None], 0.0), axis=1
    )
    partial_out = (
        expert_project(normed_moe, combine.T[:, :, None], packed)
        .transpose(1, 0, 2)
        .reshape(tok_count, model_width)
    )
    hid_count = lax.axis_size("hid")
    hid_index = lax.axis_index("hid")
    expert_sum = lax.dynamic_slice_in_dim(partial_out, hid_index * share_width, share_width, 1)
    for shift in range(1, hid_count):
        block = (hid_index + shift) % hid_count
        outgoing = lax.dynamic_slice_in_dim(partial_out, block * share_width, share_width, 1)
        pairs = [(index, (index + shift) % hid_count) for index in range(hid_count)]
        incoming = lax.ppermute(outgoing.astype(jnp.bfloat16), "hid", pairs)
        expert_sum = expert_sum + incoming.astype(jnp.float32)
    hidden_out = (middle_share.astype(jnp.float32) + expert_sum).astype(jnp.bfloat16)
    return (hidden_out, kv_pages)


def solution(mesh):
    in_specs = (
        P("req", "hid"),
        P("req", None),
        P("req", None),
        P("req", None, "hid", None),
        P("req", None),
        P(),
        P(None, "hid"),
        P(None, "hid"),
        P("hid", None),
        P(),
        P("req", None),
        P("req", None),
        P("req", None, None, "hid"),
        P("req", "hid", None),
    )
    out_specs = (P("req", "hid"), P("req", None, "hid", None))
    return jax.shard_map(shards, mesh=mesh, in_specs=in_specs, out_specs=out_specs, check_vma=False)
```

```python
import functools

import jax
import jax.numpy as jnp
from jax import lax
from jax.sharding import PartitionSpec as P
from jax.experimental import pallas as pl
from jax.experimental.pallas import tpu as pltpu

PAGE = 128


EPSILON = 1e-06
THETA = 10000.0


def rms_scale(row_data, gain_row):
    floats = row_data.astype(jnp.float32)
    mean_square = jnp.mean(floats * floats, axis=-1, keepdims=True)
    return (floats * lax.rsqrt(mean_square + EPSILON) * gain_row).astype(jnp.bfloat16)


def rotate(features, positions):
    half_dim = features.shape[-1] // 2
    frequency = THETA ** (-2.0 * jnp.arange(half_dim, dtype=jnp.float32) / features.shape[-1])
    angles = positions.astype(jnp.float32)[:, None] * frequency[None, :]
    cosine = jnp.cos(angles)[:, None, :]
    sine_part = jnp.sin(angles)[:, None, :]
    front_half = features[..., :half_dim]
    second = features[..., half_dim:]
    return jnp.concatenate(
        [front_half * cosine - second * sine_part, second * cosine + front_half * sine_part],
        axis=-1,
    )


def positions_of(segment_row, offset):
    earlier = jnp.sum((segment_row[None, :] < segment_row[:, None]).astype(jnp.int32), axis=1)
    token_index = jnp.arange(segment_row.shape[0], dtype=jnp.int32)
    return token_index - earlier + offset


def slots_of(route_rows, experts):
    flat_routes = route_rows.reshape(-1)
    onehot = (flat_routes[:, None] == jnp.arange(experts, dtype=jnp.int32)[None, :]).astype(
        jnp.int32
    )
    before = jnp.cumsum(onehot, axis=0) - onehot
    return (flat_routes, jnp.sum(before * onehot, axis=1))


def expert_rows(received, gate_up, down_proj):
    local_experts = down_proj.shape[0]
    slot_count = received.shape[1]
    model_width = received.shape[2]
    grouped = received.reshape(-1, local_experts, slot_count, model_width)
    gate_proj = jnp.einsum(
        "recd,edf->recf", grouped, gate_up[:, 0], preferred_element_type=jnp.float32
    )
    up_proj = jnp.einsum(
        "recd,edf->recf", grouped, gate_up[:, 1], preferred_element_type=jnp.float32
    )
    hidden = (jax.nn.silu(gate_proj) * up_proj).astype(jnp.bfloat16)
    produced = jnp.einsum("recf,efd->recd", hidden, down_proj, preferred_element_type=jnp.float32)
    return produced.reshape(-1, slot_count, model_width)


def shifted_copies(block, axis_name):
    count = lax.axis_size(axis_name)
    copies = [block]
    for shift in range(1, count):
        pairs = [(index, (index + shift) % count) for index in range(count)]
        copies.append(lax.ppermute(block, axis_name, pairs))
    return copies


def gather_in_order(block, axis_name, axis):
    count = lax.axis_size(axis_name)
    copies = jnp.stack(shifted_copies(block, axis_name))
    order = (lax.axis_index(axis_name) - jnp.arange(count, dtype=jnp.int32)) % count
    picked = jnp.take(copies, order, axis=0)
    return jnp.concatenate([picked[index] for index in range(count)], axis=axis)


def attention_body(group_ref, bound_ref, q_ref, k_ref, v_ref, segq_ref, segk_ref, prefix_ref, out_ref):
    block = pl.program_id(1)
    seg = pl.program_id(2)
    seg_count = pl.num_programs(2)
    rows = q_ref.shape[2]
    tokens = k_ref.shape[1]
    head_dim = q_ref.shape[3]

    @pl.when(seg == 0)
    def _():
        out_ref[...] = jnp.zeros_like(out_ref)

    first = bound_ref[seg]
    last = bound_ref[seg + seg_count]
    active = (first < (block + 1) * rows) & (last > block * rows)

    @pl.when(active)
    def _():
        seg_q = segq_ref[...]
        seg_k = segk_ref[...]
        t_idx = block * rows + lax.broadcasted_iota(jnp.int32, (rows, tokens), 0)
        u_idx = lax.broadcasted_iota(jnp.int32, (rows, tokens), 1)
        visible = (seg_q == seg_k) & (u_idx <= t_idx)
        keys = k_ref[0]
        values = v_ref[0]
        prefix = prefix_ref[0, 0]
        prefix_keys = prefix[:, :head_dim]
        prefix_values = prefix[:, head_dim:]
        scale = head_dim ** (-0.5)
        mine = seg_q == seg
        contract = (((1,), (1,)), ((), ()))
        for group in range(q_ref.shape[1]):
            query = q_ref[0, group]
            local = lax.dot_general(query, keys, contract, preferred_element_type=jnp.float32) * scale
            local = jnp.where(visible, local, -jnp.inf)
            cached = (
                lax.dot_general(query, prefix_keys, contract, preferred_element_type=jnp.float32)
                * scale
            )
            top = jnp.maximum(
                jnp.max(local, axis=1, keepdims=True), jnp.max(cached, axis=1, keepdims=True)
            )
            local_num = jnp.exp(local - top)
            cached_num = jnp.exp(cached - top)
            total = jnp.sum(local_num, axis=1, keepdims=True) + jnp.sum(
                cached_num, axis=1, keepdims=True
            )
            summed = jnp.dot(
                local_num.astype(jnp.bfloat16), values, preferred_element_type=jnp.float32
            ) + jnp.dot(
                cached_num.astype(jnp.bfloat16), prefix_values, preferred_element_type=jnp.float32
            )
            out_ref[0, group] = jnp.where(mine, summed / total, out_ref[0, group])


def attend(grouped_query, key_rows, value_rows, segment_row, group_row, prefix_heads, interpret=False):
    tok_count, kv_heads, q_groups, head_dim = grouped_query.shape
    seg_count = group_row.shape[0]
    prefix_len = prefix_heads.shape[2]
    rows = min(128, tok_count)
    labels = jnp.arange(seg_count, dtype=jnp.int32)
    first = jnp.sum((segment_row[None, :] < labels[:, None]).astype(jnp.int32), axis=1)
    last = jnp.sum((segment_row[None, :] <= labels[:, None]).astype(jnp.int32), axis=1)
    bounds = jnp.concatenate([first, last])
    query_heads = grouped_query.transpose(1, 2, 0, 3)
    key_heads = key_rows.transpose(1, 0, 2)
    value_heads = value_rows.transpose(1, 0, 2)
    seg_col = segment_row.reshape(tok_count, 1)
    seg_line = segment_row.reshape(1, tok_count)
    grid_spec = pltpu.PrefetchScalarGridSpec(
        num_scalar_prefetch=2,
        grid=(kv_heads, tok_count // rows, seg_count),
        in_specs=[
            pl.BlockSpec((1, q_groups, rows, head_dim), lambda h, b, s, gr, bd: (h, 0, b, 0)),
            pl.BlockSpec((1, tok_count, head_dim), lambda h, b, s, gr, bd: (h, 0, 0)),
            pl.BlockSpec((1, tok_count, head_dim), lambda h, b, s, gr, bd: (h, 0, 0)),
            pl.BlockSpec((rows, 1), lambda h, b, s, gr, bd: (b, 0)),
            pl.BlockSpec((1, tok_count), lambda h, b, s, gr, bd: (0, 0)),
            pl.BlockSpec(
                (1, 1, prefix_len, 2 * head_dim), lambda h, b, s, gr, bd: (gr[s], h, 0, 0)
            ),
        ],
        out_specs=pl.BlockSpec((1, q_groups, rows, head_dim), lambda h, b, s, gr, bd: (h, 0, b, 0)),
    )
    out = pl.pallas_call(
        attention_body,
        grid_spec=grid_spec,
        out_shape=jax.ShapeDtypeStruct((kv_heads, q_groups, tok_count, head_dim), jnp.float32),
        compiler_params=pltpu.CompilerParams(
            dimension_semantics=("arbitrary", "arbitrary", "arbitrary")
        ),
        interpret=interpret,
    )(group_row, bounds, query_heads, key_heads, value_heads, seg_col, seg_line, prefix_heads)
    return out.transpose(2, 0, 1, 3).reshape(tok_count, -1).astype(jnp.bfloat16)


def expert_body(normed_ref, combine_ref, weight_ref, down_ref, out_ref):
    @pl.when(pl.program_id(0) == 0)
    def _():
        out_ref[...] = jnp.zeros_like(out_ref)

    rows = normed_ref[...]
    gate_proj = jnp.dot(rows, weight_ref[0, 0], preferred_element_type=jnp.float32)
    up_proj = jnp.dot(rows, weight_ref[1, 0], preferred_element_type=jnp.float32)
    activated = gate_proj / (1.0 + jnp.exp(-gate_proj))
    hidden = (activated * up_proj * combine_ref[0]).astype(jnp.bfloat16)
    units = hidden.shape[1]
    for col in range(out_ref.shape[0]):
        out_ref[col] += jnp.dot(
            hidden, down_ref[0, 0, col * units : (col + 1) * units, :],
            preferred_element_type=jnp.float32,
        )


def expert_project(normed_moe, combine, packed):
    tok_count, model_width = normed_moe.shape
    experts, rows_per, lanes = packed.shape[1], packed.shape[2], packed.shape[3]
    col_blocks = rows_per // lanes
    return pl.pallas_call(
        expert_body,
        grid=(experts,),
        in_specs=[
            pl.BlockSpec((tok_count, model_width), lambda e: (0, 0)),
            pl.BlockSpec((1, tok_count, 1), lambda e: (e, 0, 0)),
            pl.BlockSpec((2, 1, model_width, lanes), lambda e: (0, e, 0, 0)),
            pl.BlockSpec((1, 1, rows_per, lanes), lambda e: (2, e, 0, 0)),
        ],
        out_specs=pl.BlockSpec((col_blocks, tok_count, lanes), lambda e: (0, 0, 0)),
        out_shape=jax.ShapeDtypeStruct((col_blocks, tok_count, lanes), jnp.float32),
        compiler_params=pltpu.CompilerParams(dimension_semantics=("arbitrary",)),
    )(normed_moe, combine, packed, packed)


def shards(
    hidden_in,
    segments,
    prefix_group,
    prefix_cache,
    page_table,
    norm_gain,
    w_query,
    w_keyval,
    w_out,
    moe_gain,
    routes,
    gates,
    w_gate_up,
    w_down,
):
    req_count = lax.axis_size("req")
    whole = gather_in_order(hidden_in, "hid", 1)
    tok_count = whole.shape[0]
    model_width = whole.shape[1]
    segment_row = segments[0]
    prefix_len = prefix_cache.shape[1]
    kv_heads = prefix_cache.shape[2]
    head_dim = prefix_cache.shape[3] // 2
    score_scale = head_dim ** (-0.5)
    normed = rms_scale(whole, norm_gain)
    position = positions_of(segment_row, prefix_len)
    projected = jnp.dot(normed, w_query, preferred_element_type=jnp.float32).reshape(
        tok_count, -1, head_dim
    )
    queries = rotate(projected, position).astype(jnp.bfloat16)
    queries, w_gate_up, w_down = lax.optimization_barrier((queries, w_gate_up, w_down))
    q_groups = queries.shape[1] // kv_heads
    grouped_query = queries.reshape(tok_count, kv_heads, q_groups, head_dim)
    key_value = jnp.dot(normed, w_keyval, preferred_element_type=jnp.float32).reshape(
        tok_count, kv_heads, 2 * head_dim
    )
    key_rows = rotate(key_value[..., :head_dim], position).astype(jnp.bfloat16)
    value_rows = key_value[..., head_dim:].astype(jnp.bfloat16)
    pages = jnp.concatenate([key_rows, value_rows], axis=-1).reshape(
        -1, PAGE, kv_heads, 2 * head_dim
    )
    kv_pages = jnp.zeros_like(pages).at[page_table[0]].set(pages)
    gathered = lax.all_gather(prefix_cache, "req", axis=0, tiled=True)
    attention = attend(
        grouped_query, key_rows, value_rows, segment_row, prefix_group[0],
        gathered.transpose(0, 2, 1, 3),
    )
    share_width = hidden_in.shape[1]
    whole_attention = jnp.concatenate(shifted_copies(attention, "hid"), axis=1)
    whole_w_out = jnp.concatenate(shifted_copies(w_out, "hid"), axis=0)
    projected_out = jnp.dot(whole_attention, whole_w_out, preferred_element_type=jnp.float32)
    middle = (whole.astype(jnp.float32) + projected_out).astype(jnp.bfloat16)
    middle_share = lax.dynamic_slice_in_dim(
        middle, lax.axis_index("hid") * share_width, share_width, 1
    )
    normed_moe = rms_scale(middle, moe_gain)
    local_experts, hidden_units, model_cols = w_down.shape
    lane_width = w_gate_up.shape[-1]
    down_view = (
        w_down.reshape(local_experts, hidden_units, model_cols // lane_width, lane_width)
        .transpose(0, 2, 1, 3)
        .reshape(local_experts, 1, -1, lane_width)
    )
    packed = jnp.concatenate([w_gate_up, down_view], axis=1).transpose(1, 0, 2, 3)
    packed = lax.all_gather(packed, "req", axis=1, tiled=True)
    experts = packed.shape[1]
    expert_ids = jnp.arange(experts, dtype=jnp.int32)
    combine = jnp.sum(
        jnp.where(routes[:, :, None] == expert_ids[None, None, :], gates[:, :, None], 0.0), axis=1
    )
    partial_out = (
        expert_project(normed_moe, combine.T[:, :, None], packed)
        .transpose(1, 0, 2)
        .reshape(tok_count, model_width)
    )
    hid_count = lax.axis_size("hid")
    hid_index = lax.axis_index("hid")
    expert_sum = lax.dynamic_slice_in_dim(partial_out, hid_index * share_width, share_width, 1)
    for shift in range(1, hid_count):
        block = (hid_index + shift) % hid_count
        outgoing = lax.dynamic_slice_in_dim(partial_out, block * share_width, share_width, 1)
        pairs = [(index, (index + shift) % hid_count) for index in range(hid_count)]
        incoming = lax.ppermute(outgoing.astype(jnp.bfloat16), "hid", pairs)
        expert_sum = expert_sum + incoming.astype(jnp.float32)
    hidden_out = (middle_share.astype(jnp.float32) + expert_sum).astype(jnp.bfloat16)
    return (hidden_out, kv_pages)


def solution(mesh):
    in_specs = (
        P("req", "hid"),
        P("req", None),
        P("req", None),
        P("req", None, "hid", None),
        P("req", None),
        P(),
        P(None, "hid"),
        P(None, "hid"),
        P("hid", None),
        P(),
        P("req", None),
        P("req", None),
        P("req", None, None, "hid"),
        P("req", "hid", None),
    )
    out_specs = (P("req", "hid"), P("req", None, "hid", None))
    return jax.shard_map(shards, mesh=mesh, in_specs=in_specs, out_specs=out_specs, check_vma=False)
```

```python
import functools

import jax
import jax.numpy as jnp
from jax import lax
from jax.sharding import PartitionSpec as P
from jax.experimental import pallas as pl
from jax.experimental.pallas import tpu as pltpu

PAGE = 128


EPSILON = 1e-06
THETA = 10000.0


def rms_scale(row_data, gain_row):
    floats = row_data.astype(jnp.float32)
    mean_square = jnp.mean(floats * floats, axis=-1, keepdims=True)
    return (floats * lax.rsqrt(mean_square + EPSILON) * gain_row).astype(jnp.bfloat16)


def rotate(features, positions):
    half_dim = features.shape[-1] // 2
    frequency = THETA ** (-2.0 * jnp.arange(half_dim, dtype=jnp.float32) / features.shape[-1])
    angles = positions.astype(jnp.float32)[:, None] * frequency[None, :]
    cosine = jnp.cos(angles)[:, None, :]
    sine_part = jnp.sin(angles)[:, None, :]
    front_half = features[..., :half_dim]
    second = features[..., half_dim:]
    return jnp.concatenate(
        [front_half * cosine - second * sine_part, second * cosine + front_half * sine_part],
        axis=-1,
    )


def positions_of(segment_row, offset):
    earlier = jnp.sum((segment_row[None, :] < segment_row[:, None]).astype(jnp.int32), axis=1)
    token_index = jnp.arange(segment_row.shape[0], dtype=jnp.int32)
    return token_index - earlier + offset


def slots_of(route_rows, experts):
    flat_routes = route_rows.reshape(-1)
    onehot = (flat_routes[:, None] == jnp.arange(experts, dtype=jnp.int32)[None, :]).astype(
        jnp.int32
    )
    before = jnp.cumsum(onehot, axis=0) - onehot
    return (flat_routes, jnp.sum(before * onehot, axis=1))


def expert_rows(received, gate_up, down_proj):
    local_experts = down_proj.shape[0]
    slot_count = received.shape[1]
    model_width = received.shape[2]
    grouped = received.reshape(-1, local_experts, slot_count, model_width)
    gate_proj = jnp.einsum(
        "recd,edf->recf", grouped, gate_up[:, 0], preferred_element_type=jnp.float32
    )
    up_proj = jnp.einsum(
        "recd,edf->recf", grouped, gate_up[:, 1], preferred_element_type=jnp.float32
    )
    hidden = (jax.nn.silu(gate_proj) * up_proj).astype(jnp.bfloat16)
    produced = jnp.einsum("recf,efd->recd", hidden, down_proj, preferred_element_type=jnp.float32)
    return produced.reshape(-1, slot_count, model_width)


def shifted_copies(block, axis_name):
    count = lax.axis_size(axis_name)
    copies = [block]
    for shift in range(1, count):
        pairs = [(index, (index + shift) % count) for index in range(count)]
        copies.append(lax.ppermute(block, axis_name, pairs))
    return copies


def gather_in_order(block, axis_name, axis):
    count = lax.axis_size(axis_name)
    copies = jnp.stack(shifted_copies(block, axis_name))
    order = (lax.axis_index(axis_name) - jnp.arange(count, dtype=jnp.int32)) % count
    picked = jnp.take(copies, order, axis=0)
    return jnp.concatenate([picked[index] for index in range(count)], axis=axis)


def attention_body(group_ref, bound_ref, q_ref, k_ref, v_ref, segq_ref, segk_ref, prefix_ref, out_ref):
    block = pl.program_id(1)
    seg = pl.program_id(2)
    seg_count = pl.num_programs(2)
    rows = q_ref.shape[2]
    tokens = k_ref.shape[1]
    head_dim = q_ref.shape[3]

    @pl.when(seg == 0)
    def _():
        out_ref[...] = jnp.zeros_like(out_ref)

    first = bound_ref[seg]
    last = bound_ref[seg + seg_count]
    active = (first < (block + 1) * rows) & (last > block * rows)

    @pl.when(active)
    def _():
        seg_q = segq_ref[...]
        seg_k = segk_ref[...]
        t_idx = block * rows + lax.broadcasted_iota(jnp.int32, (rows, tokens), 0)
        u_idx = lax.broadcasted_iota(jnp.int32, (rows, tokens), 1)
        visible = (seg_q == seg_k) & (u_idx <= t_idx)
        keys = k_ref[0]
        values = v_ref[0]
        prefix = prefix_ref[0, 0]
        prefix_keys = prefix[:, :head_dim]
        prefix_values = prefix[:, head_dim:]
        scale = head_dim ** (-0.5)
        mine = seg_q == seg
        contract = (((1,), (1,)), ((), ()))
        for group in range(q_ref.shape[1]):
            query = q_ref[0, group]
            local = lax.dot_general(query, keys, contract, preferred_element_type=jnp.float32) * scale
            local = jnp.where(visible, local, -jnp.inf)
            cached = (
                lax.dot_general(query, prefix_keys, contract, preferred_element_type=jnp.float32)
                * scale
            )
            top = jnp.maximum(
                jnp.max(local, axis=1, keepdims=True), jnp.max(cached, axis=1, keepdims=True)
            )
            local_num = jnp.exp(local - top)
            cached_num = jnp.exp(cached - top)
            total = jnp.sum(local_num, axis=1, keepdims=True) + jnp.sum(
                cached_num, axis=1, keepdims=True
            )
            summed = jnp.dot(
                local_num.astype(jnp.bfloat16), values, preferred_element_type=jnp.float32
            ) + jnp.dot(
                cached_num.astype(jnp.bfloat16), prefix_values, preferred_element_type=jnp.float32
            )
            out_ref[0, group] = jnp.where(mine, summed / total, out_ref[0, group])


def attend(grouped_query, key_rows, value_rows, segment_row, group_row, prefix_heads, interpret=False):
    tok_count, kv_heads, q_groups, head_dim = grouped_query.shape
    seg_count = group_row.shape[0]
    prefix_len = prefix_heads.shape[2]
    rows = min(128, tok_count)
    labels = jnp.arange(seg_count, dtype=jnp.int32)
    first = jnp.sum((segment_row[None, :] < labels[:, None]).astype(jnp.int32), axis=1)
    last = jnp.sum((segment_row[None, :] <= labels[:, None]).astype(jnp.int32), axis=1)
    bounds = jnp.concatenate([first, last])
    query_heads = grouped_query.transpose(1, 2, 0, 3)
    key_heads = key_rows.transpose(1, 0, 2)
    value_heads = value_rows.transpose(1, 0, 2)
    seg_col = segment_row.reshape(tok_count, 1)
    seg_line = segment_row.reshape(1, tok_count)
    grid_spec = pltpu.PrefetchScalarGridSpec(
        num_scalar_prefetch=2,
        grid=(kv_heads, tok_count // rows, seg_count),
        in_specs=[
            pl.BlockSpec((1, q_groups, rows, head_dim), lambda h, b, s, gr, bd: (h, 0, b, 0)),
            pl.BlockSpec((1, tok_count, head_dim), lambda h, b, s, gr, bd: (h, 0, 0)),
            pl.BlockSpec((1, tok_count, head_dim), lambda h, b, s, gr, bd: (h, 0, 0)),
            pl.BlockSpec((rows, 1), lambda h, b, s, gr, bd: (b, 0)),
            pl.BlockSpec((1, tok_count), lambda h, b, s, gr, bd: (0, 0)),
            pl.BlockSpec(
                (1, 1, prefix_len, 2 * head_dim), lambda h, b, s, gr, bd: (gr[s], h, 0, 0)
            ),
        ],
        out_specs=pl.BlockSpec((1, q_groups, rows, head_dim), lambda h, b, s, gr, bd: (h, 0, b, 0)),
    )
    out = pl.pallas_call(
        attention_body,
        grid_spec=grid_spec,
        out_shape=jax.ShapeDtypeStruct((kv_heads, q_groups, tok_count, head_dim), jnp.float32),
        compiler_params=pltpu.CompilerParams(
            dimension_semantics=("arbitrary", "arbitrary", "arbitrary")
        ),
        interpret=interpret,
    )(group_row, bounds, query_heads, key_heads, value_heads, seg_col, seg_line, prefix_heads)
    return out.transpose(2, 0, 1, 3).reshape(tok_count, -1).astype(jnp.bfloat16)


def expert_body(normed_ref, combine_ref, weight_ref, down_ref, out_ref, hidden_ref):
    experts = hidden_ref.shape[0]

    @pl.when(pl.program_id(0) == 0)
    def _():
        rows = normed_ref[...]
        for expert in range(experts):
            gate_proj = jnp.dot(rows, weight_ref[0, expert], preferred_element_type=jnp.float32)
            up_proj = jnp.dot(rows, weight_ref[1, expert], preferred_element_type=jnp.float32)
            activated = gate_proj / (1.0 + jnp.exp(-gate_proj))
            hidden_ref[expert] = (activated * up_proj * combine_ref[expert]).astype(jnp.bfloat16)

    total = jnp.zeros(out_ref.shape[1:], jnp.float32)
    for expert in range(experts):
        total = total + jnp.dot(
            hidden_ref[expert], down_ref[0, expert], preferred_element_type=jnp.float32
        )
    out_ref[0] = total


def expert_project(normed_moe, combine, packed):
    tok_count, model_width = normed_moe.shape
    experts, lanes = packed.shape[1], packed.shape[3]
    units = lanes
    col_blocks = packed.shape[2] // units
    return pl.pallas_call(
        expert_body,
        grid=(col_blocks,),
        in_specs=[
            pl.BlockSpec((tok_count, model_width), lambda c: (0, 0)),
            pl.BlockSpec((experts, tok_count, 1), lambda c: (0, 0, 0)),
            pl.BlockSpec((2, experts, model_width, lanes), lambda c: (0, 0, 0, 0)),
            pl.BlockSpec((1, experts, units, lanes), lambda c: (2, 0, c, 0)),
        ],
        out_specs=pl.BlockSpec((1, tok_count, lanes), lambda c: (c, 0, 0)),
        out_shape=jax.ShapeDtypeStruct((col_blocks, tok_count, lanes), jnp.float32),
        scratch_shapes=[pltpu.VMEM((experts, tok_count, units), jnp.bfloat16)],
        compiler_params=pltpu.CompilerParams(dimension_semantics=("arbitrary",)),
    )(normed_moe, combine, packed, packed)


def shards(
    hidden_in,
    segments,
    prefix_group,
    prefix_cache,
    page_table,
    norm_gain,
    w_query,
    w_keyval,
    w_out,
    moe_gain,
    routes,
    gates,
    w_gate_up,
    w_down,
):
    req_count = lax.axis_size("req")
    whole = gather_in_order(hidden_in, "hid", 1)
    tok_count = whole.shape[0]
    model_width = whole.shape[1]
    segment_row = segments[0]
    prefix_len = prefix_cache.shape[1]
    kv_heads = prefix_cache.shape[2]
    head_dim = prefix_cache.shape[3] // 2
    score_scale = head_dim ** (-0.5)
    normed = rms_scale(whole, norm_gain)
    position = positions_of(segment_row, prefix_len)
    projected = jnp.dot(normed, w_query, preferred_element_type=jnp.float32).reshape(
        tok_count, -1, head_dim
    )
    queries = rotate(projected, position).astype(jnp.bfloat16)
    queries, w_gate_up, w_down = lax.optimization_barrier((queries, w_gate_up, w_down))
    q_groups = queries.shape[1] // kv_heads
    grouped_query = queries.reshape(tok_count, kv_heads, q_groups, head_dim)
    key_value = jnp.dot(normed, w_keyval, preferred_element_type=jnp.float32).reshape(
        tok_count, kv_heads, 2 * head_dim
    )
    key_rows = rotate(key_value[..., :head_dim], position).astype(jnp.bfloat16)
    value_rows = key_value[..., head_dim:].astype(jnp.bfloat16)
    pages = jnp.concatenate([key_rows, value_rows], axis=-1).reshape(
        -1, PAGE, kv_heads, 2 * head_dim
    )
    kv_pages = jnp.zeros_like(pages).at[page_table[0]].set(pages)
    gathered = lax.all_gather(prefix_cache, "req", axis=0, tiled=True)
    attention = attend(
        grouped_query, key_rows, value_rows, segment_row, prefix_group[0],
        gathered.transpose(0, 2, 1, 3),
    )
    share_width = hidden_in.shape[1]
    whole_attention = jnp.concatenate(shifted_copies(attention, "hid"), axis=1)
    whole_w_out = jnp.concatenate(shifted_copies(w_out, "hid"), axis=0)
    projected_out = jnp.dot(whole_attention, whole_w_out, preferred_element_type=jnp.float32)
    middle = (whole.astype(jnp.float32) + projected_out).astype(jnp.bfloat16)
    middle_share = lax.dynamic_slice_in_dim(
        middle, lax.axis_index("hid") * share_width, share_width, 1
    )
    normed_moe = rms_scale(middle, moe_gain)
    local_experts, hidden_units, model_cols = w_down.shape
    lane_width = w_gate_up.shape[-1]
    down_view = (
        w_down.reshape(local_experts, hidden_units, model_cols // lane_width, lane_width)
        .transpose(0, 2, 1, 3)
        .reshape(local_experts, 1, -1, lane_width)
    )
    packed = jnp.concatenate([w_gate_up, down_view], axis=1).transpose(1, 0, 2, 3)
    packed = lax.all_gather(packed, "req", axis=1, tiled=True)
    experts = packed.shape[1]
    expert_ids = jnp.arange(experts, dtype=jnp.int32)
    combine = jnp.sum(
        jnp.where(routes[:, :, None] == expert_ids[None, None, :], gates[:, :, None], 0.0), axis=1
    )
    partial_out = (
        expert_project(normed_moe, combine.T[:, :, None], packed)
        .transpose(1, 0, 2)
        .reshape(tok_count, model_width)
    )
    hid_count = lax.axis_size("hid")
    pieces = partial_out.astype(jnp.bfloat16).reshape(tok_count, hid_count, share_width)
    received = lax.all_to_all(pieces, "hid", split_axis=1, concat_axis=1, tiled=True)
    expert_sum = jnp.sum(received.astype(jnp.float32), axis=1)
    hidden_out = (middle_share.astype(jnp.float32) + expert_sum).astype(jnp.bfloat16)
    return (hidden_out, kv_pages)


def solution(mesh):
    in_specs = (
        P("req", "hid"),
        P("req", None),
        P("req", None),
        P("req", None, "hid", None),
        P("req", None),
        P(),
        P(None, "hid"),
        P(None, "hid"),
        P("hid", None),
        P(),
        P("req", None),
        P("req", None),
        P("req", None, None, "hid"),
        P("req", "hid", None),
    )
    out_specs = (P("req", "hid"), P("req", None, "hid", None))
    return jax.shard_map(shards, mesh=mesh, in_specs=in_specs, out_specs=out_specs, check_vma=False)
```

```python
import functools

import jax
import jax.numpy as jnp
from jax import lax
from jax.sharding import PartitionSpec as P
from jax.experimental import pallas as pl
from jax.experimental.pallas import tpu as pltpu

PAGE = 128


EPSILON = 1e-06
THETA = 10000.0


def rms_scale(row_data, gain_row):
    floats = row_data.astype(jnp.float32)
    mean_square = jnp.mean(floats * floats, axis=-1, keepdims=True)
    return (floats * lax.rsqrt(mean_square + EPSILON) * gain_row).astype(jnp.bfloat16)


def rotate(features, positions):
    half_dim = features.shape[-1] // 2
    frequency = THETA ** (-2.0 * jnp.arange(half_dim, dtype=jnp.float32) / features.shape[-1])
    angles = positions.astype(jnp.float32)[:, None] * frequency[None, :]
    cosine = jnp.cos(angles)[:, None, :]
    sine_part = jnp.sin(angles)[:, None, :]
    front_half = features[..., :half_dim]
    second = features[..., half_dim:]
    return jnp.concatenate(
        [front_half * cosine - second * sine_part, second * cosine + front_half * sine_part],
        axis=-1,
    )


def positions_of(segment_row, offset):
    earlier = jnp.sum((segment_row[None, :] < segment_row[:, None]).astype(jnp.int32), axis=1)
    token_index = jnp.arange(segment_row.shape[0], dtype=jnp.int32)
    return token_index - earlier + offset


def slots_of(route_rows, experts):
    flat_routes = route_rows.reshape(-1)
    onehot = (flat_routes[:, None] == jnp.arange(experts, dtype=jnp.int32)[None, :]).astype(
        jnp.int32
    )
    before = jnp.cumsum(onehot, axis=0) - onehot
    return (flat_routes, jnp.sum(before * onehot, axis=1))


def expert_rows(received, gate_up, down_proj):
    local_experts = down_proj.shape[0]
    slot_count = received.shape[1]
    model_width = received.shape[2]
    grouped = received.reshape(-1, local_experts, slot_count, model_width)
    gate_proj = jnp.einsum(
        "recd,edf->recf", grouped, gate_up[:, 0], preferred_element_type=jnp.float32
    )
    up_proj = jnp.einsum(
        "recd,edf->recf", grouped, gate_up[:, 1], preferred_element_type=jnp.float32
    )
    hidden = (jax.nn.silu(gate_proj) * up_proj).astype(jnp.bfloat16)
    produced = jnp.einsum("recf,efd->recd", hidden, down_proj, preferred_element_type=jnp.float32)
    return produced.reshape(-1, slot_count, model_width)


def shifted_copies(block, axis_name):
    count = lax.axis_size(axis_name)
    copies = [block]
    for shift in range(1, count):
        pairs = [(index, (index + shift) % count) for index in range(count)]
        copies.append(lax.ppermute(block, axis_name, pairs))
    return copies


def gather_in_order(block, axis_name, axis):
    count = lax.axis_size(axis_name)
    copies = jnp.stack(shifted_copies(block, axis_name))
    order = (lax.axis_index(axis_name) - jnp.arange(count, dtype=jnp.int32)) % count
    picked = jnp.take(copies, order, axis=0)
    return jnp.concatenate([picked[index] for index in range(count)], axis=axis)


def attention_body(group_ref, bound_ref, q_ref, k_ref, v_ref, segq_ref, segk_ref, prefix_ref, out_ref):
    block = pl.program_id(1)
    seg = pl.program_id(2)
    seg_count = pl.num_programs(2)
    rows = q_ref.shape[2]
    tokens = k_ref.shape[1]
    head_dim = q_ref.shape[3]

    @pl.when(seg == 0)
    def _():
        out_ref[...] = jnp.zeros_like(out_ref)

    first = bound_ref[seg]
    last = bound_ref[seg + seg_count]
    active = (first < (block + 1) * rows) & (last > block * rows)

    @pl.when(active)
    def _():
        seg_q = segq_ref[...]
        seg_k = segk_ref[...]
        t_idx = block * rows + lax.broadcasted_iota(jnp.int32, (rows, tokens), 0)
        u_idx = lax.broadcasted_iota(jnp.int32, (rows, tokens), 1)
        visible = (seg_q == seg_k) & (u_idx <= t_idx)
        keys = k_ref[0]
        values = v_ref[0]
        prefix = prefix_ref[0, 0]
        prefix_keys = prefix[:, :head_dim]
        prefix_values = prefix[:, head_dim:]
        scale = head_dim ** (-0.5)
        mine = seg_q == seg
        contract = (((1,), (1,)), ((), ()))
        for group in range(q_ref.shape[1]):
            query = q_ref[0, group]
            local = lax.dot_general(query, keys, contract, preferred_element_type=jnp.float32) * scale
            local = jnp.where(visible, local, -jnp.inf)
            cached = (
                lax.dot_general(query, prefix_keys, contract, preferred_element_type=jnp.float32)
                * scale
            )
            top = jnp.maximum(
                jnp.max(local, axis=1, keepdims=True), jnp.max(cached, axis=1, keepdims=True)
            )
            local_num = jnp.exp(local - top)
            cached_num = jnp.exp(cached - top)
            total = jnp.sum(local_num, axis=1, keepdims=True) + jnp.sum(
                cached_num, axis=1, keepdims=True
            )
            summed = jnp.dot(
                local_num.astype(jnp.bfloat16), values, preferred_element_type=jnp.float32
            ) + jnp.dot(
                cached_num.astype(jnp.bfloat16), prefix_values, preferred_element_type=jnp.float32
            )
            out_ref[0, group] = jnp.where(mine, summed / total, out_ref[0, group])


def attend(grouped_query, key_rows, value_rows, segment_row, group_row, prefix_heads, interpret=False):
    tok_count, kv_heads, q_groups, head_dim = grouped_query.shape
    seg_count = group_row.shape[0]
    prefix_len = prefix_heads.shape[2]
    rows = min(128, tok_count)
    labels = jnp.arange(seg_count, dtype=jnp.int32)
    first = jnp.sum((segment_row[None, :] < labels[:, None]).astype(jnp.int32), axis=1)
    last = jnp.sum((segment_row[None, :] <= labels[:, None]).astype(jnp.int32), axis=1)
    bounds = jnp.concatenate([first, last])
    query_heads = grouped_query.transpose(1, 2, 0, 3)
    key_heads = key_rows.transpose(1, 0, 2)
    value_heads = value_rows.transpose(1, 0, 2)
    seg_col = segment_row.reshape(tok_count, 1)
    seg_line = segment_row.reshape(1, tok_count)
    grid_spec = pltpu.PrefetchScalarGridSpec(
        num_scalar_prefetch=2,
        grid=(kv_heads, tok_count // rows, seg_count),
        in_specs=[
            pl.BlockSpec((1, q_groups, rows, head_dim), lambda h, b, s, gr, bd: (h, 0, b, 0)),
            pl.BlockSpec((1, tok_count, head_dim), lambda h, b, s, gr, bd: (h, 0, 0)),
            pl.BlockSpec((1, tok_count, head_dim), lambda h, b, s, gr, bd: (h, 0, 0)),
            pl.BlockSpec((rows, 1), lambda h, b, s, gr, bd: (b, 0)),
            pl.BlockSpec((1, tok_count), lambda h, b, s, gr, bd: (0, 0)),
            pl.BlockSpec(
                (1, 1, prefix_len, 2 * head_dim), lambda h, b, s, gr, bd: (gr[s], h, 0, 0)
            ),
        ],
        out_specs=pl.BlockSpec((1, q_groups, rows, head_dim), lambda h, b, s, gr, bd: (h, 0, b, 0)),
    )
    out = pl.pallas_call(
        attention_body,
        grid_spec=grid_spec,
        out_shape=jax.ShapeDtypeStruct((kv_heads, q_groups, tok_count, head_dim), jnp.float32),
        compiler_params=pltpu.CompilerParams(
            dimension_semantics=("arbitrary", "arbitrary", "arbitrary")
        ),
        interpret=interpret,
    )(group_row, bounds, query_heads, key_heads, value_heads, seg_col, seg_line, prefix_heads)
    return out.transpose(2, 0, 1, 3).reshape(tok_count, -1).astype(jnp.bfloat16)


def expert_body(normed_ref, combine_ref, weight_ref, down_ref, out_ref, hidden_ref):
    experts = hidden_ref.shape[0]

    @pl.when(pl.program_id(0) == 0)
    def _():
        rows = normed_ref[...]
        for expert in range(experts):
            gate_proj = jnp.dot(rows, weight_ref[0, expert], preferred_element_type=jnp.float32)
            up_proj = jnp.dot(rows, weight_ref[1, expert], preferred_element_type=jnp.float32)
            activated = gate_proj / (1.0 + jnp.exp(-gate_proj))
            hidden_ref[expert] = (activated * up_proj * combine_ref[expert]).astype(jnp.bfloat16)

    units = hidden_ref.shape[2]
    for col in range(out_ref.shape[0]):
        total = jnp.zeros(out_ref.shape[1:], jnp.float32)
        for expert in range(experts):
            total = total + jnp.dot(
                hidden_ref[expert],
                down_ref[0, expert, col * units : (col + 1) * units, :],
                preferred_element_type=jnp.float32,
            )
        out_ref[col] = total


def expert_project(normed_moe, combine, packed):
    tok_count, model_width = normed_moe.shape
    experts, lanes = packed.shape[1], packed.shape[3]
    units = lanes
    col_blocks = packed.shape[2] // units
    per_step = 4 if col_blocks % 4 == 0 else 1
    return pl.pallas_call(
        expert_body,
        grid=(col_blocks // per_step,),
        in_specs=[
            pl.BlockSpec((tok_count, model_width), lambda c: (0, 0)),
            pl.BlockSpec((experts, tok_count, 1), lambda c: (0, 0, 0)),
            pl.BlockSpec((2, experts, model_width, lanes), lambda c: (0, 0, 0, 0)),
            pl.BlockSpec((1, experts, per_step * units, lanes), lambda c: (2, 0, c, 0)),
        ],
        out_specs=pl.BlockSpec((per_step, tok_count, lanes), lambda c: (c, 0, 0)),
        out_shape=jax.ShapeDtypeStruct((col_blocks, tok_count, lanes), jnp.float32),
        scratch_shapes=[pltpu.VMEM((experts, tok_count, units), jnp.bfloat16)],
        compiler_params=pltpu.CompilerParams(dimension_semantics=("arbitrary",)),
    )(normed_moe, combine, packed, packed)


def shards(
    hidden_in,
    segments,
    prefix_group,
    prefix_cache,
    page_table,
    norm_gain,
    w_query,
    w_keyval,
    w_out,
    moe_gain,
    routes,
    gates,
    w_gate_up,
    w_down,
):
    req_count = lax.axis_size("req")
    whole = gather_in_order(hidden_in, "hid", 1)
    tok_count = whole.shape[0]
    model_width = whole.shape[1]
    segment_row = segments[0]
    prefix_len = prefix_cache.shape[1]
    kv_heads = prefix_cache.shape[2]
    head_dim = prefix_cache.shape[3] // 2
    score_scale = head_dim ** (-0.5)
    normed = rms_scale(whole, norm_gain)
    position = positions_of(segment_row, prefix_len)
    projected = jnp.dot(normed, w_query, preferred_element_type=jnp.float32).reshape(
        tok_count, -1, head_dim
    )
    queries = rotate(projected, position).astype(jnp.bfloat16)
    queries, w_gate_up, w_down = lax.optimization_barrier((queries, w_gate_up, w_down))
    q_groups = queries.shape[1] // kv_heads
    grouped_query = queries.reshape(tok_count, kv_heads, q_groups, head_dim)
    key_value = jnp.dot(normed, w_keyval, preferred_element_type=jnp.float32).reshape(
        tok_count, kv_heads, 2 * head_dim
    )
    key_rows = rotate(key_value[..., :head_dim], position).astype(jnp.bfloat16)
    value_rows = key_value[..., head_dim:].astype(jnp.bfloat16)
    pages = jnp.concatenate([key_rows, value_rows], axis=-1).reshape(
        -1, PAGE, kv_heads, 2 * head_dim
    )
    kv_pages = jnp.zeros_like(pages).at[page_table[0]].set(pages)
    gathered = lax.all_gather(prefix_cache, "req", axis=0, tiled=True)
    attention = attend(
        grouped_query, key_rows, value_rows, segment_row, prefix_group[0],
        gathered.transpose(0, 2, 1, 3),
    )
    share_width = hidden_in.shape[1]
    whole_attention = jnp.concatenate(shifted_copies(attention, "hid"), axis=1)
    whole_w_out = jnp.concatenate(shifted_copies(w_out, "hid"), axis=0)
    projected_out = jnp.dot(whole_attention, whole_w_out, preferred_element_type=jnp.float32)
    middle = (whole.astype(jnp.float32) + projected_out).astype(jnp.bfloat16)
    middle_share = lax.dynamic_slice_in_dim(
        middle, lax.axis_index("hid") * share_width, share_width, 1
    )
    normed_moe = rms_scale(middle, moe_gain)
    local_experts, hidden_units, model_cols = w_down.shape
    lane_width = w_gate_up.shape[-1]
    down_view = (
        w_down.reshape(local_experts, hidden_units, model_cols // lane_width, lane_width)
        .transpose(0, 2, 1, 3)
        .reshape(local_experts, 1, -1, lane_width)
    )
    packed = jnp.concatenate([w_gate_up, down_view], axis=1).transpose(1, 0, 2, 3)
    packed = lax.all_gather(packed, "req", axis=1, tiled=True)
    experts = packed.shape[1]
    expert_ids = jnp.arange(experts, dtype=jnp.int32)
    combine = jnp.sum(
        jnp.where(routes[:, :, None] == expert_ids[None, None, :], gates[:, :, None], 0.0), axis=1
    )
    partial_out = (
        expert_project(normed_moe, combine.T[:, :, None], packed)
        .transpose(1, 0, 2)
        .reshape(tok_count, model_width)
    )
    hid_count = lax.axis_size("hid")
    hid_index = lax.axis_index("hid")
    expert_sum = lax.dynamic_slice_in_dim(partial_out, hid_index * share_width, share_width, 1)
    for shift in range(1, hid_count):
        block = (hid_index + shift) % hid_count
        outgoing = lax.dynamic_slice_in_dim(partial_out, block * share_width, share_width, 1)
        pairs = [(index, (index + shift) % hid_count) for index in range(hid_count)]
        incoming = lax.ppermute(outgoing.astype(jnp.bfloat16), "hid", pairs)
        expert_sum = expert_sum + incoming.astype(jnp.float32)
    hidden_out = (middle_share.astype(jnp.float32) + expert_sum).astype(jnp.bfloat16)
    return (hidden_out, kv_pages)


def solution(mesh):
    in_specs = (
        P("req", "hid"),
        P("req", None),
        P("req", None),
        P("req", None, "hid", None),
        P("req", None),
        P(),
        P(None, "hid"),
        P(None, "hid"),
        P("hid", None),
        P(),
        P("req", None),
        P("req", None),
        P("req", None, None, "hid"),
        P("req", "hid", None),
    )
    out_specs = (P("req", "hid"), P("req", None, "hid", None))
    return jax.shard_map(shards, mesh=mesh, in_specs=in_specs, out_specs=out_specs, check_vma=False)
```

```python
import functools

import jax
import jax.numpy as jnp
from jax import lax
from jax.sharding import PartitionSpec as P
from jax.experimental import pallas as pl
from jax.experimental.pallas import tpu as pltpu

PAGE = 128


EPSILON = 1e-06
THETA = 10000.0


def rms_scale(row_data, gain_row):
    floats = row_data.astype(jnp.float32)
    mean_square = jnp.mean(floats * floats, axis=-1, keepdims=True)
    return (floats * lax.rsqrt(mean_square + EPSILON) * gain_row).astype(jnp.bfloat16)


def rotate(features, positions):
    half_dim = features.shape[-1] // 2
    frequency = THETA ** (-2.0 * jnp.arange(half_dim, dtype=jnp.float32) / features.shape[-1])
    angles = positions.astype(jnp.float32)[:, None] * frequency[None, :]
    cosine = jnp.cos(angles)[:, None, :]
    sine_part = jnp.sin(angles)[:, None, :]
    front_half = features[..., :half_dim]
    second = features[..., half_dim:]
    return jnp.concatenate(
        [front_half * cosine - second * sine_part, second * cosine + front_half * sine_part],
        axis=-1,
    )


def positions_of(segment_row, offset):
    earlier = jnp.sum((segment_row[None, :] < segment_row[:, None]).astype(jnp.int32), axis=1)
    token_index = jnp.arange(segment_row.shape[0], dtype=jnp.int32)
    return token_index - earlier + offset


def slots_of(route_rows, experts):
    flat_routes = route_rows.reshape(-1)
    onehot = (flat_routes[:, None] == jnp.arange(experts, dtype=jnp.int32)[None, :]).astype(
        jnp.int32
    )
    before = jnp.cumsum(onehot, axis=0) - onehot
    return (flat_routes, jnp.sum(before * onehot, axis=1))


def expert_rows(received, gate_up, down_proj):
    local_experts = down_proj.shape[0]
    slot_count = received.shape[1]
    model_width = received.shape[2]
    grouped = received.reshape(-1, local_experts, slot_count, model_width)
    gate_proj = jnp.einsum(
        "recd,edf->recf", grouped, gate_up[:, 0], preferred_element_type=jnp.float32
    )
    up_proj = jnp.einsum(
        "recd,edf->recf", grouped, gate_up[:, 1], preferred_element_type=jnp.float32
    )
    hidden = (jax.nn.silu(gate_proj) * up_proj).astype(jnp.bfloat16)
    produced = jnp.einsum("recf,efd->recd", hidden, down_proj, preferred_element_type=jnp.float32)
    return produced.reshape(-1, slot_count, model_width)


def shifted_copies(block, axis_name):
    count = lax.axis_size(axis_name)
    copies = [block]
    for shift in range(1, count):
        pairs = [(index, (index + shift) % count) for index in range(count)]
        copies.append(lax.ppermute(block, axis_name, pairs))
    return copies


def gather_in_order(block, axis_name, axis):
    count = lax.axis_size(axis_name)
    copies = jnp.stack(shifted_copies(block, axis_name))
    order = (lax.axis_index(axis_name) - jnp.arange(count, dtype=jnp.int32)) % count
    picked = jnp.take(copies, order, axis=0)
    return jnp.concatenate([picked[index] for index in range(count)], axis=axis)


def attention_body(group_ref, bound_ref, q_ref, k_ref, v_ref, segq_ref, segk_ref, prefix_ref, out_ref):
    block = pl.program_id(1)
    seg = pl.program_id(2)
    seg_count = pl.num_programs(2)
    rows = q_ref.shape[2]
    tokens = k_ref.shape[1]
    head_dim = q_ref.shape[3]

    @pl.when(seg == 0)
    def _():
        out_ref[...] = jnp.zeros_like(out_ref)

    first = bound_ref[seg]
    last = bound_ref[seg + seg_count]
    active = (first < (block + 1) * rows) & (last > block * rows)

    @pl.when(active)
    def _():
        seg_q = segq_ref[...]
        seg_k = segk_ref[...]
        t_idx = block * rows + lax.broadcasted_iota(jnp.int32, (rows, tokens), 0)
        u_idx = lax.broadcasted_iota(jnp.int32, (rows, tokens), 1)
        visible = (seg_q == seg_k) & (u_idx <= t_idx)
        keys = k_ref[0]
        values = v_ref[0]
        prefix = prefix_ref[0, 0]
        prefix_keys = prefix[:, :head_dim]
        prefix_values = prefix[:, head_dim:]
        scale = head_dim ** (-0.5)
        mine = seg_q == seg
        contract = (((1,), (1,)), ((), ()))
        for group in range(q_ref.shape[1]):
            query = q_ref[0, group]
            local = lax.dot_general(query, keys, contract, preferred_element_type=jnp.float32) * scale
            local = jnp.where(visible, local, -jnp.inf)
            cached = (
                lax.dot_general(query, prefix_keys, contract, preferred_element_type=jnp.float32)
                * scale
            )
            top = jnp.maximum(
                jnp.max(local, axis=1, keepdims=True), jnp.max(cached, axis=1, keepdims=True)
            )
            local_num = jnp.exp(local - top)
            cached_num = jnp.exp(cached - top)
            total = jnp.sum(local_num, axis=1, keepdims=True) + jnp.sum(
                cached_num, axis=1, keepdims=True
            )
            summed = jnp.dot(
                local_num.astype(jnp.bfloat16), values, preferred_element_type=jnp.float32
            ) + jnp.dot(
                cached_num.astype(jnp.bfloat16), prefix_values, preferred_element_type=jnp.float32
            )
            out_ref[0, group] = jnp.where(mine, summed / total, out_ref[0, group])


def attend(grouped_query, key_rows, value_rows, segment_row, group_row, prefix_heads, interpret=False):
    tok_count, kv_heads, q_groups, head_dim = grouped_query.shape
    seg_count = group_row.shape[0]
    prefix_len = prefix_heads.shape[2]
    rows = min(128, tok_count)
    labels = jnp.arange(seg_count, dtype=jnp.int32)
    first = jnp.sum((segment_row[None, :] < labels[:, None]).astype(jnp.int32), axis=1)
    last = jnp.sum((segment_row[None, :] <= labels[:, None]).astype(jnp.int32), axis=1)
    bounds = jnp.concatenate([first, last])
    query_heads = grouped_query.transpose(1, 2, 0, 3)
    key_heads = key_rows.transpose(1, 0, 2)
    value_heads = value_rows.transpose(1, 0, 2)
    seg_col = segment_row.reshape(tok_count, 1)
    seg_line = segment_row.reshape(1, tok_count)
    grid_spec = pltpu.PrefetchScalarGridSpec(
        num_scalar_prefetch=2,
        grid=(kv_heads, tok_count // rows, seg_count),
        in_specs=[
            pl.BlockSpec((1, q_groups, rows, head_dim), lambda h, b, s, gr, bd: (h, 0, b, 0)),
            pl.BlockSpec((1, tok_count, head_dim), lambda h, b, s, gr, bd: (h, 0, 0)),
            pl.BlockSpec((1, tok_count, head_dim), lambda h, b, s, gr, bd: (h, 0, 0)),
            pl.BlockSpec((rows, 1), lambda h, b, s, gr, bd: (b, 0)),
            pl.BlockSpec((1, tok_count), lambda h, b, s, gr, bd: (0, 0)),
            pl.BlockSpec(
                (1, 1, prefix_len, 2 * head_dim), lambda h, b, s, gr, bd: (gr[s], h, 0, 0)
            ),
        ],
        out_specs=pl.BlockSpec((1, q_groups, rows, head_dim), lambda h, b, s, gr, bd: (h, 0, b, 0)),
    )
    out = pl.pallas_call(
        attention_body,
        grid_spec=grid_spec,
        out_shape=jax.ShapeDtypeStruct((kv_heads, q_groups, tok_count, head_dim), jnp.float32),
        compiler_params=pltpu.CompilerParams(
            dimension_semantics=("arbitrary", "arbitrary", "arbitrary")
        ),
        interpret=interpret,
    )(group_row, bounds, query_heads, key_heads, value_heads, seg_col, seg_line, prefix_heads)
    return out.transpose(2, 0, 1, 3).reshape(tok_count, -1).astype(jnp.bfloat16)


def expert_body(normed_ref, combine_ref, weight_ref, down_ref, out_ref, hidden_ref):
    experts = hidden_ref.shape[0]

    @pl.when(pl.program_id(0) == 0)
    def _():
        rows = normed_ref[...]
        for expert in range(experts):
            gate_proj = jnp.dot(rows, weight_ref[0, expert], preferred_element_type=jnp.float32)
            up_proj = jnp.dot(rows, weight_ref[1, expert], preferred_element_type=jnp.float32)
            activated = gate_proj / (1.0 + jnp.exp(-gate_proj))
            hidden_ref[expert] = (activated * up_proj * combine_ref[expert]).astype(jnp.bfloat16)

    units = hidden_ref.shape[2]
    for col in range(out_ref.shape[0]):
        total = jnp.zeros(out_ref.shape[1:], jnp.float32)
        for expert in range(experts):
            total = total + jnp.dot(
                hidden_ref[expert],
                down_ref[0, expert, col * units : (col + 1) * units, :],
                preferred_element_type=jnp.float32,
            )
        out_ref[col] = total


def expert_project(normed_moe, combine, packed):
    tok_count, model_width = normed_moe.shape
    experts, lanes = packed.shape[1], packed.shape[3]
    units = lanes
    col_blocks = packed.shape[2] // units
    per_step = col_blocks
    return pl.pallas_call(
        expert_body,
        grid=(col_blocks // per_step,),
        in_specs=[
            pl.BlockSpec((tok_count, model_width), lambda c: (0, 0)),
            pl.BlockSpec((experts, tok_count, 1), lambda c: (0, 0, 0)),
            pl.BlockSpec((2, experts, model_width, lanes), lambda c: (0, 0, 0, 0)),
            pl.BlockSpec((1, experts, per_step * units, lanes), lambda c: (2, 0, c, 0)),
        ],
        out_specs=pl.BlockSpec((per_step, tok_count, lanes), lambda c: (c, 0, 0)),
        out_shape=jax.ShapeDtypeStruct((col_blocks, tok_count, lanes), jnp.float32),
        scratch_shapes=[pltpu.VMEM((experts, tok_count, units), jnp.bfloat16)],
        compiler_params=pltpu.CompilerParams(dimension_semantics=("arbitrary",)),
    )(normed_moe, combine, packed, packed)


def shards(
    hidden_in,
    segments,
    prefix_group,
    prefix_cache,
    page_table,
    norm_gain,
    w_query,
    w_keyval,
    w_out,
    moe_gain,
    routes,
    gates,
    w_gate_up,
    w_down,
):
    req_count = lax.axis_size("req")
    whole = gather_in_order(hidden_in, "hid", 1)
    tok_count = whole.shape[0]
    model_width = whole.shape[1]
    segment_row = segments[0]
    prefix_len = prefix_cache.shape[1]
    kv_heads = prefix_cache.shape[2]
    head_dim = prefix_cache.shape[3] // 2
    score_scale = head_dim ** (-0.5)
    normed = rms_scale(whole, norm_gain)
    position = positions_of(segment_row, prefix_len)
    projected = jnp.dot(normed, w_query, preferred_element_type=jnp.float32).reshape(
        tok_count, -1, head_dim
    )
    queries = rotate(projected, position).astype(jnp.bfloat16)
    queries, w_gate_up, w_down = lax.optimization_barrier((queries, w_gate_up, w_down))
    q_groups = queries.shape[1] // kv_heads
    grouped_query = queries.reshape(tok_count, kv_heads, q_groups, head_dim)
    key_value = jnp.dot(normed, w_keyval, preferred_element_type=jnp.float32).reshape(
        tok_count, kv_heads, 2 * head_dim
    )
    key_rows = rotate(key_value[..., :head_dim], position).astype(jnp.bfloat16)
    value_rows = key_value[..., head_dim:].astype(jnp.bfloat16)
    pages = jnp.concatenate([key_rows, value_rows], axis=-1).reshape(
        -1, PAGE, kv_heads, 2 * head_dim
    )
    kv_pages = jnp.zeros_like(pages).at[page_table[0]].set(pages)
    gathered = lax.all_gather(prefix_cache, "req", axis=0, tiled=True)
    attention = attend(
        grouped_query, key_rows, value_rows, segment_row, prefix_group[0],
        gathered.transpose(0, 2, 1, 3),
    )
    share_width = hidden_in.shape[1]
    whole_attention = jnp.concatenate(shifted_copies(attention, "hid"), axis=1)
    whole_w_out = jnp.concatenate(shifted_copies(w_out, "hid"), axis=0)
    projected_out = jnp.dot(whole_attention, whole_w_out, preferred_element_type=jnp.float32)
    middle = (whole.astype(jnp.float32) + projected_out).astype(jnp.bfloat16)
    middle_share = lax.dynamic_slice_in_dim(
        middle, lax.axis_index("hid") * share_width, share_width, 1
    )
    normed_moe = rms_scale(middle, moe_gain)
    local_experts, hidden_units, model_cols = w_down.shape
    lane_width = w_gate_up.shape[-1]
    down_view = (
        w_down.reshape(local_experts, hidden_units, model_cols // lane_width, lane_width)
        .transpose(0, 2, 1, 3)
        .reshape(local_experts, 1, -1, lane_width)
    )
    packed = jnp.concatenate([w_gate_up, down_view], axis=1).transpose(1, 0, 2, 3)
    packed = lax.all_gather(packed, "req", axis=1, tiled=True)
    experts = packed.shape[1]
    expert_ids = jnp.arange(experts, dtype=jnp.int32)
    combine = jnp.sum(
        jnp.where(routes[:, :, None] == expert_ids[None, None, :], gates[:, :, None], 0.0), axis=1
    )
    partial_out = (
        expert_project(normed_moe, combine.T[:, :, None], packed)
        .transpose(1, 0, 2)
        .reshape(tok_count, model_width)
    )
    hid_count = lax.axis_size("hid")
    hid_index = lax.axis_index("hid")
    expert_sum = lax.dynamic_slice_in_dim(partial_out, hid_index * share_width, share_width, 1)
    for shift in range(1, hid_count):
        block = (hid_index + shift) % hid_count
        outgoing = lax.dynamic_slice_in_dim(partial_out, block * share_width, share_width, 1)
        pairs = [(index, (index + shift) % hid_count) for index in range(hid_count)]
        incoming = lax.ppermute(outgoing.astype(jnp.bfloat16), "hid", pairs)
        expert_sum = expert_sum + incoming.astype(jnp.float32)
    hidden_out = (middle_share.astype(jnp.float32) + expert_sum).astype(jnp.bfloat16)
    return (hidden_out, kv_pages)


def solution(mesh):
    in_specs = (
        P("req", "hid"),
        P("req", None),
        P("req", None),
        P("req", None, "hid", None),
        P("req", None),
        P(),
        P(None, "hid"),
        P(None, "hid"),
        P("hid", None),
        P(),
        P("req", None),
        P("req", None),
        P("req", None, None, "hid"),
        P("req", "hid", None),
    )
    out_specs = (P("req", "hid"), P("req", None, "hid", None))
    return jax.shard_map(shards, mesh=mesh, in_specs=in_specs, out_specs=out_specs, check_vma=False)
```

```python
import functools

import jax
import jax.numpy as jnp
from jax import lax
from jax.sharding import PartitionSpec as P
from jax.experimental import pallas as pl
from jax.experimental.pallas import tpu as pltpu

PAGE = 128


EPSILON = 1e-06
THETA = 10000.0


def rms_scale(row_data, gain_row):
    floats = row_data.astype(jnp.float32)
    mean_square = jnp.mean(floats * floats, axis=-1, keepdims=True)
    return (floats * lax.rsqrt(mean_square + EPSILON) * gain_row).astype(jnp.bfloat16)


def rotate(features, positions):
    half_dim = features.shape[-1] // 2
    frequency = THETA ** (-2.0 * jnp.arange(half_dim, dtype=jnp.float32) / features.shape[-1])
    angles = positions.astype(jnp.float32)[:, None] * frequency[None, :]
    cosine = jnp.cos(angles)[:, None, :]
    sine_part = jnp.sin(angles)[:, None, :]
    front_half = features[..., :half_dim]
    second = features[..., half_dim:]
    return jnp.concatenate(
        [front_half * cosine - second * sine_part, second * cosine + front_half * sine_part],
        axis=-1,
    )


def positions_of(segment_row, offset):
    earlier = jnp.sum((segment_row[None, :] < segment_row[:, None]).astype(jnp.int32), axis=1)
    token_index = jnp.arange(segment_row.shape[0], dtype=jnp.int32)
    return token_index - earlier + offset


def slots_of(route_rows, experts):
    flat_routes = route_rows.reshape(-1)
    onehot = (flat_routes[:, None] == jnp.arange(experts, dtype=jnp.int32)[None, :]).astype(
        jnp.int32
    )
    before = jnp.cumsum(onehot, axis=0) - onehot
    return (flat_routes, jnp.sum(before * onehot, axis=1))


def expert_rows(received, gate_up, down_proj):
    local_experts = down_proj.shape[0]
    slot_count = received.shape[1]
    model_width = received.shape[2]
    grouped = received.reshape(-1, local_experts, slot_count, model_width)
    gate_proj = jnp.einsum(
        "recd,edf->recf", grouped, gate_up[:, 0], preferred_element_type=jnp.float32
    )
    up_proj = jnp.einsum(
        "recd,edf->recf", grouped, gate_up[:, 1], preferred_element_type=jnp.float32
    )
    hidden = (jax.nn.silu(gate_proj) * up_proj).astype(jnp.bfloat16)
    produced = jnp.einsum("recf,efd->recd", hidden, down_proj, preferred_element_type=jnp.float32)
    return produced.reshape(-1, slot_count, model_width)


def shifted_copies(block, axis_name):
    count = lax.axis_size(axis_name)
    copies = [block]
    for shift in range(1, count):
        pairs = [(index, (index + shift) % count) for index in range(count)]
        copies.append(lax.ppermute(block, axis_name, pairs))
    return copies


def gather_in_order(block, axis_name, axis):
    count = lax.axis_size(axis_name)
    copies = jnp.stack(shifted_copies(block, axis_name))
    order = (lax.axis_index(axis_name) - jnp.arange(count, dtype=jnp.int32)) % count
    picked = jnp.take(copies, order, axis=0)
    return jnp.concatenate([picked[index] for index in range(count)], axis=axis)


def attention_body(group_ref, bound_ref, q_ref, k_ref, v_ref, segq_ref, segk_ref, prefix_ref, out_ref):
    block = pl.program_id(1)
    seg = pl.program_id(2)
    seg_count = pl.num_programs(2)
    rows = q_ref.shape[2]
    tokens = k_ref.shape[1]
    head_dim = q_ref.shape[3]

    @pl.when(seg == 0)
    def _():
        out_ref[...] = jnp.zeros_like(out_ref)

    first = bound_ref[seg]
    last = bound_ref[seg + seg_count]
    active = (first < (block + 1) * rows) & (last > block * rows)

    @pl.when(active)
    def _():
        seg_q = segq_ref[...]
        seg_k = segk_ref[...]
        t_idx = block * rows + lax.broadcasted_iota(jnp.int32, (rows, tokens), 0)
        u_idx = lax.broadcasted_iota(jnp.int32, (rows, tokens), 1)
        visible = (seg_q == seg_k) & (u_idx <= t_idx)
        keys = k_ref[0]
        values = v_ref[0]
        prefix = prefix_ref[0, 0]
        prefix_keys = prefix[:, :head_dim]
        prefix_values = prefix[:, head_dim:]
        scale = head_dim ** (-0.5)
        mine = seg_q == seg
        contract = (((1,), (1,)), ((), ()))
        for group in range(q_ref.shape[1]):
            query = q_ref[0, group]
            local = lax.dot_general(query, keys, contract, preferred_element_type=jnp.float32) * scale
            local = jnp.where(visible, local, -jnp.inf)
            cached = (
                lax.dot_general(query, prefix_keys, contract, preferred_element_type=jnp.float32)
                * scale
            )
            top = jnp.maximum(
                jnp.max(local, axis=1, keepdims=True), jnp.max(cached, axis=1, keepdims=True)
            )
            local_num = jnp.exp(local - top)
            cached_num = jnp.exp(cached - top)
            total = jnp.sum(local_num, axis=1, keepdims=True) + jnp.sum(
                cached_num, axis=1, keepdims=True
            )
            summed = jnp.dot(
                local_num.astype(jnp.bfloat16), values, preferred_element_type=jnp.float32
            ) + jnp.dot(
                cached_num.astype(jnp.bfloat16), prefix_values, preferred_element_type=jnp.float32
            )
            out_ref[0, group] = jnp.where(mine, summed / total, out_ref[0, group])


def attend(grouped_query, key_rows, value_rows, segment_row, group_row, prefix_heads, interpret=False):
    tok_count, kv_heads, q_groups, head_dim = grouped_query.shape
    seg_count = group_row.shape[0]
    prefix_len = prefix_heads.shape[2]
    rows = min(128, tok_count)
    labels = jnp.arange(seg_count, dtype=jnp.int32)
    first = jnp.sum((segment_row[None, :] < labels[:, None]).astype(jnp.int32), axis=1)
    last = jnp.sum((segment_row[None, :] <= labels[:, None]).astype(jnp.int32), axis=1)
    bounds = jnp.concatenate([first, last])
    query_heads = grouped_query.transpose(1, 2, 0, 3)
    key_heads = key_rows.transpose(1, 0, 2)
    value_heads = value_rows.transpose(1, 0, 2)
    seg_col = segment_row.reshape(tok_count, 1)
    seg_line = segment_row.reshape(1, tok_count)
    grid_spec = pltpu.PrefetchScalarGridSpec(
        num_scalar_prefetch=2,
        grid=(kv_heads, tok_count // rows, seg_count),
        in_specs=[
            pl.BlockSpec((1, q_groups, rows, head_dim), lambda h, b, s, gr, bd: (h, 0, b, 0)),
            pl.BlockSpec((1, tok_count, head_dim), lambda h, b, s, gr, bd: (h, 0, 0)),
            pl.BlockSpec((1, tok_count, head_dim), lambda h, b, s, gr, bd: (h, 0, 0)),
            pl.BlockSpec((rows, 1), lambda h, b, s, gr, bd: (b, 0)),
            pl.BlockSpec((1, tok_count), lambda h, b, s, gr, bd: (0, 0)),
            pl.BlockSpec(
                (1, 1, prefix_len, 2 * head_dim), lambda h, b, s, gr, bd: (gr[s], h, 0, 0)
            ),
        ],
        out_specs=pl.BlockSpec((1, q_groups, rows, head_dim), lambda h, b, s, gr, bd: (h, 0, b, 0)),
    )
    out = pl.pallas_call(
        attention_body,
        grid_spec=grid_spec,
        out_shape=jax.ShapeDtypeStruct((kv_heads, q_groups, tok_count, head_dim), jnp.float32),
        compiler_params=pltpu.CompilerParams(
            dimension_semantics=("arbitrary", "arbitrary", "arbitrary")
        ),
        interpret=interpret,
    )(group_row, bounds, query_heads, key_heads, value_heads, seg_col, seg_line, prefix_heads)
    return out.transpose(2, 0, 1, 3).reshape(tok_count, -1).astype(jnp.bfloat16)


def expert_body(normed_ref, combine_ref, weight_ref, down_ref, out_ref, hidden_ref):
    experts = hidden_ref.shape[0]

    @pl.when(pl.program_id(0) == 0)
    def _():
        rows = normed_ref[...]
        for expert in range(experts):
            gate_proj = jnp.dot(rows, weight_ref[0, expert], preferred_element_type=jnp.float32)
            up_proj = jnp.dot(rows, weight_ref[1, expert], preferred_element_type=jnp.float32)
            activated = gate_proj / (1.0 + jnp.exp(-gate_proj))
            hidden_ref[expert] = (activated * up_proj * combine_ref[expert]).astype(jnp.bfloat16)

    units = hidden_ref.shape[2]
    per_block = down_ref.shape[2] // units
    for col in range(per_block):
        total = jnp.zeros((out_ref.shape[0], out_ref.shape[1] // per_block), jnp.float32)
        for expert in range(experts):
            total = total + jnp.dot(
                hidden_ref[expert],
                down_ref[0, expert, col * units : (col + 1) * units, :],
                preferred_element_type=jnp.float32,
            )
        out_ref[:, col * out_ref.shape[1] // per_block : (col + 1) * out_ref.shape[1] // per_block] = total


def expert_project(normed_moe, combine, packed):
    tok_count, model_width = normed_moe.shape
    experts, lanes = packed.shape[1], packed.shape[3]
    units = lanes
    col_blocks = packed.shape[2] // units
    per_step = 4 if col_blocks % 4 == 0 and (4 * lanes) % 128 == 0 else col_blocks
    return pl.pallas_call(
        expert_body,
        grid=(col_blocks // per_step,),
        in_specs=[
            pl.BlockSpec((tok_count, model_width), lambda c: (0, 0)),
            pl.BlockSpec((experts, tok_count, 1), lambda c: (0, 0, 0)),
            pl.BlockSpec((2, experts, model_width, lanes), lambda c: (0, 0, 0, 0)),
            pl.BlockSpec((1, experts, per_step * units, lanes), lambda c: (2, 0, c, 0)),
        ],
        out_specs=pl.BlockSpec((tok_count, per_step * lanes), lambda c: (0, c)),
        out_shape=jax.ShapeDtypeStruct((tok_count, col_blocks * lanes), jnp.float32),
        scratch_shapes=[pltpu.VMEM((experts, tok_count, units), jnp.bfloat16)],
        compiler_params=pltpu.CompilerParams(dimension_semantics=("arbitrary",)),
    )(normed_moe, combine, packed, packed)


def shards(
    hidden_in,
    segments,
    prefix_group,
    prefix_cache,
    page_table,
    norm_gain,
    w_query,
    w_keyval,
    w_out,
    moe_gain,
    routes,
    gates,
    w_gate_up,
    w_down,
):
    req_count = lax.axis_size("req")
    whole = gather_in_order(hidden_in, "hid", 1)
    tok_count = whole.shape[0]
    model_width = whole.shape[1]
    segment_row = segments[0]
    prefix_len = prefix_cache.shape[1]
    kv_heads = prefix_cache.shape[2]
    head_dim = prefix_cache.shape[3] // 2
    score_scale = head_dim ** (-0.5)
    normed = rms_scale(whole, norm_gain)
    position = positions_of(segment_row, prefix_len)
    projected = jnp.dot(normed, w_query, preferred_element_type=jnp.float32).reshape(
        tok_count, -1, head_dim
    )
    queries = rotate(projected, position).astype(jnp.bfloat16)
    queries, w_gate_up, w_down = lax.optimization_barrier((queries, w_gate_up, w_down))
    q_groups = queries.shape[1] // kv_heads
    grouped_query = queries.reshape(tok_count, kv_heads, q_groups, head_dim)
    key_value = jnp.dot(normed, w_keyval, preferred_element_type=jnp.float32).reshape(
        tok_count, kv_heads, 2 * head_dim
    )
    key_rows = rotate(key_value[..., :head_dim], position).astype(jnp.bfloat16)
    value_rows = key_value[..., head_dim:].astype(jnp.bfloat16)
    pages = jnp.concatenate([key_rows, value_rows], axis=-1).reshape(
        -1, PAGE, kv_heads, 2 * head_dim
    )
    kv_pages = jnp.zeros_like(pages).at[page_table[0]].set(pages)
    gathered = lax.all_gather(prefix_cache, "req", axis=0, tiled=True)
    attention = attend(
        grouped_query, key_rows, value_rows, segment_row, prefix_group[0],
        gathered.transpose(0, 2, 1, 3),
    )
    share_width = hidden_in.shape[1]
    whole_attention = jnp.concatenate(shifted_copies(attention, "hid"), axis=1)
    whole_w_out = jnp.concatenate(shifted_copies(w_out, "hid"), axis=0)
    projected_out = jnp.dot(whole_attention, whole_w_out, preferred_element_type=jnp.float32)
    middle = (whole.astype(jnp.float32) + projected_out).astype(jnp.bfloat16)
    middle_share = lax.dynamic_slice_in_dim(
        middle, lax.axis_index("hid") * share_width, share_width, 1
    )
    normed_moe = rms_scale(middle, moe_gain)
    local_experts, hidden_units, model_cols = w_down.shape
    lane_width = w_gate_up.shape[-1]
    down_view = (
        w_down.reshape(local_experts, hidden_units, model_cols // lane_width, lane_width)
        .transpose(0, 2, 1, 3)
        .reshape(local_experts, 1, -1, lane_width)
    )
    packed = jnp.concatenate([w_gate_up, down_view], axis=1).transpose(1, 0, 2, 3)
    packed = lax.all_gather(packed, "req", axis=1, tiled=True)
    experts = packed.shape[1]
    expert_ids = jnp.arange(experts, dtype=jnp.int32)
    combine = jnp.sum(
        jnp.where(routes[:, :, None] == expert_ids[None, None, :], gates[:, :, None], 0.0), axis=1
    )
    partial_out = expert_project(normed_moe, combine.T[:, :, None], packed)
    hid_count = lax.axis_size("hid")
    hid_index = lax.axis_index("hid")
    expert_sum = lax.dynamic_slice_in_dim(partial_out, hid_index * share_width, share_width, 1)
    for shift in range(1, hid_count):
        block = (hid_index + shift) % hid_count
        outgoing = lax.dynamic_slice_in_dim(partial_out, block * share_width, share_width, 1)
        pairs = [(index, (index + shift) % hid_count) for index in range(hid_count)]
        incoming = lax.ppermute(outgoing.astype(jnp.bfloat16), "hid", pairs)
        expert_sum = expert_sum + incoming.astype(jnp.float32)
    hidden_out = (middle_share.astype(jnp.float32) + expert_sum).astype(jnp.bfloat16)
    return (hidden_out, kv_pages)


def solution(mesh):
    in_specs = (
        P("req", "hid"),
        P("req", None),
        P("req", None),
        P("req", None, "hid", None),
        P("req", None),
        P(),
        P(None, "hid"),
        P(None, "hid"),
        P("hid", None),
        P(),
        P("req", None),
        P("req", None),
        P("req", None, None, "hid"),
        P("req", "hid", None),
    )
    out_specs = (P("req", "hid"), P("req", None, "hid", None))
    return jax.shard_map(shards, mesh=mesh, in_specs=in_specs, out_specs=out_specs, check_vma=False)
```

```python
import functools

import jax
import jax.numpy as jnp
from jax import lax
from jax.sharding import PartitionSpec as P
from jax.experimental import pallas as pl
from jax.experimental.pallas import tpu as pltpu

PAGE = 128


EPSILON = 1e-06
THETA = 10000.0


def rms_scale(row_data, gain_row):
    floats = row_data.astype(jnp.float32)
    mean_square = jnp.mean(floats * floats, axis=-1, keepdims=True)
    return (floats * lax.rsqrt(mean_square + EPSILON) * gain_row).astype(jnp.bfloat16)


def rotate(features, positions):
    half_dim = features.shape[-1] // 2
    frequency = THETA ** (-2.0 * jnp.arange(half_dim, dtype=jnp.float32) / features.shape[-1])
    angles = positions.astype(jnp.float32)[:, None] * frequency[None, :]
    cosine = jnp.cos(angles)[:, None, :]
    sine_part = jnp.sin(angles)[:, None, :]
    front_half = features[..., :half_dim]
    second = features[..., half_dim:]
    return jnp.concatenate(
        [front_half * cosine - second * sine_part, second * cosine + front_half * sine_part],
        axis=-1,
    )


def positions_of(segment_row, offset):
    earlier = jnp.sum((segment_row[None, :] < segment_row[:, None]).astype(jnp.int32), axis=1)
    token_index = jnp.arange(segment_row.shape[0], dtype=jnp.int32)
    return token_index - earlier + offset


def slots_of(route_rows, experts):
    flat_routes = route_rows.reshape(-1)
    onehot = (flat_routes[:, None] == jnp.arange(experts, dtype=jnp.int32)[None, :]).astype(
        jnp.int32
    )
    before = jnp.cumsum(onehot, axis=0) - onehot
    return (flat_routes, jnp.sum(before * onehot, axis=1))


def expert_rows(received, gate_up, down_proj):
    local_experts = down_proj.shape[0]
    slot_count = received.shape[1]
    model_width = received.shape[2]
    grouped = received.reshape(-1, local_experts, slot_count, model_width)
    gate_proj = jnp.einsum(
        "recd,edf->recf", grouped, gate_up[:, 0], preferred_element_type=jnp.float32
    )
    up_proj = jnp.einsum(
        "recd,edf->recf", grouped, gate_up[:, 1], preferred_element_type=jnp.float32
    )
    hidden = (jax.nn.silu(gate_proj) * up_proj).astype(jnp.bfloat16)
    produced = jnp.einsum("recf,efd->recd", hidden, down_proj, preferred_element_type=jnp.float32)
    return produced.reshape(-1, slot_count, model_width)


def shifted_copies(block, axis_name):
    count = lax.axis_size(axis_name)
    copies = [block]
    for shift in range(1, count):
        pairs = [(index, (index + shift) % count) for index in range(count)]
        copies.append(lax.ppermute(block, axis_name, pairs))
    return copies


def gather_in_order(block, axis_name, axis):
    count = lax.axis_size(axis_name)
    copies = jnp.stack(shifted_copies(block, axis_name))
    order = (lax.axis_index(axis_name) - jnp.arange(count, dtype=jnp.int32)) % count
    picked = jnp.take(copies, order, axis=0)
    return jnp.concatenate([picked[index] for index in range(count)], axis=axis)


def attention_body(group_ref, bound_ref, q_ref, k_ref, v_ref, segq_ref, segk_ref, prefix_ref, out_ref):
    block = pl.program_id(1)
    seg = pl.program_id(2)
    seg_count = pl.num_programs(2)
    rows = q_ref.shape[2]
    tokens = k_ref.shape[1]
    head_dim = q_ref.shape[3]

    @pl.when(seg == 0)
    def _():
        out_ref[...] = jnp.zeros_like(out_ref)

    first = bound_ref[seg]
    last = bound_ref[seg + seg_count]
    active = (first < (block + 1) * rows) & (last > block * rows)

    @pl.when(active)
    def _():
        seg_q = segq_ref[...]
        seg_k = segk_ref[...]
        t_idx = block * rows + lax.broadcasted_iota(jnp.int32, (rows, tokens), 0)
        u_idx = lax.broadcasted_iota(jnp.int32, (rows, tokens), 1)
        visible = (seg_q == seg_k) & (u_idx <= t_idx)
        keys = k_ref[0]
        values = v_ref[0]
        prefix = prefix_ref[0, 0]
        prefix_keys = prefix[:, :head_dim]
        prefix_values = prefix[:, head_dim:]
        scale = head_dim ** (-0.5)
        mine = seg_q == seg
        contract = (((1,), (1,)), ((), ()))
        for group in range(q_ref.shape[1]):
            query = q_ref[0, group]
            local = lax.dot_general(query, keys, contract, preferred_element_type=jnp.float32) * scale
            local = jnp.where(visible, local, -jnp.inf)
            cached = (
                lax.dot_general(query, prefix_keys, contract, preferred_element_type=jnp.float32)
                * scale
            )
            top = jnp.maximum(
                jnp.max(local, axis=1, keepdims=True), jnp.max(cached, axis=1, keepdims=True)
            )
            local_num = jnp.exp(local - top)
            cached_num = jnp.exp(cached - top)
            total = jnp.sum(local_num, axis=1, keepdims=True) + jnp.sum(
                cached_num, axis=1, keepdims=True
            )
            summed = jnp.dot(
                local_num.astype(jnp.bfloat16), values, preferred_element_type=jnp.float32
            ) + jnp.dot(
                cached_num.astype(jnp.bfloat16), prefix_values, preferred_element_type=jnp.float32
            )
            out_ref[0, group] = jnp.where(mine, summed / total, out_ref[0, group])


def attend(grouped_query, key_rows, value_rows, segment_row, group_row, prefix_heads, interpret=False):
    tok_count, kv_heads, q_groups, head_dim = grouped_query.shape
    seg_count = group_row.shape[0]
    prefix_len = prefix_heads.shape[2]
    rows = min(128, tok_count)
    labels = jnp.arange(seg_count, dtype=jnp.int32)
    first = jnp.sum((segment_row[None, :] < labels[:, None]).astype(jnp.int32), axis=1)
    last = jnp.sum((segment_row[None, :] <= labels[:, None]).astype(jnp.int32), axis=1)
    bounds = jnp.concatenate([first, last])
    query_heads = grouped_query.transpose(1, 2, 0, 3)
    key_heads = key_rows.transpose(1, 0, 2)
    value_heads = value_rows.transpose(1, 0, 2)
    seg_col = segment_row.reshape(tok_count, 1)
    seg_line = segment_row.reshape(1, tok_count)
    grid_spec = pltpu.PrefetchScalarGridSpec(
        num_scalar_prefetch=2,
        grid=(kv_heads, tok_count // rows, seg_count),
        in_specs=[
            pl.BlockSpec((1, q_groups, rows, head_dim), lambda h, b, s, gr, bd: (h, 0, b, 0)),
            pl.BlockSpec((1, tok_count, head_dim), lambda h, b, s, gr, bd: (h, 0, 0)),
            pl.BlockSpec((1, tok_count, head_dim), lambda h, b, s, gr, bd: (h, 0, 0)),
            pl.BlockSpec((rows, 1), lambda h, b, s, gr, bd: (b, 0)),
            pl.BlockSpec((1, tok_count), lambda h, b, s, gr, bd: (0, 0)),
            pl.BlockSpec(
                (1, 1, prefix_len, 2 * head_dim), lambda h, b, s, gr, bd: (gr[s], h, 0, 0)
            ),
        ],
        out_specs=pl.BlockSpec((1, q_groups, rows, head_dim), lambda h, b, s, gr, bd: (h, 0, b, 0)),
    )
    out = pl.pallas_call(
        attention_body,
        grid_spec=grid_spec,
        out_shape=jax.ShapeDtypeStruct((kv_heads, q_groups, tok_count, head_dim), jnp.float32),
        compiler_params=pltpu.CompilerParams(
            dimension_semantics=("arbitrary", "arbitrary", "arbitrary")
        ),
        interpret=interpret,
    )(group_row, bounds, query_heads, key_heads, value_heads, seg_col, seg_line, prefix_heads)
    return out.transpose(2, 0, 1, 3).reshape(tok_count, -1).astype(jnp.bfloat16)


def expert_body(normed_ref, combine_ref, weight_ref, down_ref, out_ref, hidden_ref):
    experts = hidden_ref.shape[0]

    @pl.when(pl.program_id(0) == 0)
    def _():
        rows = normed_ref[...]
        for expert in range(experts):
            gate_proj = jnp.dot(rows, weight_ref[0, expert], preferred_element_type=jnp.float32)
            up_proj = jnp.dot(rows, weight_ref[1, expert], preferred_element_type=jnp.float32)
            activated = gate_proj / (1.0 + jnp.exp(-gate_proj))
            hidden_ref[expert] = (activated * up_proj * combine_ref[expert]).astype(jnp.bfloat16)

    units = hidden_ref.shape[2]
    for col in range(out_ref.shape[0]):
        total = jnp.zeros(out_ref.shape[1:], jnp.float32)
        for expert in range(experts):
            total = total + jnp.dot(
                hidden_ref[expert],
                down_ref[0, expert, col * units : (col + 1) * units, :],
                preferred_element_type=jnp.float32,
            )
        out_ref[col] = total


def expert_project(normed_moe, combine, packed):
    tok_count, model_width = normed_moe.shape
    experts, lanes = packed.shape[1], packed.shape[3]
    units = lanes
    col_blocks = packed.shape[2] // units
    per_step = 2 if col_blocks % 2 == 0 else 1
    return pl.pallas_call(
        expert_body,
        grid=(col_blocks // per_step,),
        in_specs=[
            pl.BlockSpec((tok_count, model_width), lambda c: (0, 0)),
            pl.BlockSpec((experts, tok_count, 1), lambda c: (0, 0, 0)),
            pl.BlockSpec((2, experts, model_width, lanes), lambda c: (0, 0, 0, 0)),
            pl.BlockSpec((1, experts, per_step * units, lanes), lambda c: (2, 0, c, 0)),
        ],
        out_specs=pl.BlockSpec((per_step, tok_count, lanes), lambda c: (c, 0, 0)),
        out_shape=jax.ShapeDtypeStruct((col_blocks, tok_count, lanes), jnp.float32),
        scratch_shapes=[pltpu.VMEM((experts, tok_count, units), jnp.bfloat16)],
        compiler_params=pltpu.CompilerParams(dimension_semantics=("arbitrary",)),
    )(normed_moe, combine, packed, packed)


def shards(
    hidden_in,
    segments,
    prefix_group,
    prefix_cache,
    page_table,
    norm_gain,
    w_query,
    w_keyval,
    w_out,
    moe_gain,
    routes,
    gates,
    w_gate_up,
    w_down,
):
    req_count = lax.axis_size("req")
    whole = gather_in_order(hidden_in, "hid", 1)
    tok_count = whole.shape[0]
    model_width = whole.shape[1]
    segment_row = segments[0]
    prefix_len = prefix_cache.shape[1]
    kv_heads = prefix_cache.shape[2]
    head_dim = prefix_cache.shape[3] // 2
    score_scale = head_dim ** (-0.5)
    normed = rms_scale(whole, norm_gain)
    position = positions_of(segment_row, prefix_len)
    projected = jnp.dot(normed, w_query, preferred_element_type=jnp.float32).reshape(
        tok_count, -1, head_dim
    )
    queries = rotate(projected, position).astype(jnp.bfloat16)
    queries, w_gate_up, w_down = lax.optimization_barrier((queries, w_gate_up, w_down))
    q_groups = queries.shape[1] // kv_heads
    grouped_query = queries.reshape(tok_count, kv_heads, q_groups, head_dim)
    key_value = jnp.dot(normed, w_keyval, preferred_element_type=jnp.float32).reshape(
        tok_count, kv_heads, 2 * head_dim
    )
    key_rows = rotate(key_value[..., :head_dim], position).astype(jnp.bfloat16)
    value_rows = key_value[..., head_dim:].astype(jnp.bfloat16)
    pages = jnp.concatenate([key_rows, value_rows], axis=-1).reshape(
        -1, PAGE, kv_heads, 2 * head_dim
    )
    kv_pages = jnp.zeros_like(pages).at[page_table[0]].set(pages)
    gathered = lax.all_gather(prefix_cache, "req", axis=0, tiled=True)
    attention = attend(
        grouped_query, key_rows, value_rows, segment_row, prefix_group[0],
        gathered.transpose(0, 2, 1, 3),
    )
    share_width = hidden_in.shape[1]
    whole_attention = jnp.concatenate(shifted_copies(attention, "hid"), axis=1)
    whole_w_out = jnp.concatenate(shifted_copies(w_out, "hid"), axis=0)
    projected_out = jnp.dot(whole_attention, whole_w_out, preferred_element_type=jnp.float32)
    middle = (whole.astype(jnp.float32) + projected_out).astype(jnp.bfloat16)
    middle_share = lax.dynamic_slice_in_dim(
        middle, lax.axis_index("hid") * share_width, share_width, 1
    )
    normed_moe = rms_scale(middle, moe_gain)
    local_experts, hidden_units, model_cols = w_down.shape
    lane_width = w_gate_up.shape[-1]
    down_view = (
        w_down.reshape(local_experts, hidden_units, model_cols // lane_width, lane_width)
        .transpose(0, 2, 1, 3)
        .reshape(local_experts, 1, -1, lane_width)
    )
    packed = jnp.concatenate([w_gate_up, down_view], axis=1).transpose(1, 0, 2, 3)
    packed = lax.all_gather(packed, "req", axis=1, tiled=True)
    experts = packed.shape[1]
    expert_ids = jnp.arange(experts, dtype=jnp.int32)
    combine = jnp.sum(
        jnp.where(routes[:, :, None] == expert_ids[None, None, :], gates[:, :, None], 0.0), axis=1
    )
    partial_out = (
        expert_project(normed_moe, combine.T[:, :, None], packed)
        .transpose(1, 0, 2)
        .reshape(tok_count, model_width)
    )
    hid_count = lax.axis_size("hid")
    hid_index = lax.axis_index("hid")
    expert_sum = lax.dynamic_slice_in_dim(partial_out, hid_index * share_width, share_width, 1)
    for shift in range(1, hid_count):
        block = (hid_index + shift) % hid_count
        outgoing = lax.dynamic_slice_in_dim(partial_out, block * share_width, share_width, 1)
        pairs = [(index, (index + shift) % hid_count) for index in range(hid_count)]
        incoming = lax.ppermute(outgoing.astype(jnp.bfloat16), "hid", pairs)
        expert_sum = expert_sum + incoming.astype(jnp.float32)
    hidden_out = (middle_share.astype(jnp.float32) + expert_sum).astype(jnp.bfloat16)
    return (hidden_out, kv_pages)


def solution(mesh):
    in_specs = (
        P("req", "hid"),
        P("req", None),
        P("req", None),
        P("req", None, "hid", None),
        P("req", None),
        P(),
        P(None, "hid"),
        P(None, "hid"),
        P("hid", None),
        P(),
        P("req", None),
        P("req", None),
        P("req", None, None, "hid"),
        P("req", "hid", None),
    )
    out_specs = (P("req", "hid"), P("req", None, "hid", None))
    return jax.shard_map(shards, mesh=mesh, in_specs=in_specs, out_specs=out_specs, check_vma=False)
```
